32 devices in a mesh: seq: 8 (over z, y), head: 4 (over x, core).
Axes of the slice: x: 2, y: 2, z: 4, core: 2. Of those that a mesh axis runs over, the one named last changes fastest.
Arguments:
- projected: bfloat16 [1024, 3, 4096], P('seq', None, 'head'), may hold values from -8 to 8
- destination: int32 [1024], P('seq'), may hold values from 0 to 1023, as said below
- doc_lengths: int32 [4], replicated, may hold values from 1 to 512, 1024 in all
- random_blocks: int32 [8, 3], replicated, may hold values from 0 to 7, as said below
- global_owner: int32 [8], replicated, may hold values from 0 to 7, as said below
- out_weight: bfloat16 [4096, 4096], P('head'), may hold values from -0.09375 to 0.09375
Outputs:
- attended: bfloat16 [1024, 4096], P(('seq', 'head'))
The draws below stay inside these ranges and needn't reach their ends.
Inputs may be any that keep to these rules, and one draw needn't show every extreme that they name: Each packed position appears exactly once. Of the rows of one device (one index of seq, 128 rows), at most 32 have destinations owned by one owner (destination // 128), and in every draw some device sends exactly 32 rows to some owner. The owner (index) of random_blocks[b, r] lies at most 2 owners away from the owner of block b, counted cyclically over the owners. `global_owner`: each owner appears exactly once.
All inputs are finite; a program needn't handle non-finite values.
Results may differ from the reference program's by a relative error of at most 0.015.
Values may be sent and summed in bfloat16 or wider, within the bound.
No kernel may reach another device: no remote copies, remote signals or barrier semaphores. Data moves between devices by JAX's collectives and lax.ppermute only.
A program may use at most 128 MiB of HBM per device.

```python
import math
import jax
import jax.numpy as jnp
import numpy as np
from jax import lax

D = 4096
HEADS = 32
HD = 128
TOK_DEV = 128
BLK = 128
R = 3
RDEV = 2
TOKENS = 1024
GLOB = 128
NBLK = 8
BPD = 1
DOCS = 4
MOST = 512


def route_plan(key):
    owners = TOKENS // TOK_DEV
    base_count = TOK_DEV // owners
    half_cycle = owners // 2
    key_delta, key_pick, key_order, key_shuffle = jax.random.split(key, 4)
    deltas = jax.random.randint(key_delta, (half_cycle,), -base_count, base_count + 1)
    picked = jax.random.randint(key_pick, (), 0, owners)
    forced = jnp.where(picked < half_cycle, base_count, -base_count)
    deltas = deltas.at[picked % half_cycle].set(forced)
    cycle_counts = jnp.concatenate([deltas, -deltas])
    cycle_offset = (jnp.arange(owners)[None, :] - jnp.arange(owners)[:, None]) % owners
    counts = base_count + cycle_counts[cycle_offset]
    inclusive = jnp.cumsum(counts, axis=1)
    exclusive = inclusive - counts
    row_ids = jnp.arange(TOK_DEV)
    owner_of = jnp.sum((inclusive[:, None, :] <= row_ids[None, :, None]).astype(jnp.int32), axis=2)
    within = row_ids[None, :] - jnp.take_along_axis(exclusive, owner_of, axis=1)
    column_before = jnp.cumsum(counts, axis=0) - counts
    local_slot = jnp.take_along_axis(column_before, owner_of, axis=1) + within
    orders = jax.vmap(lambda sub: jax.random.permutation(sub, TOK_DEV))(jax.random.split(key_order, owners))
    final_slot = orders[owner_of, local_slot]
    packed = owner_of * TOK_DEV + final_slot
    shuffles = jax.vmap(lambda sub: jax.random.permutation(sub, TOK_DEV))(jax.random.split(key_shuffle, owners))
    packed = jnp.take_along_axis(packed, shuffles, axis=1)
    return packed.reshape(-1).astype(jnp.int32)


def owner_plan(key):
    return jax.random.permutation(key, TOKENS // TOK_DEV).astype(jnp.int32)


def draw_destination(key, part):
    return route_plan(jax.random.fold_in(key, 11))


def draw_global_owner(key, part):
    return owner_plan(jax.random.fold_in(key, 12))


def draw_random_blocks(key, part):
    owners = NBLK // BPD
    key_move, key_inner = jax.random.split(jax.random.fold_in(key, 13))
    moves = jax.random.randint(key_move, (NBLK, R), -RDEV, RDEV + 1)
    inner = jax.random.randint(key_inner, (NBLK, R), 0, BPD)
    home = (jnp.arange(NBLK) // BPD)[:, None]
    return ((home + moves) % owners * BPD + inner).astype(jnp.int32)


def draw_projected(key, part):
    key_base = jax.random.fold_in(jax.random.fold_in(key, 14), 0)
    values = jnp.clip(jax.random.normal(key_base, (TOKENS, 3, D), jnp.float32), -5.0, 5.0)
    return values.astype(jnp.bfloat16)


def shard_levels(own_key, dims, shards, low, high):
    gain, own = 1.0, jax.random.fold_in(own_key, 6)
    for position, shards_of in shards:
        draws = jnp.exp(jax.random.uniform(jax.random.fold_in(own, position), (shards_of,), jnp.float32, low / len(shards), high / len(shards)))
        gain = gain * jnp.repeat(draws, dims[position] // shards_of).reshape([-1 if axis == position else 1 for axis in range(len(dims))])
    return gain


def length_profile(number_of, total, reach, skew):
    portions = [(1 << 20) // math.isqrt(standing ** skew) + 1 for standing in range(2, number_of + 1)]
    spare, holding = total - reach - (number_of - 1), [1] * (number_of - 1)
    while spare > 0:
        movable = [i for i in range(number_of - 1) if holding[i] < reach]
        mass, remaining = sum([portions[i] for i in movable]), spare
        for i in movable:
            more = min(reach - holding[i], max(1, remaining * portions[i] // mass), spare)
            holding[i] = holding[i] + more
            spare = spare - more
    return np.array([reach] + holding)


def ragged_sizes(rng, count, total, bound, skew):
    if count == 2:
        one = jax.random.randint(rng, (), max(1, total - bound), min(bound, total - 1) + 1)
        return jnp.stack([one, total - one])
    sizes = jnp.asarray(length_profile(count, total, bound, skew), jnp.int32)
    pairs = (count - 1) // 2
    source_of, taker = sizes[1:1 + 2 * pairs:2], sizes[2:2 + 2 * pairs:2]
    margin = jnp.minimum(source_of - 1, bound - taker)
    moved = jax.random.randint(jax.random.fold_in(rng, 1), (pairs,), 0, 1 << 20) % (margin + 1)
    sizes = sizes.at[1:1 + 2 * pairs:2].set(source_of - moved).at[2:2 + 2 * pairs:2].set(taker + moved)
    return sizes[jax.random.permutation(jax.random.fold_in(rng, 2), count)]


def centred(own_key, dims, scale, reach, pieces=(), held_as=jnp.bfloat16):
    factor_of = shard_levels(own_key, dims, pieces, -0.22, 0.18) if pieces else 1.0
    drawn = jax.random.normal(own_key, dims, jnp.float32) * scale * factor_of
    return jnp.minimum(jnp.maximum(drawn, -reach), reach).astype(held_as)


def setup_inputs(seed: int = 0) -> dict:
    arg_keys = jax.random.split(jax.random.key(seed), 7)
    return {
        "projected": draw_projected(jax.random.fold_in(arg_keys[6], 71), 0),
        "destination": draw_destination(jax.random.fold_in(arg_keys[6], 71), 0),
        "doc_lengths": ragged_sizes(arg_keys[2], DOCS, TOKENS, MOST, 2).astype(jnp.int32),
        "random_blocks": draw_random_blocks(jax.random.fold_in(arg_keys[6], 71), 0),
        "global_owner": draw_global_owner(jax.random.fold_in(arg_keys[6], 71), 0),
        "out_weight": centred(arg_keys[5], (D, D), D ** -0.5, 0.09375, ((0, 4),)),
    }


big_negative = -1e+30

def segment_of(positions, bounds):
    return lax.optimization_barrier(jnp.sum((bounds[None, :] <= positions[:, None]).astype(jnp.int32), axis=1))

def reference(projected, destination, doc_lengths, random_blocks, global_owner, out_weight):
    routed = jnp.zeros_like(projected).at[destination].set(projected)
    score_scale = 1.0 / math.sqrt(HD)
    queries = routed[:, 0, :].reshape(TOKENS, HEADS, HD)
    keys_all = routed[:, 1, :].reshape(TOKENS, HEADS, HD)
    values_all = routed[:, 2, :].reshape(TOKENS, HEADS, HD)
    key_blocks = keys_all.reshape(NBLK, BLK, HEADS, HD)
    value_blocks = values_all.reshape(NBLK, BLK, HEADS, HD)
    bounds = jnp.cumsum(doc_lengths).astype(jnp.int32)
    glob_start = (global_owner[0] * TOK_DEV).astype(jnp.int32)
    glob_keys = lax.dynamic_slice_in_dim(keys_all, glob_start, GLOB, 0).astype(jnp.float32)
    glob_values = lax.dynamic_slice_in_dim(values_all, glob_start, GLOB, 0).astype(jnp.float32)
    glob_queries = lax.dynamic_slice_in_dim(queries, glob_start, GLOB, 0).astype(jnp.float32)

    def sparse_block(block_id):
        block_queries = lax.dynamic_slice_in_dim(queries, (block_id * BLK).astype(jnp.int32), BLK, 0).astype(jnp.float32)
        window_ids = ((block_id + jnp.arange(-1, 2, dtype=jnp.int32)) % NBLK).astype(jnp.int32)
        picked = jnp.concatenate([window_ids, random_blocks[block_id].astype(jnp.int32)])
        near_keys = key_blocks[picked].reshape((3 + R) * BLK, HEADS, HD).astype(jnp.float32)
        near_values = value_blocks[picked].reshape((3 + R) * BLK, HEADS, HD).astype(jnp.float32)
        near_scores = jnp.einsum('qhd,khd->hqk', block_queries, near_keys) * score_scale
        far_scores = jnp.einsum('qhd,khd->hqk', block_queries, glob_keys) * score_scale
        query_doc = segment_of(block_id * BLK + jnp.arange(BLK, dtype=jnp.int32), bounds)
        key_pos = (window_ids[:, None] * BLK + jnp.arange(BLK, dtype=jnp.int32)[None, :]).reshape(-1)
        key_doc = segment_of(key_pos, bounds)
        allowed = jnp.concatenate([query_doc[:, None] == key_doc[None, :], jnp.ones((BLK, R * BLK), dtype=jnp.bool_)], axis=1)
        near_scores = jnp.where(allowed[None], near_scores, big_negative)
        row_peak = jnp.maximum(lax.optimization_barrier(jnp.max(near_scores, axis=2)), lax.optimization_barrier(jnp.max(far_scores, axis=2)))
        near_exp = jnp.exp(near_scores - row_peak[:, :, None])
        far_exp = jnp.exp(far_scores - row_peak[:, :, None])
        denominator = lax.optimization_barrier(jnp.sum(near_exp, axis=2)) + lax.optimization_barrier(jnp.sum(far_exp, axis=2))
        near_weights = near_exp.astype(jnp.bfloat16).astype(jnp.float32)
        far_weights = far_exp.astype(jnp.bfloat16).astype(jnp.float32)
        mixed_sum = jnp.einsum('hqk,khd->qhd', near_weights, near_values)
        mixed_sum = mixed_sum + jnp.einsum('hqk,khd->qhd', far_weights, glob_values)
        return (mixed_sum / denominator.T[:, :, None]).reshape(BLK, D).astype(jnp.bfloat16)
    sparse = lax.map(sparse_block, jnp.arange(NBLK, dtype=jnp.int32)).reshape(TOKENS, D)

    def global_head(head_id):
        head_queries = glob_queries[:, head_id, :]
        head_keys = keys_all[:, head_id, :].astype(jnp.float32)
        head_values = values_all[:, head_id, :].astype(jnp.float32)
        head_scores = jnp.dot(head_queries, head_keys.T, precision=lax.Precision.HIGHEST) * score_scale
        head_peak = lax.optimization_barrier(jnp.max(head_scores, axis=1))
        head_exp = jnp.exp(head_scores - head_peak[:, None])
        head_sum = jnp.dot(head_exp, head_values, precision=lax.Precision.HIGHEST)
        return head_sum / lax.optimization_barrier(jnp.sum(head_exp, axis=1))[:, None]
    glob_out = lax.map(global_head, jnp.arange(HEADS, dtype=jnp.int32))
    glob_out = jnp.transpose(glob_out, (1, 0, 2)).reshape(GLOB, D).astype(jnp.bfloat16)
    attn_rows = lax.dynamic_update_slice_in_dim(sparse, glob_out, glob_start, 0)
    return jnp.dot(attn_rows, out_weight, preferred_element_type=jnp.float32).astype(jnp.bfloat16)
```

```python
import math

import jax
import jax.numpy as jnp
from jax import lax
from jax.sharding import PartitionSpec as P

HD = 128
BLK = 128
R = 3
RDEV = 2


big_negative = -1e30


def from_behind(block, axis, distance):
    devices = range(lax.axis_size(axis))
    route = [((i - distance) % len(devices), i) for i in devices]
    return lax.ppermute(block, axis, route)


def from_root(x, axis, root):
    mine = lax.axis_index(axis) == root
    return lax.psum(jnp.where(mine, x, jnp.zeros_like(x)), axis)


def combined_all(x, axis, combine):
    everything = jax.tree.map(lambda part: lax.all_gather(part, axis), x)
    first = jax.tree.map(lambda part: part[0], everything)

    def step(k, so_far):
        return combine(so_far, jax.tree.map(lambda part: part[k], everything))

    return lax.fori_loop(1, lax.axis_size(axis), step, first)


def segment_of(positions, bounds):
    return jnp.sum((bounds[None, :] <= positions[:, None]).astype(jnp.int32), axis=1)


def combine_parts(left_part, right_part):
    top_left, total_left, accum_left = left_part
    top_right, total_right, accum_right = right_part
    row_peak = jnp.maximum(top_left, top_right)
    factor_left = jnp.exp(top_left - row_peak)
    factor_right = jnp.exp(top_right - row_peak)
    return (
        row_peak,
        total_left * factor_left + total_right * factor_right,
        accum_left * factor_left[:, :, None] + accum_right * factor_right[:, :, None],
    )


def shards_ring(projected, destination, doc_lengths, random_blocks, global_owner, out_weight):
    owners = lax.axis_size("seq")
    own_index = lax.axis_index("seq")
    tok_dev = projected.shape[0]
    columns = projected.shape[2]
    heads_here = columns // HD
    per_dev = tok_dev // BLK
    blocks_all = owners * per_dev
    capacity = 2 * (tok_dev // owners)
    score_scale = 1.0 / math.sqrt(HD)
    target_owner = destination // tok_dev
    onehot = (target_owner[:, None] == jnp.arange(owners, dtype=jnp.int32)[None, :]).astype(
        jnp.int32
    )
    before = jnp.cumsum(onehot, axis=0) - onehot
    slot_rank = jnp.sum(before * onehot, axis=1)
    outgoing = (
        jnp.zeros((owners, capacity, 3, columns), projected.dtype)
        .at[target_owner, slot_rank]
        .set(projected)
    )
    slots = (
        jnp.full((owners, capacity), -1, jnp.int32)
        .at[target_owner, slot_rank]
        .set(destination % tok_dev)
    )
    incoming, landing = (
        lax.all_to_all(outgoing, "seq", split_axis=0, concat_axis=0, tiled=True),
        lax.all_to_all(slots, "seq", split_axis=0, concat_axis=0, tiled=True),
    )
    landing = landing.reshape(-1)
    landing = jnp.where(landing >= 0, landing, tok_dev)
    routed = (
        jnp.zeros((tok_dev, 3, columns), projected.dtype)
        .at[landing]
        .set(incoming.reshape(owners * capacity, 3, columns), mode="drop")
    )
    keyval = routed[:, 1:, :]
    fetched = {0: keyval}
    offsets = list(range(-RDEV, 0)) + list(range(1, RDEV + 1))
    for offset in offsets:
        fetched[offset] = from_behind(keyval, "seq", -offset)
    band_blocks = jnp.stack([fetched[offset] for offset in range(-RDEV, RDEV + 1)])
    block_ids = own_index * per_dev + jnp.arange(per_dev, dtype=jnp.int32)
    local_pick = jnp.arange(per_dev, dtype=jnp.int32) + RDEV * per_dev
    window_pick = local_pick[:, None] + jnp.arange(-1, 2, dtype=jnp.int32)[None, :]
    chosen_rand = lax.dynamic_slice_in_dim(random_blocks, own_index * per_dev, per_dev, 0)
    away_dev = (chosen_rand // per_dev - own_index) % owners
    away_dev = jnp.where(away_dev > owners // 2, away_dev - owners, away_dev)
    rand_pick = (away_dev + RDEV) * per_dev + chosen_rand % per_dev
    block_picks = jnp.concatenate([window_pick, rand_pick], axis=1)
    gathered = jnp.take(band_blocks, block_picks, axis=0)
    near_keys = gathered[:, :, :, 0, :].reshape(per_dev, (3 + R) * BLK, heads_here, HD)
    near_values = gathered[:, :, :, 1, :].reshape(per_dev, (3 + R) * BLK, heads_here, HD)
    owner_dev = global_owner[0]
    global_rows = from_root(routed, "seq", owner_dev)
    glob_keys = global_rows[:, 1, :].reshape(tok_dev, heads_here, HD)
    glob_values = global_rows[:, 2, :].reshape(tok_dev, heads_here, HD)
    queries = routed[:, 0, :].reshape(per_dev, BLK, heads_here, HD)
    near_scores = (
        jnp.einsum("bqhd,bkhd->bhqk", queries, near_keys, preferred_element_type=jnp.float32)
        * score_scale
    )
    far_scores = (
        jnp.einsum("bqhd,khd->bhqk", queries, glob_keys, preferred_element_type=jnp.float32)
        * score_scale
    )
    bounds = jnp.cumsum(doc_lengths)
    query_pos = own_index * tok_dev + jnp.arange(tok_dev, dtype=jnp.int32)
    query_doc = segment_of(query_pos, bounds).reshape(per_dev, BLK)
    window_blocks = (block_ids[:, None] + jnp.arange(-1, 2, dtype=jnp.int32)[None, :]) % blocks_all
    key_pos = (
        window_blocks[:, :, None] * BLK + jnp.arange(BLK, dtype=jnp.int32)[None, None, :]
    ).reshape(-1)
    key_doc = segment_of(key_pos, bounds).reshape(per_dev, 3 * BLK)
    same_doc = query_doc[:, :, None] == key_doc[:, None, :]
    allowed = jnp.concatenate(
        [same_doc, jnp.ones((per_dev, BLK, R * BLK), dtype=jnp.bool_)], axis=2
    )
    near_scores = jnp.where(allowed[:, None], near_scores, big_negative)
    row_peak = jnp.maximum(jnp.max(near_scores, axis=3), jnp.max(far_scores, axis=3))
    near_exp = jnp.exp(near_scores - row_peak[..., None])
    far_exp = jnp.exp(far_scores - row_peak[..., None])
    denominator = jnp.sum(near_exp, axis=3) + jnp.sum(far_exp, axis=3)
    mixed_sum = jnp.einsum(
        "bhqk,bkhd->bqhd",
        near_exp.astype(jnp.bfloat16),
        near_values,
        preferred_element_type=jnp.float32,
    )
    mixed_sum = mixed_sum + jnp.einsum(
        "bhqk,khd->bqhd",
        far_exp.astype(jnp.bfloat16),
        glob_values,
        preferred_element_type=jnp.float32,
    )
    sparse = (mixed_sum / jnp.transpose(denominator, (0, 2, 1))[..., None]).reshape(
        tok_dev, columns
    )
    sparse = sparse.astype(jnp.bfloat16)
    glob_queries = global_rows[:, 0, :].reshape(tok_dev, heads_here, HD)
    local_keys = routed[:, 1, :].reshape(tok_dev, heads_here, HD)
    local_values = routed[:, 2, :].reshape(tok_dev, heads_here, HD).astype(jnp.float32)
    all_scores = (
        jnp.einsum("qhd,khd->hqk", glob_queries, local_keys, preferred_element_type=jnp.float32)
        * score_scale
    )
    local_peak = jnp.max(all_scores, axis=2)
    weights = jnp.exp(all_scores - local_peak[..., None])
    part_total = jnp.sum(weights, axis=2)
    part_accum = jnp.einsum("hqk,khd->hqd", weights, local_values, precision=lax.Precision.HIGHEST)
    peak_all, total_all, accum_all = combined_all(
        (local_peak, part_total, part_accum), "seq", combine_parts
    )
    glob_out = jnp.transpose(accum_all / total_all[..., None], (1, 0, 2)).reshape(tok_dev, columns)
    glob_out = glob_out.astype(jnp.bfloat16)
    attn_rows = jnp.where(own_index == owner_dev, glob_out, sparse)
    return lax.psum_scatter(
        jnp.dot(attn_rows, out_weight, preferred_element_type=jnp.float32).astype(jnp.bfloat16),
        "head",
        scatter_dimension=0,
        tiled=True,
    )


def gathered_plan(projected, destination, doc_lengths, random_blocks, global_owner, out_weight):
    owners = lax.axis_size("seq")
    own_index = lax.axis_index("seq")
    tok_dev = projected.shape[0]
    columns = projected.shape[2]
    heads_here = columns // HD
    tokens = owners * tok_dev
    blocks_all = tokens // BLK
    score_scale = 1.0 / math.sqrt(HD)
    everything = lax.all_gather(projected, "seq", tiled=True)
    arrival_dest = lax.all_gather(destination, "seq", tiled=True)
    my_pos = own_index * tok_dev + jnp.arange(tok_dev, dtype=jnp.int32)
    pick = (arrival_dest[None, :] == my_pos[:, None]).astype(projected.dtype)
    queries = jnp.dot(pick, everything[:, 0, :], preferred_element_type=jnp.float32)
    queries = queries.astype(projected.dtype).reshape(tok_dev, heads_here, HD)
    keys = everything[:, 1, :].reshape(tokens, heads_here, HD)
    values = everything[:, 2, :].reshape(tokens, heads_here, HD)
    scores = (
        jnp.einsum("qhd,khd->hqk", queries, keys, preferred_element_type=jnp.float32)
        * score_scale
    )
    bounds = jnp.cumsum(doc_lengths)
    key_block = arrival_dest // BLK
    key_doc = segment_of(arrival_dest, bounds)
    query_block = my_pos // BLK
    query_doc = segment_of(my_pos, bounds)
    same_doc = query_doc[:, None] == key_doc[None, :]
    window = jnp.zeros((tok_dev, tokens), jnp.int32)
    for step in (-1, 0, 1):
        near = (query_block + step) % blocks_all
        window = window + (key_block[None, :] == near[:, None]).astype(jnp.int32)
    window = jnp.where(same_doc, window, 0)
    chosen = random_blocks[query_block]
    drawn = jnp.zeros((tok_dev, tokens), jnp.int32)
    for r in range(chosen.shape[1]):
        drawn = drawn + (key_block[None, :] == chosen[:, r][:, None]).astype(jnp.int32)
    glob_start = global_owner[0] * tok_dev
    in_glob = (arrival_dest >= glob_start) & (arrival_dest < glob_start + tok_dev)
    count = window + drawn + in_glob[None, :].astype(jnp.int32)
    live = count > 0
    near_scores = jnp.where(live[None], scores, big_negative)
    row_peak = jnp.max(near_scores, axis=2)
    near_exp = jnp.exp(near_scores - row_peak[..., None])
    count_f = count.astype(jnp.float32)[None]
    denominator = jnp.sum(near_exp * count_f, axis=2)
    weighted = near_exp.astype(jnp.bfloat16).astype(jnp.float32) * count_f
    weight_hi = weighted.astype(jnp.bfloat16)
    weight_lo = (weighted - weight_hi.astype(jnp.float32)).astype(jnp.bfloat16)
    mixed_sum = jnp.einsum("hqk,khd->qhd", weight_hi, values, preferred_element_type=jnp.float32)
    mixed_sum = mixed_sum + jnp.einsum(
        "hqk,khd->qhd", weight_lo, values, preferred_element_type=jnp.float32
    )
    sparse = (mixed_sum / jnp.transpose(denominator)[..., None]).reshape(tok_dev, columns)
    sparse = sparse.astype(jnp.bfloat16)
    glob_peak = jnp.max(scores, axis=2)
    glob_exp = jnp.exp(scores - glob_peak[..., None])
    glob_total = jnp.sum(glob_exp, axis=2)
    glob_accum = jnp.einsum(
        "hqk,khd->qhd", glob_exp, values.astype(jnp.float32), precision=lax.Precision.HIGHEST
    )
    glob_out = (glob_accum / jnp.transpose(glob_total)[..., None]).reshape(tok_dev, columns)
    glob_out = glob_out.astype(jnp.bfloat16)
    attn_rows = jnp.where(own_index == global_owner[0], glob_out, sparse)
    return lax.psum_scatter(
        jnp.dot(attn_rows, out_weight, preferred_element_type=jnp.float32).astype(jnp.bfloat16),
        "head",
        scatter_dimension=0,
        tiled=True,
    )


GATHER_LIMIT = 16 * 2**20


def shards(projected, destination, doc_lengths, random_blocks, global_owner, out_weight):
    gathered_bytes = lax.axis_size("seq") * projected.size * projected.dtype.itemsize
    if gathered_bytes <= GATHER_LIMIT:
        return gathered_plan(
            projected, destination, doc_lengths, random_blocks, global_owner, out_weight
        )
    return shards_ring(projected, destination, doc_lengths, random_blocks, global_owner, out_weight)


def solution(mesh):
    in_specs = (P("seq", None, "head"), P("seq"), P(), P(), P(), P("head", None))
    out_specs = P(("seq", "head"), None)
    return jax.shard_map(shards, mesh=mesh, in_specs=in_specs, out_specs=out_specs, check_vma=False)
```

```python
import math

import jax
import jax.numpy as jnp
from jax import lax
from jax.sharding import PartitionSpec as P

HD = 128
BLK = 128
R = 3
RDEV = 2


big_negative = -1e30


def from_behind(block, axis, distance):
    devices = range(lax.axis_size(axis))
    route = [((i - distance) % len(devices), i) for i in devices]
    return lax.ppermute(block, axis, route)


def from_root(x, axis, root):
    mine = lax.axis_index(axis) == root
    return lax.psum(jnp.where(mine, x, jnp.zeros_like(x)), axis)


def combined_all(x, axis, combine):
    everything = jax.tree.map(lambda part: lax.all_gather(part, axis), x)
    first = jax.tree.map(lambda part: part[0], everything)

    def step(k, so_far):
        return combine(so_far, jax.tree.map(lambda part: part[k], everything))

    return lax.fori_loop(1, lax.axis_size(axis), step, first)


def segment_of(positions, bounds):
    return jnp.sum((bounds[None, :] <= positions[:, None]).astype(jnp.int32), axis=1)


def combine_parts(left_part, right_part):
    top_left, total_left, accum_left = left_part
    top_right, total_right, accum_right = right_part
    row_peak = jnp.maximum(top_left, top_right)
    factor_left = jnp.exp(top_left - row_peak)
    factor_right = jnp.exp(top_right - row_peak)
    return (
        row_peak,
        total_left * factor_left + total_right * factor_right,
        accum_left * factor_left[:, :, None] + accum_right * factor_right[:, :, None],
    )


def shards_ring(projected, destination, doc_lengths, random_blocks, global_owner, out_weight):
    owners = lax.axis_size("seq")
    own_index = lax.axis_index("seq")
    tok_dev = projected.shape[0]
    columns = projected.shape[2]
    heads_here = columns // HD
    per_dev = tok_dev // BLK
    blocks_all = owners * per_dev
    capacity = 2 * (tok_dev // owners)
    score_scale = 1.0 / math.sqrt(HD)
    target_owner = destination // tok_dev
    onehot = (target_owner[:, None] == jnp.arange(owners, dtype=jnp.int32)[None, :]).astype(
        jnp.int32
    )
    before = jnp.cumsum(onehot, axis=0) - onehot
    slot_rank = jnp.sum(before * onehot, axis=1)
    outgoing = (
        jnp.zeros((owners, capacity, 3, columns), projected.dtype)
        .at[target_owner, slot_rank]
        .set(projected)
    )
    slots = (
        jnp.full((owners, capacity), -1, jnp.int32)
        .at[target_owner, slot_rank]
        .set(destination % tok_dev)
    )
    incoming, landing = (
        lax.all_to_all(outgoing, "seq", split_axis=0, concat_axis=0, tiled=True),
        lax.all_to_all(slots, "seq", split_axis=0, concat_axis=0, tiled=True),
    )
    landing = landing.reshape(-1)
    landing = jnp.where(landing >= 0, landing, tok_dev)
    routed = (
        jnp.zeros((tok_dev, 3, columns), projected.dtype)
        .at[landing]
        .set(incoming.reshape(owners * capacity, 3, columns), mode="drop")
    )
    keyval = routed[:, 1:, :]
    fetched = {0: keyval}
    offsets = list(range(-RDEV, 0)) + list(range(1, RDEV + 1))
    for offset in offsets:
        fetched[offset] = from_behind(keyval, "seq", -offset)
    band_blocks = jnp.stack([fetched[offset] for offset in range(-RDEV, RDEV + 1)])
    block_ids = own_index * per_dev + jnp.arange(per_dev, dtype=jnp.int32)
    local_pick = jnp.arange(per_dev, dtype=jnp.int32) + RDEV * per_dev
    window_pick = local_pick[:, None] + jnp.arange(-1, 2, dtype=jnp.int32)[None, :]
    chosen_rand = lax.dynamic_slice_in_dim(random_blocks, own_index * per_dev, per_dev, 0)
    away_dev = (chosen_rand // per_dev - own_index) % owners
    away_dev = jnp.where(away_dev > owners // 2, away_dev - owners, away_dev)
    rand_pick = (away_dev + RDEV) * per_dev + chosen_rand % per_dev
    block_picks = jnp.concatenate([window_pick, rand_pick], axis=1)
    gathered = jnp.take(band_blocks, block_picks, axis=0)
    near_keys = gathered[:, :, :, 0, :].reshape(per_dev, (3 + R) * BLK, heads_here, HD)
    near_values = gathered[:, :, :, 1, :].reshape(per_dev, (3 + R) * BLK, heads_here, HD)
    owner_dev = global_owner[0]
    global_rows = from_root(routed, "seq", owner_dev)
    glob_keys = global_rows[:, 1, :].reshape(tok_dev, heads_here, HD)
    glob_values = global_rows[:, 2, :].reshape(tok_dev, heads_here, HD)
    queries = routed[:, 0, :].reshape(per_dev, BLK, heads_here, HD)
    near_scores = (
        jnp.einsum("bqhd,bkhd->bhqk", queries, near_keys, preferred_element_type=jnp.float32)
        * score_scale
    )
    far_scores = (
        jnp.einsum("bqhd,khd->bhqk", queries, glob_keys, preferred_element_type=jnp.float32)
        * score_scale
    )
    bounds = jnp.cumsum(doc_lengths)
    query_pos = own_index * tok_dev + jnp.arange(tok_dev, dtype=jnp.int32)
    query_doc = segment_of(query_pos, bounds).reshape(per_dev, BLK)
    window_blocks = (block_ids[:, None] + jnp.arange(-1, 2, dtype=jnp.int32)[None, :]) % blocks_all
    key_pos = (
        window_blocks[:, :, None] * BLK + jnp.arange(BLK, dtype=jnp.int32)[None, None, :]
    ).reshape(-1)
    key_doc = segment_of(key_pos, bounds).reshape(per_dev, 3 * BLK)
    same_doc = query_doc[:, :, None] == key_doc[:, None, :]
    allowed = jnp.concatenate(
        [same_doc, jnp.ones((per_dev, BLK, R * BLK), dtype=jnp.bool_)], axis=2
    )
    near_scores = jnp.where(allowed[:, None], near_scores, big_negative)
    row_peak = jnp.maximum(jnp.max(near_scores, axis=3), jnp.max(far_scores, axis=3))
    near_exp = jnp.exp(near_scores - row_peak[..., None])
    far_exp = jnp.exp(far_scores - row_peak[..., None])
    denominator = jnp.sum(near_exp, axis=3) + jnp.sum(far_exp, axis=3)
    mixed_sum = jnp.einsum(
        "bhqk,bkhd->bqhd",
        near_exp.astype(jnp.bfloat16),
        near_values,
        preferred_element_type=jnp.float32,
    )
    mixed_sum = mixed_sum + jnp.einsum(
        "bhqk,khd->bqhd",
        far_exp.astype(jnp.bfloat16),
        glob_values,
        preferred_element_type=jnp.float32,
    )
    sparse = (mixed_sum / jnp.transpose(denominator, (0, 2, 1))[..., None]).reshape(
        tok_dev, columns
    )
    sparse = sparse.astype(jnp.bfloat16)
    glob_queries = global_rows[:, 0, :].reshape(tok_dev, heads_here, HD)
    local_keys = routed[:, 1, :].reshape(tok_dev, heads_here, HD)
    local_values = routed[:, 2, :].reshape(tok_dev, heads_here, HD).astype(jnp.float32)
    all_scores = (
        jnp.einsum("qhd,khd->hqk", glob_queries, local_keys, preferred_element_type=jnp.float32)
        * score_scale
    )
    local_peak = jnp.max(all_scores, axis=2)
    weights = jnp.exp(all_scores - local_peak[..., None])
    part_total = jnp.sum(weights, axis=2)
    part_accum = jnp.einsum("hqk,khd->hqd", weights, local_values, precision=lax.Precision.HIGHEST)
    peak_all, total_all, accum_all = combined_all(
        (local_peak, part_total, part_accum), "seq", combine_parts
    )
    glob_out = jnp.transpose(accum_all / total_all[..., None], (1, 0, 2)).reshape(tok_dev, columns)
    glob_out = glob_out.astype(jnp.bfloat16)
    attn_rows = jnp.where(own_index == owner_dev, glob_out, sparse)
    return lax.psum_scatter(
        jnp.dot(attn_rows, out_weight, preferred_element_type=jnp.float32).astype(jnp.bfloat16),
        "head",
        scatter_dimension=0,
        tiled=True,
    )


def gathered_plan(projected, destination, doc_lengths, random_blocks, global_owner, out_weight):
    owners = lax.axis_size("seq")
    own_index = lax.axis_index("seq")
    tok_dev = projected.shape[0]
    columns = projected.shape[2]
    heads_here = columns // HD
    tokens = owners * tok_dev
    blocks_all = tokens // BLK
    score_scale = 1.0 / math.sqrt(HD)
    capacity = 2 * (tok_dev // owners)
    arrival_dest = lax.all_gather(destination, "seq", tiled=True)
    keyval = lax.all_gather(projected[:, 1:, :], "seq", tiled=True)
    target_all = arrival_dest.reshape(owners, tok_dev) // tok_dev
    onehot = (target_all[:, :, None] == jnp.arange(owners, dtype=jnp.int32)).astype(jnp.int32)
    slot_all = jnp.sum((jnp.cumsum(onehot, axis=1) - onehot) * onehot, axis=2)
    target = destination // tok_dev
    mine = (target[:, None] == jnp.arange(owners, dtype=jnp.int32)[None, :]).astype(jnp.int32)
    slot = jnp.sum((jnp.cumsum(mine, axis=0) - mine) * mine, axis=1)
    send_col = target * capacity + slot
    send_pick = (
        jnp.arange(owners * capacity, dtype=jnp.int32)[:, None] == send_col[None, :]
    ).astype(projected.dtype)
    outgoing = jnp.dot(send_pick, projected[:, 0, :], preferred_element_type=jnp.float32)
    outgoing = outgoing.astype(projected.dtype).reshape(owners, capacity, columns)
    incoming = lax.all_to_all(outgoing, "seq", split_axis=0, concat_axis=0, tiled=True)
    my_pos = own_index * tok_dev + jnp.arange(tok_dev, dtype=jnp.int32)
    source = jnp.arange(tokens, dtype=jnp.int32) // tok_dev
    land_col = (source * capacity + slot_all.reshape(-1))[None, :]
    hit = arrival_dest[None, :] == my_pos[:, None]
    col_of_pos = jnp.sum(jnp.where(hit, land_col, 0), axis=1)
    land_pick = (
        col_of_pos[:, None] == jnp.arange(owners * capacity, dtype=jnp.int32)[None, :]
    ).astype(projected.dtype)
    queries = jnp.dot(
        land_pick, incoming.reshape(owners * capacity, columns), preferred_element_type=jnp.float32
    )
    queries = queries.astype(projected.dtype).reshape(tok_dev, heads_here, HD)
    keys = keyval[:, 0, :].reshape(tokens, heads_here, HD)
    values = keyval[:, 1, :].reshape(tokens, heads_here, HD)
    scores = (
        jnp.einsum("qhd,khd->hqk", queries, keys, preferred_element_type=jnp.float32)
        * score_scale
    )
    bounds = jnp.cumsum(doc_lengths)
    key_block = arrival_dest // BLK
    key_doc = segment_of(arrival_dest, bounds)
    query_block = my_pos // BLK
    query_doc = segment_of(my_pos, bounds)
    same_doc = query_doc[:, None] == key_doc[None, :]
    window = jnp.zeros((tok_dev, tokens), jnp.int32)
    for step in (-1, 0, 1):
        near = (query_block + step) % blocks_all
        window = window + (key_block[None, :] == near[:, None]).astype(jnp.int32)
    window = jnp.where(same_doc, window, 0)
    chosen = random_blocks[query_block]
    drawn = jnp.zeros((tok_dev, tokens), jnp.int32)
    for r in range(chosen.shape[1]):
        drawn = drawn + (key_block[None, :] == chosen[:, r][:, None]).astype(jnp.int32)
    glob_start = global_owner[0] * tok_dev
    in_glob = (arrival_dest >= glob_start) & (arrival_dest < glob_start + tok_dev)
    count = window + drawn + in_glob[None, :].astype(jnp.int32)
    live = count > 0
    near_scores = jnp.where(live[None], scores, big_negative)
    row_peak = jnp.max(near_scores, axis=2)
    near_exp = jnp.exp(near_scores - row_peak[..., None])
    count_f = count.astype(jnp.float32)[None]
    denominator = jnp.sum(near_exp * count_f, axis=2)
    weighted = near_exp.astype(jnp.bfloat16).astype(jnp.float32) * count_f
    weight_hi = weighted.astype(jnp.bfloat16)
    weight_lo = (weighted - weight_hi.astype(jnp.float32)).astype(jnp.bfloat16)
    mixed_sum = jnp.einsum("hqk,khd->qhd", weight_hi, values, preferred_element_type=jnp.float32)
    mixed_sum = mixed_sum + jnp.einsum(
        "hqk,khd->qhd", weight_lo, values, preferred_element_type=jnp.float32
    )
    sparse = (mixed_sum / jnp.transpose(denominator)[..., None]).reshape(tok_dev, columns)
    sparse = sparse.astype(jnp.bfloat16)
    glob_peak = jnp.max(scores, axis=2)
    glob_exp = jnp.exp(scores - glob_peak[..., None])
    glob_total = jnp.sum(glob_exp, axis=2)
    glob_accum = jnp.einsum(
        "hqk,khd->qhd", glob_exp, values.astype(jnp.float32), precision=lax.Precision.HIGHEST
    )
    glob_out = (glob_accum / jnp.transpose(glob_total)[..., None]).reshape(tok_dev, columns)
    glob_out = glob_out.astype(jnp.bfloat16)
    attn_rows = jnp.where(own_index == global_owner[0], glob_out, sparse)
    return lax.psum_scatter(
        jnp.dot(attn_rows, out_weight, preferred_element_type=jnp.float32).astype(jnp.bfloat16),
        "head",
        scatter_dimension=0,
        tiled=True,
    )


GATHER_LIMIT = 16 * 2**20


def shards(projected, destination, doc_lengths, random_blocks, global_owner, out_weight):
    gathered_bytes = lax.axis_size("seq") * projected.size * projected.dtype.itemsize
    if gathered_bytes <= GATHER_LIMIT:
        return gathered_plan(
            projected, destination, doc_lengths, random_blocks, global_owner, out_weight
        )
    return shards_ring(projected, destination, doc_lengths, random_blocks, global_owner, out_weight)


def solution(mesh):
    in_specs = (P("seq", None, "head"), P("seq"), P(), P(), P(), P("head", None))
    out_specs = P(("seq", "head"), None)
    return jax.shard_map(shards, mesh=mesh, in_specs=in_specs, out_specs=out_specs, check_vma=False)
```

```python
import math

import jax
import jax.numpy as jnp
from jax import lax
from jax.sharding import PartitionSpec as P

HD = 128
BLK = 128
R = 3
RDEV = 2


big_negative = -1e30


def from_behind(block, axis, distance):
    devices = range(lax.axis_size(axis))
    route = [((i - distance) % len(devices), i) for i in devices]
    return lax.ppermute(block, axis, route)


def from_root(x, axis, root):
    mine = lax.axis_index(axis) == root
    return lax.psum(jnp.where(mine, x, jnp.zeros_like(x)), axis)


def combined_all(x, axis, combine):
    everything = jax.tree.map(lambda part: lax.all_gather(part, axis), x)
    first = jax.tree.map(lambda part: part[0], everything)

    def step(k, so_far):
        return combine(so_far, jax.tree.map(lambda part: part[k], everything))

    return lax.fori_loop(1, lax.axis_size(axis), step, first)


def segment_of(positions, bounds):
    return jnp.sum((bounds[None, :] <= positions[:, None]).astype(jnp.int32), axis=1)


def combine_parts(left_part, right_part):
    top_left, total_left, accum_left = left_part
    top_right, total_right, accum_right = right_part
    row_peak = jnp.maximum(top_left, top_right)
    factor_left = jnp.exp(top_left - row_peak)
    factor_right = jnp.exp(top_right - row_peak)
    return (
        row_peak,
        total_left * factor_left + total_right * factor_right,
        accum_left * factor_left[:, :, None] + accum_right * factor_right[:, :, None],
    )


def shards_ring(projected, destination, doc_lengths, random_blocks, global_owner, out_weight):
    owners = lax.axis_size("seq")
    own_index = lax.axis_index("seq")
    tok_dev = projected.shape[0]
    columns = projected.shape[2]
    heads_here = columns // HD
    per_dev = tok_dev // BLK
    blocks_all = owners * per_dev
    capacity = 2 * (tok_dev // owners)
    score_scale = 1.0 / math.sqrt(HD)
    target_owner = destination // tok_dev
    onehot = (target_owner[:, None] == jnp.arange(owners, dtype=jnp.int32)[None, :]).astype(
        jnp.int32
    )
    before = jnp.cumsum(onehot, axis=0) - onehot
    slot_rank = jnp.sum(before * onehot, axis=1)
    outgoing = (
        jnp.zeros((owners, capacity, 3, columns), projected.dtype)
        .at[target_owner, slot_rank]
        .set(projected)
    )
    slots = (
        jnp.full((owners, capacity), -1, jnp.int32)
        .at[target_owner, slot_rank]
        .set(destination % tok_dev)
    )
    incoming, landing = (
        lax.all_to_all(outgoing, "seq", split_axis=0, concat_axis=0, tiled=True),
        lax.all_to_all(slots, "seq", split_axis=0, concat_axis=0, tiled=True),
    )
    landing = landing.reshape(-1)
    landing = jnp.where(landing >= 0, landing, tok_dev)
    routed = (
        jnp.zeros((tok_dev, 3, columns), projected.dtype)
        .at[landing]
        .set(incoming.reshape(owners * capacity, 3, columns), mode="drop")
    )
    keyval = routed[:, 1:, :]
    fetched = {0: keyval}
    offsets = list(range(-RDEV, 0)) + list(range(1, RDEV + 1))
    for offset in offsets:
        fetched[offset] = from_behind(keyval, "seq", -offset)
    band_blocks = jnp.stack([fetched[offset] for offset in range(-RDEV, RDEV + 1)])
    block_ids = own_index * per_dev + jnp.arange(per_dev, dtype=jnp.int32)
    local_pick = jnp.arange(per_dev, dtype=jnp.int32) + RDEV * per_dev
    window_pick = local_pick[:, None] + jnp.arange(-1, 2, dtype=jnp.int32)[None, :]
    chosen_rand = lax.dynamic_slice_in_dim(random_blocks, own_index * per_dev, per_dev, 0)
    away_dev = (chosen_rand // per_dev - own_index) % owners
    away_dev = jnp.where(away_dev > owners // 2, away_dev - owners, away_dev)
    rand_pick = (away_dev + RDEV) * per_dev + chosen_rand % per_dev
    block_picks = jnp.concatenate([window_pick, rand_pick], axis=1)
    gathered = jnp.take(band_blocks, block_picks, axis=0)
    near_keys = gathered[:, :, :, 0, :].reshape(per_dev, (3 + R) * BLK, heads_here, HD)
    near_values = gathered[:, :, :, 1, :].reshape(per_dev, (3 + R) * BLK, heads_here, HD)
    owner_dev = global_owner[0]
    global_rows = from_root(routed, "seq", owner_dev)
    glob_keys = global_rows[:, 1, :].reshape(tok_dev, heads_here, HD)
    glob_values = global_rows[:, 2, :].reshape(tok_dev, heads_here, HD)
    queries = routed[:, 0, :].reshape(per_dev, BLK, heads_here, HD)
    near_scores = (
        jnp.einsum("bqhd,bkhd->bhqk", queries, near_keys, preferred_element_type=jnp.float32)
        * score_scale
    )
    far_scores = (
        jnp.einsum("bqhd,khd->bhqk", queries, glob_keys, preferred_element_type=jnp.float32)
        * score_scale
    )
    bounds = jnp.cumsum(doc_lengths)
    query_pos = own_index * tok_dev + jnp.arange(tok_dev, dtype=jnp.int32)
    query_doc = segment_of(query_pos, bounds).reshape(per_dev, BLK)
    window_blocks = (block_ids[:, None] + jnp.arange(-1, 2, dtype=jnp.int32)[None, :]) % blocks_all
    key_pos = (
        window_blocks[:, :, None] * BLK + jnp.arange(BLK, dtype=jnp.int32)[None, None, :]
    ).reshape(-1)
    key_doc = segment_of(key_pos, bounds).reshape(per_dev, 3 * BLK)
    same_doc = query_doc[:, :, None] == key_doc[:, None, :]
    allowed = jnp.concatenate(
        [same_doc, jnp.ones((per_dev, BLK, R * BLK), dtype=jnp.bool_)], axis=2
    )
    near_scores = jnp.where(allowed[:, None], near_scores, big_negative)
    row_peak = jnp.maximum(jnp.max(near_scores, axis=3), jnp.max(far_scores, axis=3))
    near_exp = jnp.exp(near_scores - row_peak[..., None])
    far_exp = jnp.exp(far_scores - row_peak[..., None])
    denominator = jnp.sum(near_exp, axis=3) + jnp.sum(far_exp, axis=3)
    mixed_sum = jnp.einsum(
        "bhqk,bkhd->bqhd",
        near_exp.astype(jnp.bfloat16),
        near_values,
        preferred_element_type=jnp.float32,
    )
    mixed_sum = mixed_sum + jnp.einsum(
        "bhqk,khd->bqhd",
        far_exp.astype(jnp.bfloat16),
        glob_values,
        preferred_element_type=jnp.float32,
    )
    sparse = (mixed_sum / jnp.transpose(denominator, (0, 2, 1))[..., None]).reshape(
        tok_dev, columns
    )
    sparse = sparse.astype(jnp.bfloat16)
    glob_queries = global_rows[:, 0, :].reshape(tok_dev, heads_here, HD)
    local_keys = routed[:, 1, :].reshape(tok_dev, heads_here, HD)
    local_values = routed[:, 2, :].reshape(tok_dev, heads_here, HD).astype(jnp.float32)
    all_scores = (
        jnp.einsum("qhd,khd->hqk", glob_queries, local_keys, preferred_element_type=jnp.float32)
        * score_scale
    )
    local_peak = jnp.max(all_scores, axis=2)
    weights = jnp.exp(all_scores - local_peak[..., None])
    part_total = jnp.sum(weights, axis=2)
    part_accum = jnp.einsum("hqk,khd->hqd", weights, local_values, precision=lax.Precision.HIGHEST)
    peak_all, total_all, accum_all = combined_all(
        (local_peak, part_total, part_accum), "seq", combine_parts
    )
    glob_out = jnp.transpose(accum_all / total_all[..., None], (1, 0, 2)).reshape(tok_dev, columns)
    glob_out = glob_out.astype(jnp.bfloat16)
    attn_rows = jnp.where(own_index == owner_dev, glob_out, sparse)
    return lax.psum_scatter(
        jnp.dot(attn_rows, out_weight, preferred_element_type=jnp.float32).astype(jnp.bfloat16),
        "head",
        scatter_dimension=0,
        tiled=True,
    )


def gathered_plan(projected, destination, doc_lengths, random_blocks, global_owner, out_weight):
    owners = lax.axis_size("seq")
    own_index = lax.axis_index("seq")
    tok_dev = projected.shape[0]
    columns = projected.shape[2]
    heads_here = columns // HD
    tokens = owners * tok_dev
    blocks_all = tokens // BLK
    score_scale = 1.0 / math.sqrt(HD)
    capacity = 2 * (tok_dev // owners)
    arrival_dest = lax.all_gather(destination, "seq", tiled=True)
    keyval = lax.all_gather(projected[:, 1:, :], "seq", tiled=True)
    target_all = arrival_dest.reshape(owners, tok_dev) // tok_dev
    onehot = (target_all[:, :, None] == jnp.arange(owners, dtype=jnp.int32)).astype(jnp.int32)
    slot_all = jnp.sum((jnp.cumsum(onehot, axis=1) - onehot) * onehot, axis=2)
    target = destination // tok_dev
    mine = (target[:, None] == jnp.arange(owners, dtype=jnp.int32)[None, :]).astype(jnp.int32)
    slot = jnp.sum((jnp.cumsum(mine, axis=0) - mine) * mine, axis=1)
    send_col = target * capacity + slot
    send_pick = (
        jnp.arange(owners * capacity, dtype=jnp.int32)[:, None] == send_col[None, :]
    ).astype(projected.dtype)
    outgoing = jnp.dot(send_pick, projected[:, 0, :], preferred_element_type=jnp.float32)
    outgoing = outgoing.astype(projected.dtype).reshape(owners, capacity, columns)
    incoming = lax.all_to_all(outgoing, "seq", split_axis=0, concat_axis=0, tiled=True)
    my_pos = own_index * tok_dev + jnp.arange(tok_dev, dtype=jnp.int32)
    source = jnp.arange(tokens, dtype=jnp.int32) // tok_dev
    land_col = (source * capacity + slot_all.reshape(-1))[None, :]
    hit = arrival_dest[None, :] == my_pos[:, None]
    col_of_pos = jnp.sum(jnp.where(hit, land_col, 0), axis=1)
    land_pick = (
        col_of_pos[:, None] == jnp.arange(owners * capacity, dtype=jnp.int32)[None, :]
    ).astype(projected.dtype)
    queries = jnp.dot(
        land_pick, incoming.reshape(owners * capacity, columns), preferred_element_type=jnp.float32
    )
    queries = queries.astype(projected.dtype).reshape(tok_dev, heads_here, HD)
    keys = keyval[:, 0, :].reshape(tokens, heads_here, HD)
    values = keyval[:, 1, :].reshape(tokens, heads_here, HD)
    scores = (
        jnp.einsum("qhd,khd->hqk", queries, keys, preferred_element_type=jnp.float32)
        * score_scale
    )
    bounds = jnp.cumsum(doc_lengths)
    key_block = arrival_dest // BLK
    key_doc = segment_of(arrival_dest, bounds)
    query_block = my_pos // BLK
    query_doc = segment_of(my_pos, bounds)
    same_doc = query_doc[:, None] == key_doc[None, :]
    window = jnp.zeros((tok_dev, tokens), jnp.int32)
    for step in (-1, 0, 1):
        near = (query_block + step) % blocks_all
        window = window + (key_block[None, :] == near[:, None]).astype(jnp.int32)
    window = jnp.where(same_doc, window, 0)
    chosen = random_blocks[query_block]
    drawn = jnp.zeros((tok_dev, tokens), jnp.int32)
    for r in range(chosen.shape[1]):
        drawn = drawn + (key_block[None, :] == chosen[:, r][:, None]).astype(jnp.int32)
    glob_start = global_owner[0] * tok_dev
    in_glob = (arrival_dest >= glob_start) & (arrival_dest < glob_start + tok_dev)
    count = window + drawn + in_glob[None, :].astype(jnp.int32)
    live = count > 0
    near_scores = jnp.where(live[None], scores, big_negative)
    row_peak = jnp.max(near_scores, axis=2)
    near_exp = jnp.exp(near_scores - row_peak[..., None])
    count_f = count.astype(jnp.float32)[None]
    denominator = jnp.sum(near_exp * count_f, axis=2)
    weighted = near_exp.astype(jnp.bfloat16).astype(jnp.float32) * count_f
    weight_hi = weighted.astype(jnp.bfloat16)
    weight_lo = (weighted - weight_hi.astype(jnp.float32)).astype(jnp.bfloat16)
    mixed_sum = jnp.einsum("hqk,khd->qhd", weight_hi, values, preferred_element_type=jnp.float32)
    mixed_sum = mixed_sum + jnp.einsum(
        "hqk,khd->qhd", weight_lo, values, preferred_element_type=jnp.float32
    )
    sparse = (mixed_sum / jnp.transpose(denominator)[..., None]).reshape(tok_dev, columns)
    sparse = sparse.astype(jnp.bfloat16)
    glob_peak = jnp.max(scores, axis=2)
    glob_exp = jnp.exp(scores - glob_peak[..., None])
    glob_total = jnp.sum(glob_exp, axis=2)
    glob_accum = jnp.einsum(
        "hqk,khd->qhd", glob_exp, values.astype(jnp.float32), precision=lax.Precision.HIGHEST
    )
    glob_out = (glob_accum / jnp.transpose(glob_total)[..., None]).reshape(tok_dev, columns)
    glob_out = glob_out.astype(jnp.bfloat16)
    attn_rows = jnp.where(own_index == global_owner[0], glob_out, sparse)
    return head_sum(jnp.dot(attn_rows, out_weight, preferred_element_type=jnp.float32))


def head_sum(partial):
    members = lax.axis_size("head")
    if members & (members - 1):
        return lax.psum_scatter(
            partial.astype(jnp.bfloat16), "head", scatter_dimension=0, tiled=True
        )
    me = lax.axis_index("head")
    bit = members // 2
    while bit >= 1:
        half = partial.shape[0] // 2
        upper = (me & bit) != 0
        keep = jnp.where(upper, partial[half:], partial[:half])
        send = jnp.where(upper, partial[:half], partial[half:]).astype(jnp.bfloat16)
        got = lax.ppermute(send, "head", [(i, i ^ bit) for i in range(members)])
        partial = keep + got.astype(jnp.float32)
        bit //= 2
    return partial.astype(jnp.bfloat16)


GATHER_LIMIT = 16 * 2**20


def shards(projected, destination, doc_lengths, random_blocks, global_owner, out_weight):
    gathered_bytes = lax.axis_size("seq") * projected.size * projected.dtype.itemsize
    if gathered_bytes <= GATHER_LIMIT:
        return gathered_plan(
            projected, destination, doc_lengths, random_blocks, global_owner, out_weight
        )
    return shards_ring(projected, destination, doc_lengths, random_blocks, global_owner, out_weight)


def solution(mesh):
    in_specs = (P("seq", None, "head"), P("seq"), P(), P(), P(), P("head", None))
    out_specs = P(("seq", "head"), None)
    return jax.shard_map(shards, mesh=mesh, in_specs=in_specs, out_specs=out_specs, check_vma=False)
```

```python
import math

import jax
import jax.numpy as jnp
from jax import lax
from jax.sharding import PartitionSpec as P

HD = 128
BLK = 128
R = 3
RDEV = 2


big_negative = -1e30


def from_behind(block, axis, distance):
    devices = range(lax.axis_size(axis))
    route = [((i - distance) % len(devices), i) for i in devices]
    return lax.ppermute(block, axis, route)


def from_root(x, axis, root):
    mine = lax.axis_index(axis) == root
    return lax.psum(jnp.where(mine, x, jnp.zeros_like(x)), axis)


def combined_all(x, axis, combine):
    everything = jax.tree.map(lambda part: lax.all_gather(part, axis), x)
    first = jax.tree.map(lambda part: part[0], everything)

    def step(k, so_far):
        return combine(so_far, jax.tree.map(lambda part: part[k], everything))

    return lax.fori_loop(1, lax.axis_size(axis), step, first)


def segment_of(positions, bounds):
    return jnp.sum((bounds[None, :] <= positions[:, None]).astype(jnp.int32), axis=1)


def combine_parts(left_part, right_part):
    top_left, total_left, accum_left = left_part
    top_right, total_right, accum_right = right_part
    row_peak = jnp.maximum(top_left, top_right)
    factor_left = jnp.exp(top_left - row_peak)
    factor_right = jnp.exp(top_right - row_peak)
    return (
        row_peak,
        total_left * factor_left + total_right * factor_right,
        accum_left * factor_left[:, :, None] + accum_right * factor_right[:, :, None],
    )


def shards_ring(projected, destination, doc_lengths, random_blocks, global_owner, out_weight):
    owners = lax.axis_size("seq")
    own_index = lax.axis_index("seq")
    tok_dev = projected.shape[0]
    columns = projected.shape[2]
    heads_here = columns // HD
    per_dev = tok_dev // BLK
    blocks_all = owners * per_dev
    capacity = 2 * (tok_dev // owners)
    score_scale = 1.0 / math.sqrt(HD)
    target_owner = destination // tok_dev
    onehot = (target_owner[:, None] == jnp.arange(owners, dtype=jnp.int32)[None, :]).astype(
        jnp.int32
    )
    before = jnp.cumsum(onehot, axis=0) - onehot
    slot_rank = jnp.sum(before * onehot, axis=1)
    outgoing = (
        jnp.zeros((owners, capacity, 3, columns), projected.dtype)
        .at[target_owner, slot_rank]
        .set(projected)
    )
    slots = (
        jnp.full((owners, capacity), -1, jnp.int32)
        .at[target_owner, slot_rank]
        .set(destination % tok_dev)
    )
    incoming, landing = (
        lax.all_to_all(outgoing, "seq", split_axis=0, concat_axis=0, tiled=True),
        lax.all_to_all(slots, "seq", split_axis=0, concat_axis=0, tiled=True),
    )
    landing = landing.reshape(-1)
    landing = jnp.where(landing >= 0, landing, tok_dev)
    routed = (
        jnp.zeros((tok_dev, 3, columns), projected.dtype)
        .at[landing]
        .set(incoming.reshape(owners * capacity, 3, columns), mode="drop")
    )
    keyval = routed[:, 1:, :]
    fetched = {0: keyval}
    offsets = list(range(-RDEV, 0)) + list(range(1, RDEV + 1))
    for offset in offsets:
        fetched[offset] = from_behind(keyval, "seq", -offset)
    band_blocks = jnp.stack([fetched[offset] for offset in range(-RDEV, RDEV + 1)])
    block_ids = own_index * per_dev + jnp.arange(per_dev, dtype=jnp.int32)
    local_pick = jnp.arange(per_dev, dtype=jnp.int32) + RDEV * per_dev
    window_pick = local_pick[:, None] + jnp.arange(-1, 2, dtype=jnp.int32)[None, :]
    chosen_rand = lax.dynamic_slice_in_dim(random_blocks, own_index * per_dev, per_dev, 0)
    away_dev = (chosen_rand // per_dev - own_index) % owners
    away_dev = jnp.where(away_dev > owners // 2, away_dev - owners, away_dev)
    rand_pick = (away_dev + RDEV) * per_dev + chosen_rand % per_dev
    block_picks = jnp.concatenate([window_pick, rand_pick], axis=1)
    gathered = jnp.take(band_blocks, block_picks, axis=0)
    near_keys = gathered[:, :, :, 0, :].reshape(per_dev, (3 + R) * BLK, heads_here, HD)
    near_values = gathered[:, :, :, 1, :].reshape(per_dev, (3 + R) * BLK, heads_here, HD)
    owner_dev = global_owner[0]
    global_rows = from_root(routed, "seq", owner_dev)
    glob_keys = global_rows[:, 1, :].reshape(tok_dev, heads_here, HD)
    glob_values = global_rows[:, 2, :].reshape(tok_dev, heads_here, HD)
    queries = routed[:, 0, :].reshape(per_dev, BLK, heads_here, HD)
    near_scores = (
        jnp.einsum("bqhd,bkhd->bhqk", queries, near_keys, preferred_element_type=jnp.float32)
        * score_scale
    )
    far_scores = (
        jnp.einsum("bqhd,khd->bhqk", queries, glob_keys, preferred_element_type=jnp.float32)
        * score_scale
    )
    bounds = jnp.cumsum(doc_lengths)
    query_pos = own_index * tok_dev + jnp.arange(tok_dev, dtype=jnp.int32)
    query_doc = segment_of(query_pos, bounds).reshape(per_dev, BLK)
    window_blocks = (block_ids[:, None] + jnp.arange(-1, 2, dtype=jnp.int32)[None, :]) % blocks_all
    key_pos = (
        window_blocks[:, :, None] * BLK + jnp.arange(BLK, dtype=jnp.int32)[None, None, :]
    ).reshape(-1)
    key_doc = segment_of(key_pos, bounds).reshape(per_dev, 3 * BLK)
    same_doc = query_doc[:, :, None] == key_doc[:, None, :]
    allowed = jnp.concatenate(
        [same_doc, jnp.ones((per_dev, BLK, R * BLK), dtype=jnp.bool_)], axis=2
    )
    near_scores = jnp.where(allowed[:, None], near_scores, big_negative)
    row_peak = jnp.maximum(jnp.max(near_scores, axis=3), jnp.max(far_scores, axis=3))
    near_exp = jnp.exp(near_scores - row_peak[..., None])
    far_exp = jnp.exp(far_scores - row_peak[..., None])
    denominator = jnp.sum(near_exp, axis=3) + jnp.sum(far_exp, axis=3)
    mixed_sum = jnp.einsum(
        "bhqk,bkhd->bqhd",
        near_exp.astype(jnp.bfloat16),
        near_values,
        preferred_element_type=jnp.float32,
    )
    mixed_sum = mixed_sum + jnp.einsum(
        "bhqk,khd->bqhd",
        far_exp.astype(jnp.bfloat16),
        glob_values,
        preferred_element_type=jnp.float32,
    )
    sparse = (mixed_sum / jnp.transpose(denominator, (0, 2, 1))[..., None]).reshape(
        tok_dev, columns
    )
    sparse = sparse.astype(jnp.bfloat16)
    glob_queries = global_rows[:, 0, :].reshape(tok_dev, heads_here, HD)
    local_keys = routed[:, 1, :].reshape(tok_dev, heads_here, HD)
    local_values = routed[:, 2, :].reshape(tok_dev, heads_here, HD).astype(jnp.float32)
    all_scores = (
        jnp.einsum("qhd,khd->hqk", glob_queries, local_keys, preferred_element_type=jnp.float32)
        * score_scale
    )
    local_peak = jnp.max(all_scores, axis=2)
    weights = jnp.exp(all_scores - local_peak[..., None])
    part_total = jnp.sum(weights, axis=2)
    part_accum = jnp.einsum("hqk,khd->hqd", weights, local_values, precision=lax.Precision.HIGHEST)
    peak_all, total_all, accum_all = combined_all(
        (local_peak, part_total, part_accum), "seq", combine_parts
    )
    glob_out = jnp.transpose(accum_all / total_all[..., None], (1, 0, 2)).reshape(tok_dev, columns)
    glob_out = glob_out.astype(jnp.bfloat16)
    attn_rows = jnp.where(own_index == owner_dev, glob_out, sparse)
    return lax.psum_scatter(
        jnp.dot(attn_rows, out_weight, preferred_element_type=jnp.float32).astype(jnp.bfloat16),
        "head",
        scatter_dimension=0,
        tiled=True,
    )


def gathered_plan(projected, destination, doc_lengths, random_blocks, global_owner, out_weight):
    owners = lax.axis_size("seq")
    own_index = lax.axis_index("seq")
    tok_dev = projected.shape[0]
    columns = projected.shape[2]
    heads_here = columns // HD
    tokens = owners * tok_dev
    blocks_all = tokens // BLK
    score_scale = 1.0 / math.sqrt(HD)
    capacity = 2 * (tok_dev // owners)
    arrival_dest = lax.all_gather(destination, "seq", tiled=True)
    keyval = lax.all_gather(projected[:, 1:, :], "seq", tiled=True)
    target_all = arrival_dest.reshape(owners, tok_dev) // tok_dev
    onehot = (target_all[:, :, None] == jnp.arange(owners, dtype=jnp.int32)).astype(jnp.int32)
    slot_all = jnp.sum((jnp.cumsum(onehot, axis=1) - onehot) * onehot, axis=2)
    target = destination // tok_dev
    mine = (target[:, None] == jnp.arange(owners, dtype=jnp.int32)[None, :]).astype(jnp.int32)
    slot = jnp.sum((jnp.cumsum(mine, axis=0) - mine) * mine, axis=1)
    send_col = target * capacity + slot
    send_pick = (
        jnp.arange(owners * capacity, dtype=jnp.int32)[:, None] == send_col[None, :]
    ).astype(projected.dtype)
    outgoing = jnp.dot(send_pick, projected[:, 0, :], preferred_element_type=jnp.float32)
    outgoing = outgoing.astype(projected.dtype).reshape(owners, capacity, columns)
    incoming = lax.all_to_all(outgoing, "seq", split_axis=0, concat_axis=0, tiled=True)
    my_pos = own_index * tok_dev + jnp.arange(tok_dev, dtype=jnp.int32)
    source = jnp.arange(tokens, dtype=jnp.int32) // tok_dev
    land_col = (source * capacity + slot_all.reshape(-1))[None, :]
    hit = arrival_dest[None, :] == my_pos[:, None]
    col_of_pos = jnp.sum(jnp.where(hit, land_col, 0), axis=1)
    land_pick = (
        col_of_pos[:, None] == jnp.arange(owners * capacity, dtype=jnp.int32)[None, :]
    ).astype(projected.dtype)
    queries = jnp.dot(
        land_pick, incoming.reshape(owners * capacity, columns), preferred_element_type=jnp.float32
    )
    queries = queries.astype(projected.dtype).reshape(tok_dev, heads_here, HD)
    keys = keyval[:, 0, :].reshape(tokens, heads_here, HD)
    values = keyval[:, 1, :].reshape(tokens, heads_here, HD)
    scores = (
        jnp.einsum("qhd,khd->hqk", queries, keys, preferred_element_type=jnp.float32)
        * score_scale
    )
    bounds = jnp.cumsum(doc_lengths)
    key_block = arrival_dest // BLK
    key_doc = segment_of(arrival_dest, bounds)
    query_block = my_pos // BLK
    query_doc = segment_of(my_pos, bounds)
    same_doc = query_doc[:, None] == key_doc[None, :]
    window = jnp.zeros((tok_dev, tokens), jnp.int32)
    for step in (-1, 0, 1):
        near = (query_block + step) % blocks_all
        window = window + (key_block[None, :] == near[:, None]).astype(jnp.int32)
    window = jnp.where(same_doc, window, 0)
    chosen = random_blocks[query_block]
    drawn = jnp.zeros((tok_dev, tokens), jnp.int32)
    for r in range(chosen.shape[1]):
        drawn = drawn + (key_block[None, :] == chosen[:, r][:, None]).astype(jnp.int32)
    glob_start = global_owner[0] * tok_dev
    in_glob = (arrival_dest >= glob_start) & (arrival_dest < glob_start + tok_dev)
    holds_glob = own_index == global_owner[0]
    count = window + drawn + in_glob[None, :].astype(jnp.int32)
    count = jnp.where(holds_glob, 1, count)
    live = count > 0
    near_scores = jnp.where(live[None], scores, big_negative)
    row_peak = jnp.max(near_scores, axis=2)
    near_exp = jnp.exp(near_scores - row_peak[..., None])
    count_f = count.astype(jnp.float32)[None]
    denominator = jnp.sum(near_exp * count_f, axis=2)
    rounded = jnp.where(holds_glob, near_exp, near_exp.astype(jnp.bfloat16).astype(jnp.float32))
    weighted = rounded * count_f
    weight_hi = weighted.astype(jnp.bfloat16)
    weight_lo = (weighted - weight_hi.astype(jnp.float32)).astype(jnp.bfloat16)
    mixed_sum = jnp.einsum("hqk,khd->qhd", weight_hi, values, preferred_element_type=jnp.float32)
    mixed_sum = mixed_sum + jnp.einsum(
        "hqk,khd->qhd", weight_lo, values, preferred_element_type=jnp.float32
    )
    attn_rows = (mixed_sum / jnp.transpose(denominator)[..., None]).reshape(tok_dev, columns)
    attn_rows = attn_rows.astype(jnp.bfloat16)
    return head_sum(jnp.dot(attn_rows, out_weight, preferred_element_type=jnp.float32))


def head_sum(partial):
    members = lax.axis_size("head")
    if members & (members - 1):
        return lax.psum_scatter(
            partial.astype(jnp.bfloat16), "head", scatter_dimension=0, tiled=True
        )
    me = lax.axis_index("head")
    bit = members // 2
    while bit >= 1:
        half = partial.shape[0] // 2
        upper = (me & bit) != 0
        keep = jnp.where(upper, partial[half:], partial[:half])
        send = jnp.where(upper, partial[:half], partial[half:]).astype(jnp.bfloat16)
        got = lax.ppermute(send, "head", [(i, i ^ bit) for i in range(members)])
        partial = keep + got.astype(jnp.float32)
        bit //= 2
    return partial.astype(jnp.bfloat16)


GATHER_LIMIT = 16 * 2**20


def shards(projected, destination, doc_lengths, random_blocks, global_owner, out_weight):
    gathered_bytes = lax.axis_size("seq") * projected.size * projected.dtype.itemsize
    if gathered_bytes <= GATHER_LIMIT:
        return gathered_plan(
            projected, destination, doc_lengths, random_blocks, global_owner, out_weight
        )
    return shards_ring(projected, destination, doc_lengths, random_blocks, global_owner, out_weight)


def solution(mesh):
    in_specs = (P("seq", None, "head"), P("seq"), P(), P(), P(), P("head", None))
    out_specs = P(("seq", "head"), None)
    return jax.shard_map(shards, mesh=mesh, in_specs=in_specs, out_specs=out_specs, check_vma=False)
```

```python
import math

import jax
import jax.numpy as jnp
from jax import lax
from jax.sharding import PartitionSpec as P

HD = 128
BLK = 128
R = 3
RDEV = 2


big_negative = -1e30


def from_behind(block, axis, distance):
    devices = range(lax.axis_size(axis))
    route = [((i - distance) % len(devices), i) for i in devices]
    return lax.ppermute(block, axis, route)


def from_root(x, axis, root):
    mine = lax.axis_index(axis) == root
    return lax.psum(jnp.where(mine, x, jnp.zeros_like(x)), axis)


def combined_all(x, axis, combine):
    everything = jax.tree.map(lambda part: lax.all_gather(part, axis), x)
    first = jax.tree.map(lambda part: part[0], everything)

    def step(k, so_far):
        return combine(so_far, jax.tree.map(lambda part: part[k], everything))

    return lax.fori_loop(1, lax.axis_size(axis), step, first)


def segment_of(positions, bounds):
    return jnp.sum((bounds[None, :] <= positions[:, None]).astype(jnp.int32), axis=1)


def combine_parts(left_part, right_part):
    top_left, total_left, accum_left = left_part
    top_right, total_right, accum_right = right_part
    row_peak = jnp.maximum(top_left, top_right)
    factor_left = jnp.exp(top_left - row_peak)
    factor_right = jnp.exp(top_right - row_peak)
    return (
        row_peak,
        total_left * factor_left + total_right * factor_right,
        accum_left * factor_left[:, :, None] + accum_right * factor_right[:, :, None],
    )


def shards_ring(projected, destination, doc_lengths, random_blocks, global_owner, out_weight):
    owners = lax.axis_size("seq")
    own_index = lax.axis_index("seq")
    tok_dev = projected.shape[0]
    columns = projected.shape[2]
    heads_here = columns // HD
    per_dev = tok_dev // BLK
    blocks_all = owners * per_dev
    capacity = 2 * (tok_dev // owners)
    score_scale = 1.0 / math.sqrt(HD)
    target_owner = destination // tok_dev
    onehot = (target_owner[:, None] == jnp.arange(owners, dtype=jnp.int32)[None, :]).astype(
        jnp.int32
    )
    before = jnp.cumsum(onehot, axis=0) - onehot
    slot_rank = jnp.sum(before * onehot, axis=1)
    outgoing = (
        jnp.zeros((owners, capacity, 3, columns), projected.dtype)
        .at[target_owner, slot_rank]
        .set(projected)
    )
    slots = (
        jnp.full((owners, capacity), -1, jnp.int32)
        .at[target_owner, slot_rank]
        .set(destination % tok_dev)
    )
    incoming, landing = (
        lax.all_to_all(outgoing, "seq", split_axis=0, concat_axis=0, tiled=True),
        lax.all_to_all(slots, "seq", split_axis=0, concat_axis=0, tiled=True),
    )
    landing = landing.reshape(-1)
    landing = jnp.where(landing >= 0, landing, tok_dev)
    routed = (
        jnp.zeros((tok_dev, 3, columns), projected.dtype)
        .at[landing]
        .set(incoming.reshape(owners * capacity, 3, columns), mode="drop")
    )
    keyval = routed[:, 1:, :]
    fetched = {0: keyval}
    offsets = list(range(-RDEV, 0)) + list(range(1, RDEV + 1))
    for offset in offsets:
        fetched[offset] = from_behind(keyval, "seq", -offset)
    band_blocks = jnp.stack([fetched[offset] for offset in range(-RDEV, RDEV + 1)])
    block_ids = own_index * per_dev + jnp.arange(per_dev, dtype=jnp.int32)
    local_pick = jnp.arange(per_dev, dtype=jnp.int32) + RDEV * per_dev
    window_pick = local_pick[:, None] + jnp.arange(-1, 2, dtype=jnp.int32)[None, :]
    chosen_rand = lax.dynamic_slice_in_dim(random_blocks, own_index * per_dev, per_dev, 0)
    away_dev = (chosen_rand // per_dev - own_index) % owners
    away_dev = jnp.where(away_dev > owners // 2, away_dev - owners, away_dev)
    rand_pick = (away_dev + RDEV) * per_dev + chosen_rand % per_dev
    block_picks = jnp.concatenate([window_pick, rand_pick], axis=1)
    gathered = jnp.take(band_blocks, block_picks, axis=0)
    near_keys = gathered[:, :, :, 0, :].reshape(per_dev, (3 + R) * BLK, heads_here, HD)
    near_values = gathered[:, :, :, 1, :].reshape(per_dev, (3 + R) * BLK, heads_here, HD)
    owner_dev = global_owner[0]
    global_rows = from_root(routed, "seq", owner_dev)
    glob_keys = global_rows[:, 1, :].reshape(tok_dev, heads_here, HD)
    glob_values = global_rows[:, 2, :].reshape(tok_dev, heads_here, HD)
    queries = routed[:, 0, :].reshape(per_dev, BLK, heads_here, HD)
    near_scores = (
        jnp.einsum("bqhd,bkhd->bhqk", queries, near_keys, preferred_element_type=jnp.float32)
        * score_scale
    )
    far_scores = (
        jnp.einsum("bqhd,khd->bhqk", queries, glob_keys, preferred_element_type=jnp.float32)
        * score_scale
    )
    bounds = jnp.cumsum(doc_lengths)
    query_pos = own_index * tok_dev + jnp.arange(tok_dev, dtype=jnp.int32)
    query_doc = segment_of(query_pos, bounds).reshape(per_dev, BLK)
    window_blocks = (block_ids[:, None] + jnp.arange(-1, 2, dtype=jnp.int32)[None, :]) % blocks_all
    key_pos = (
        window_blocks[:, :, None] * BLK + jnp.arange(BLK, dtype=jnp.int32)[None, None, :]
    ).reshape(-1)
    key_doc = segment_of(key_pos, bounds).reshape(per_dev, 3 * BLK)
    same_doc = query_doc[:, :, None] == key_doc[:, None, :]
    allowed = jnp.concatenate(
        [same_doc, jnp.ones((per_dev, BLK, R * BLK), dtype=jnp.bool_)], axis=2
    )
    near_scores = jnp.where(allowed[:, None], near_scores, big_negative)
    row_peak = jnp.maximum(jnp.max(near_scores, axis=3), jnp.max(far_scores, axis=3))
    near_exp = jnp.exp(near_scores - row_peak[..., None])
    far_exp = jnp.exp(far_scores - row_peak[..., None])
    denominator = jnp.sum(near_exp, axis=3) + jnp.sum(far_exp, axis=3)
    mixed_sum = jnp.einsum(
        "bhqk,bkhd->bqhd",
        near_exp.astype(jnp.bfloat16),
        near_values,
        preferred_element_type=jnp.float32,
    )
    mixed_sum = mixed_sum + jnp.einsum(
        "bhqk,khd->bqhd",
        far_exp.astype(jnp.bfloat16),
        glob_values,
        preferred_element_type=jnp.float32,
    )
    sparse = (mixed_sum / jnp.transpose(denominator, (0, 2, 1))[..., None]).reshape(
        tok_dev, columns
    )
    sparse = sparse.astype(jnp.bfloat16)
    glob_queries = global_rows[:, 0, :].reshape(tok_dev, heads_here, HD)
    local_keys = routed[:, 1, :].reshape(tok_dev, heads_here, HD)
    local_values = routed[:, 2, :].reshape(tok_dev, heads_here, HD).astype(jnp.float32)
    all_scores = (
        jnp.einsum("qhd,khd->hqk", glob_queries, local_keys, preferred_element_type=jnp.float32)
        * score_scale
    )
    local_peak = jnp.max(all_scores, axis=2)
    weights = jnp.exp(all_scores - local_peak[..., None])
    part_total = jnp.sum(weights, axis=2)
    part_accum = jnp.einsum("hqk,khd->hqd", weights, local_values, precision=lax.Precision.HIGHEST)
    peak_all, total_all, accum_all = combined_all(
        (local_peak, part_total, part_accum), "seq", combine_parts
    )
    glob_out = jnp.transpose(accum_all / total_all[..., None], (1, 0, 2)).reshape(tok_dev, columns)
    glob_out = glob_out.astype(jnp.bfloat16)
    attn_rows = jnp.where(own_index == owner_dev, glob_out, sparse)
    return lax.psum_scatter(
        jnp.dot(attn_rows, out_weight, preferred_element_type=jnp.float32).astype(jnp.bfloat16),
        "head",
        scatter_dimension=0,
        tiled=True,
    )


def gathered_plan(projected, destination, doc_lengths, random_blocks, global_owner, out_weight):
    owners = lax.axis_size("seq")
    own_index = lax.axis_index("seq")
    tok_dev = projected.shape[0]
    columns = projected.shape[2]
    heads_here = columns // HD
    tokens = owners * tok_dev
    blocks_all = tokens // BLK
    score_scale = 1.0 / math.sqrt(HD)
    capacity = 2 * (tok_dev // owners)
    arrival_dest = lax.all_gather(destination, "seq", tiled=True)
    keyval = lax.all_gather(projected[:, 1:, :], "seq", tiled=True)
    target_all = arrival_dest.reshape(owners, tok_dev) // tok_dev
    onehot = (target_all[:, :, None] == jnp.arange(owners, dtype=jnp.int32)).astype(jnp.int32)
    slot_all = jnp.sum((jnp.cumsum(onehot, axis=1) - onehot) * onehot, axis=2)
    target = destination // tok_dev
    mine = (target[:, None] == jnp.arange(owners, dtype=jnp.int32)[None, :]).astype(jnp.int32)
    slot = jnp.sum((jnp.cumsum(mine, axis=0) - mine) * mine, axis=1)
    send_col = target * capacity + slot
    send_pick = (
        jnp.arange(owners * capacity, dtype=jnp.int32)[:, None] == send_col[None, :]
    ).astype(projected.dtype)
    outgoing = jnp.dot(send_pick, projected[:, 0, :], preferred_element_type=jnp.float32)
    outgoing = outgoing.astype(projected.dtype).reshape(owners, capacity, columns)
    incoming = lax.all_to_all(outgoing, "seq", split_axis=0, concat_axis=0, tiled=True)
    my_pos = own_index * tok_dev + jnp.arange(tok_dev, dtype=jnp.int32)
    source = jnp.arange(tokens, dtype=jnp.int32) // tok_dev
    land_col = (source * capacity + slot_all.reshape(-1))[None, :]
    hit = arrival_dest[None, :] == my_pos[:, None]
    col_of_pos = jnp.sum(jnp.where(hit, land_col, 0), axis=1)
    land_pick = (
        col_of_pos[:, None] == jnp.arange(owners * capacity, dtype=jnp.int32)[None, :]
    ).astype(projected.dtype)
    queries = jnp.dot(
        land_pick, incoming.reshape(owners * capacity, columns), preferred_element_type=jnp.float32
    )
    queries = queries.astype(projected.dtype).reshape(tok_dev, heads_here, HD)
    keys = keyval[:, 0, :].reshape(tokens, heads_here, HD)
    values = keyval[:, 1, :].reshape(tokens, heads_here, HD)
    scores = (
        jnp.einsum("qhd,khd->hqk", queries, keys, preferred_element_type=jnp.float32)
        * score_scale
    )
    bounds = jnp.cumsum(doc_lengths)
    key_block = arrival_dest // BLK
    key_doc = segment_of(arrival_dest, bounds)
    query_block = my_pos // BLK
    query_doc = segment_of(my_pos, bounds)
    same_doc = query_doc[:, None] == key_doc[None, :]
    window = jnp.zeros((tok_dev, tokens), jnp.int32)
    for step in (-1, 0, 1):
        near = (query_block + step) % blocks_all
        window = window + (key_block[None, :] == near[:, None]).astype(jnp.int32)
    window = jnp.where(same_doc, window, 0)
    chosen = random_blocks[query_block]
    drawn = jnp.zeros((tok_dev, tokens), jnp.int32)
    for r in range(chosen.shape[1]):
        drawn = drawn + (key_block[None, :] == chosen[:, r][:, None]).astype(jnp.int32)
    glob_start = global_owner[0] * tok_dev
    in_glob = (arrival_dest >= glob_start) & (arrival_dest < glob_start + tok_dev)
    holds_glob = own_index == global_owner[0]
    count = window + drawn + in_glob[None, :].astype(jnp.int32)
    count = jnp.where(holds_glob, 1, count)
    live = count > 0
    near_scores = jnp.where(live[None], scores, big_negative)
    row_peak = jnp.max(near_scores, axis=2)
    near_exp = jnp.exp(near_scores - row_peak[..., None])
    count_f = count.astype(jnp.float32)[None]
    denominator = jnp.sum(near_exp * count_f, axis=2)
    rounded = jnp.where(holds_glob, near_exp, near_exp.astype(jnp.bfloat16).astype(jnp.float32))
    weighted = rounded * count_f
    weight_hi = weighted.astype(jnp.bfloat16)
    weight_lo = (weighted - weight_hi.astype(jnp.float32)).astype(jnp.bfloat16)
    mixed_sum = jnp.einsum("hqk,khd->qhd", weight_hi, values, preferred_element_type=jnp.float32)
    mixed_sum = mixed_sum + jnp.einsum(
        "hqk,khd->qhd", weight_lo, values, preferred_element_type=jnp.float32
    )
    attn_rows = (mixed_sum / jnp.transpose(denominator)[..., None]).reshape(tok_dev, columns)
    attn_rows = attn_rows.astype(jnp.bfloat16)
    return head_sum(jnp.dot(attn_rows, out_weight, preferred_element_type=jnp.float32))


def head_sum(partial):
    members = lax.axis_size("head")
    if members & (members - 1):
        return lax.psum_scatter(
            partial.astype(jnp.bfloat16), "head", scatter_dimension=0, tiled=True
        )
    me = lax.axis_index("head")
    rows = partial.shape[0] // members
    partial = partial.reshape(members, rows, partial.shape[1])
    bit = 1
    while bit < members:
        pairs = partial.reshape(partial.shape[0] // 2, 2, rows, partial.shape[2])
        upper = (me & bit) != 0
        keep = jnp.where(upper, pairs[:, 1], pairs[:, 0])
        send = jnp.where(upper, pairs[:, 0], pairs[:, 1]).astype(jnp.bfloat16)
        got = lax.ppermute(send, "head", [(i, i ^ bit) for i in range(members)])
        partial = keep + got.astype(jnp.float32)
        bit *= 2
    partial = partial.reshape(rows, partial.shape[2])
    return partial.astype(jnp.bfloat16)


GATHER_LIMIT = 16 * 2**20


def shards(projected, destination, doc_lengths, random_blocks, global_owner, out_weight):
    gathered_bytes = lax.axis_size("seq") * projected.size * projected.dtype.itemsize
    if gathered_bytes <= GATHER_LIMIT:
        return gathered_plan(
            projected, destination, doc_lengths, random_blocks, global_owner, out_weight
        )
    return shards_ring(projected, destination, doc_lengths, random_blocks, global_owner, out_weight)


def solution(mesh):
    in_specs = (P("seq", None, "head"), P("seq"), P(), P(), P(), P("head", None))
    out_specs = P(("seq", "head"), None)
    return jax.shard_map(shards, mesh=mesh, in_specs=in_specs, out_specs=out_specs, check_vma=False)
```

```python
import math

import jax
import jax.numpy as jnp
from jax import lax
from jax.sharding import PartitionSpec as P

HD = 128
BLK = 128
R = 3
RDEV = 2


big_negative = -1e30


def from_behind(block, axis, distance):
    devices = range(lax.axis_size(axis))
    route = [((i - distance) % len(devices), i) for i in devices]
    return lax.ppermute(block, axis, route)


def from_root(x, axis, root):
    mine = lax.axis_index(axis) == root
    return lax.psum(jnp.where(mine, x, jnp.zeros_like(x)), axis)


def combined_all(x, axis, combine):
    everything = jax.tree.map(lambda part: lax.all_gather(part, axis), x)
    first = jax.tree.map(lambda part: part[0], everything)

    def step(k, so_far):
        return combine(so_far, jax.tree.map(lambda part: part[k], everything))

    return lax.fori_loop(1, lax.axis_size(axis), step, first)


def segment_of(positions, bounds):
    return jnp.sum((bounds[None, :] <= positions[:, None]).astype(jnp.int32), axis=1)


def combine_parts(left_part, right_part):
    top_left, total_left, accum_left = left_part
    top_right, total_right, accum_right = right_part
    row_peak = jnp.maximum(top_left, top_right)
    factor_left = jnp.exp(top_left - row_peak)
    factor_right = jnp.exp(top_right - row_peak)
    return (
        row_peak,
        total_left * factor_left + total_right * factor_right,
        accum_left * factor_left[:, :, None] + accum_right * factor_right[:, :, None],
    )


def shards_ring(projected, destination, doc_lengths, random_blocks, global_owner, out_weight):
    owners = lax.axis_size("seq")
    own_index = lax.axis_index("seq")
    tok_dev = projected.shape[0]
    columns = projected.shape[2]
    heads_here = columns // HD
    per_dev = tok_dev // BLK
    blocks_all = owners * per_dev
    capacity = 2 * (tok_dev // owners)
    score_scale = 1.0 / math.sqrt(HD)
    target_owner = destination // tok_dev
    onehot = (target_owner[:, None] == jnp.arange(owners, dtype=jnp.int32)[None, :]).astype(
        jnp.int32
    )
    before = jnp.cumsum(onehot, axis=0) - onehot
    slot_rank = jnp.sum(before * onehot, axis=1)
    outgoing = (
        jnp.zeros((owners, capacity, 3, columns), projected.dtype)
        .at[target_owner, slot_rank]
        .set(projected)
    )
    slots = (
        jnp.full((owners, capacity), -1, jnp.int32)
        .at[target_owner, slot_rank]
        .set(destination % tok_dev)
    )
    incoming, landing = (
        lax.all_to_all(outgoing, "seq", split_axis=0, concat_axis=0, tiled=True),
        lax.all_to_all(slots, "seq", split_axis=0, concat_axis=0, tiled=True),
    )
    landing = landing.reshape(-1)
    landing = jnp.where(landing >= 0, landing, tok_dev)
    routed = (
        jnp.zeros((tok_dev, 3, columns), projected.dtype)
        .at[landing]
        .set(incoming.reshape(owners * capacity, 3, columns), mode="drop")
    )
    keyval = routed[:, 1:, :]
    fetched = {0: keyval}
    offsets = list(range(-RDEV, 0)) + list(range(1, RDEV + 1))
    for offset in offsets:
        fetched[offset] = from_behind(keyval, "seq", -offset)
    band_blocks = jnp.stack([fetched[offset] for offset in range(-RDEV, RDEV + 1)])
    block_ids = own_index * per_dev + jnp.arange(per_dev, dtype=jnp.int32)
    local_pick = jnp.arange(per_dev, dtype=jnp.int32) + RDEV * per_dev
    window_pick = local_pick[:, None] + jnp.arange(-1, 2, dtype=jnp.int32)[None, :]
    chosen_rand = lax.dynamic_slice_in_dim(random_blocks, own_index * per_dev, per_dev, 0)
    away_dev = (chosen_rand // per_dev - own_index) % owners
    away_dev = jnp.where(away_dev > owners // 2, away_dev - owners, away_dev)
    rand_pick = (away_dev + RDEV) * per_dev + chosen_rand % per_dev
    block_picks = jnp.concatenate([window_pick, rand_pick], axis=1)
    gathered = jnp.take(band_blocks, block_picks, axis=0)
    near_keys = gathered[:, :, :, 0, :].reshape(per_dev, (3 + R) * BLK, heads_here, HD)
    near_values = gathered[:, :, :, 1, :].reshape(per_dev, (3 + R) * BLK, heads_here, HD)
    owner_dev = global_owner[0]
    global_rows = from_root(routed, "seq", owner_dev)
    glob_keys = global_rows[:, 1, :].reshape(tok_dev, heads_here, HD)
    glob_values = global_rows[:, 2, :].reshape(tok_dev, heads_here, HD)
    queries = routed[:, 0, :].reshape(per_dev, BLK, heads_here, HD)
    near_scores = (
        jnp.einsum("bqhd,bkhd->bhqk", queries, near_keys, preferred_element_type=jnp.float32)
        * score_scale
    )
    far_scores = (
        jnp.einsum("bqhd,khd->bhqk", queries, glob_keys, preferred_element_type=jnp.float32)
        * score_scale
    )
    bounds = jnp.cumsum(doc_lengths)
    query_pos = own_index * tok_dev + jnp.arange(tok_dev, dtype=jnp.int32)
    query_doc = segment_of(query_pos, bounds).reshape(per_dev, BLK)
    window_blocks = (block_ids[:, None] + jnp.arange(-1, 2, dtype=jnp.int32)[None, :]) % blocks_all
    key_pos = (
        window_blocks[:, :, None] * BLK + jnp.arange(BLK, dtype=jnp.int32)[None, None, :]
    ).reshape(-1)
    key_doc = segment_of(key_pos, bounds).reshape(per_dev, 3 * BLK)
    same_doc = query_doc[:, :, None] == key_doc[:, None, :]
    allowed = jnp.concatenate(
        [same_doc, jnp.ones((per_dev, BLK, R * BLK), dtype=jnp.bool_)], axis=2
    )
    near_scores = jnp.where(allowed[:, None], near_scores, big_negative)
    row_peak = jnp.maximum(jnp.max(near_scores, axis=3), jnp.max(far_scores, axis=3))
    near_exp = jnp.exp(near_scores - row_peak[..., None])
    far_exp = jnp.exp(far_scores - row_peak[..., None])
    denominator = jnp.sum(near_exp, axis=3) + jnp.sum(far_exp, axis=3)
    mixed_sum = jnp.einsum(
        "bhqk,bkhd->bqhd",
        near_exp.astype(jnp.bfloat16),
        near_values,
        preferred_element_type=jnp.float32,
    )
    mixed_sum = mixed_sum + jnp.einsum(
        "bhqk,khd->bqhd",
        far_exp.astype(jnp.bfloat16),
        glob_values,
        preferred_element_type=jnp.float32,
    )
    sparse = (mixed_sum / jnp.transpose(denominator, (0, 2, 1))[..., None]).reshape(
        tok_dev, columns
    )
    sparse = sparse.astype(jnp.bfloat16)
    glob_queries = global_rows[:, 0, :].reshape(tok_dev, heads_here, HD)
    local_keys = routed[:, 1, :].reshape(tok_dev, heads_here, HD)
    local_values = routed[:, 2, :].reshape(tok_dev, heads_here, HD).astype(jnp.float32)
    all_scores = (
        jnp.einsum("qhd,khd->hqk", glob_queries, local_keys, preferred_element_type=jnp.float32)
        * score_scale
    )
    local_peak = jnp.max(all_scores, axis=2)
    weights = jnp.exp(all_scores - local_peak[..., None])
    part_total = jnp.sum(weights, axis=2)
    part_accum = jnp.einsum("hqk,khd->hqd", weights, local_values, precision=lax.Precision.HIGHEST)
    peak_all, total_all, accum_all = combined_all(
        (local_peak, part_total, part_accum), "seq", combine_parts
    )
    glob_out = jnp.transpose(accum_all / total_all[..., None], (1, 0, 2)).reshape(tok_dev, columns)
    glob_out = glob_out.astype(jnp.bfloat16)
    attn_rows = jnp.where(own_index == owner_dev, glob_out, sparse)
    return lax.psum_scatter(
        jnp.dot(attn_rows, out_weight, preferred_element_type=jnp.float32).astype(jnp.bfloat16),
        "head",
        scatter_dimension=0,
        tiled=True,
    )


def gathered_plan(projected, destination, doc_lengths, random_blocks, global_owner, out_weight):
    owners = lax.axis_size("seq")
    own_index = lax.axis_index("seq")
    tok_dev = projected.shape[0]
    columns = projected.shape[2]
    heads_here = columns // HD
    tokens = owners * tok_dev
    blocks_all = tokens // BLK
    score_scale = 1.0 / math.sqrt(HD)
    capacity = 2 * (tok_dev // owners)
    arrival_dest = lax.all_gather(destination, "seq", tiled=True)
    keyval = lax.all_gather(projected[:, 1:, :], "seq", tiled=True)
    target_all = arrival_dest.reshape(owners, tok_dev) // tok_dev
    onehot = (target_all[:, :, None] == jnp.arange(owners, dtype=jnp.int32)).astype(jnp.int32)
    slot_all = jnp.sum((jnp.cumsum(onehot, axis=1) - onehot) * onehot, axis=2)
    target = destination // tok_dev
    mine = (target[:, None] == jnp.arange(owners, dtype=jnp.int32)[None, :]).astype(jnp.int32)
    slot = jnp.sum((jnp.cumsum(mine, axis=0) - mine) * mine, axis=1)
    send_col = target * capacity + slot
    send_pick = (
        jnp.arange(owners * capacity, dtype=jnp.int32)[:, None] == send_col[None, :]
    ).astype(projected.dtype)
    outgoing = jnp.dot(send_pick, projected[:, 0, :], preferred_element_type=jnp.float32)
    outgoing = outgoing.astype(projected.dtype).reshape(owners, capacity, columns)
    incoming = lax.all_to_all(outgoing, "seq", split_axis=0, concat_axis=0, tiled=True)
    my_pos = own_index * tok_dev + jnp.arange(tok_dev, dtype=jnp.int32)
    source = jnp.arange(tokens, dtype=jnp.int32) // tok_dev
    land_col = (source * capacity + slot_all.reshape(-1))[None, :]
    hit = arrival_dest[None, :] == my_pos[:, None]
    col_of_pos = jnp.sum(jnp.where(hit, land_col, 0), axis=1)
    land_pick = (
        col_of_pos[:, None] == jnp.arange(owners * capacity, dtype=jnp.int32)[None, :]
    ).astype(projected.dtype)
    queries = jnp.dot(
        land_pick, incoming.reshape(owners * capacity, columns), preferred_element_type=jnp.float32
    )
    queries = queries.astype(projected.dtype).reshape(tok_dev, heads_here, HD)
    keys = keyval[:, 0, :].reshape(tokens, heads_here, HD)
    values = keyval[:, 1, :].reshape(tokens, heads_here, HD)
    scores = (
        jnp.einsum("qhd,khd->hqk", queries, keys, preferred_element_type=jnp.float32)
        * score_scale
    )
    bounds = jnp.cumsum(doc_lengths)
    key_block = arrival_dest // BLK
    key_doc = segment_of(arrival_dest, bounds)
    query_block = my_pos // BLK
    query_doc = segment_of(my_pos, bounds)
    same_doc = query_doc[:, None] == key_doc[None, :]
    window = jnp.zeros((tok_dev, tokens), jnp.int32)
    for step in (-1, 0, 1):
        near = (query_block + step) % blocks_all
        window = window + (key_block[None, :] == near[:, None]).astype(jnp.int32)
    window = jnp.where(same_doc, window, 0)
    chosen = random_blocks[query_block]
    drawn = jnp.zeros((tok_dev, tokens), jnp.int32)
    for r in range(chosen.shape[1]):
        drawn = drawn + (key_block[None, :] == chosen[:, r][:, None]).astype(jnp.int32)
    glob_start = global_owner[0] * tok_dev
    in_glob = (arrival_dest >= glob_start) & (arrival_dest < glob_start + tok_dev)
    holds_glob = own_index == global_owner[0]
    count = window + drawn + in_glob[None, :].astype(jnp.int32)
    count = jnp.where(holds_glob, 1, count)
    live = count > 0
    near_scores = jnp.where(live[None], scores, big_negative)
    row_peak = jnp.max(near_scores, axis=2)
    near_exp = jnp.exp(near_scores - row_peak[..., None])
    count_f = count.astype(jnp.float32)[None]
    denominator = jnp.sum(near_exp * count_f, axis=2)
    rounded = jnp.where(holds_glob, near_exp, near_exp.astype(jnp.bfloat16).astype(jnp.float32))
    weighted = rounded * count_f
    weight_hi = weighted.astype(jnp.bfloat16)
    weight_lo = (weighted - weight_hi.astype(jnp.float32)).astype(jnp.bfloat16)
    mixed_sum = jnp.einsum("hqk,khd->qhd", weight_hi, values, preferred_element_type=jnp.float32)
    mixed_sum = mixed_sum + jnp.einsum(
        "hqk,khd->qhd", weight_lo, values, preferred_element_type=jnp.float32
    )
    attn_rows = (mixed_sum / jnp.transpose(denominator)[..., None]).reshape(tok_dev, columns)
    attn_rows = attn_rows.astype(jnp.bfloat16)
    projected_rows = jnp.dot(attn_rows, out_weight, preferred_element_type=jnp.float32)
    return head_sum(lax.optimization_barrier(projected_rows))


def head_sum(partial):
    members = lax.axis_size("head")
    if members & (members - 1):
        return lax.psum_scatter(
            partial.astype(jnp.bfloat16), "head", scatter_dimension=0, tiled=True
        )
    me = lax.axis_index("head")
    rows = partial.shape[0] // members
    partial = partial.reshape(members, rows, partial.shape[1])
    bit = 1
    while bit < members:
        pairs = partial.reshape(partial.shape[0] // 2, 2, rows, partial.shape[2])
        upper = (me & bit) != 0
        keep = jnp.where(upper, pairs[:, 1], pairs[:, 0])
        send = jnp.where(upper, pairs[:, 0], pairs[:, 1]).astype(jnp.bfloat16)
        got = lax.ppermute(send, "head", [(i, i ^ bit) for i in range(members)])
        partial = keep + got.astype(jnp.float32)
        bit *= 2
    partial = partial.reshape(rows, partial.shape[2])
    return partial.astype(jnp.bfloat16)


GATHER_LIMIT = 16 * 2**20


def shards(projected, destination, doc_lengths, random_blocks, global_owner, out_weight):
    gathered_bytes = lax.axis_size("seq") * projected.size * projected.dtype.itemsize
    if gathered_bytes <= GATHER_LIMIT:
        return gathered_plan(
            projected, destination, doc_lengths, random_blocks, global_owner, out_weight
        )
    return shards_ring(projected, destination, doc_lengths, random_blocks, global_owner, out_weight)


def solution(mesh):
    in_specs = (P("seq", None, "head"), P("seq"), P(), P(), P(), P("head", None))
    out_specs = P(("seq", "head"), None)
    return jax.shard_map(shards, mesh=mesh, in_specs=in_specs, out_specs=out_specs, check_vma=False)
```

```python
import math

import jax
import jax.numpy as jnp
from jax import lax
from jax.sharding import PartitionSpec as P

HD = 128
BLK = 128
R = 3
RDEV = 2


big_negative = -1e30


def from_behind(block, axis, distance):
    devices = range(lax.axis_size(axis))
    route = [((i - distance) % len(devices), i) for i in devices]
    return lax.ppermute(block, axis, route)


def from_root(x, axis, root):
    mine = lax.axis_index(axis) == root
    return lax.psum(jnp.where(mine, x, jnp.zeros_like(x)), axis)


def combined_all(x, axis, combine):
    everything = jax.tree.map(lambda part: lax.all_gather(part, axis), x)
    first = jax.tree.map(lambda part: part[0], everything)

    def step(k, so_far):
        return combine(so_far, jax.tree.map(lambda part: part[k], everything))

    return lax.fori_loop(1, lax.axis_size(axis), step, first)


def segment_of(positions, bounds):
    return jnp.sum((bounds[None, :] <= positions[:, None]).astype(jnp.int32), axis=1)


def combine_parts(left_part, right_part):
    top_left, total_left, accum_left = left_part
    top_right, total_right, accum_right = right_part
    row_peak = jnp.maximum(top_left, top_right)
    factor_left = jnp.exp(top_left - row_peak)
    factor_right = jnp.exp(top_right - row_peak)
    return (
        row_peak,
        total_left * factor_left + total_right * factor_right,
        accum_left * factor_left[:, :, None] + accum_right * factor_right[:, :, None],
    )


def shards_ring(projected, destination, doc_lengths, random_blocks, global_owner, out_weight):
    owners = lax.axis_size("seq")
    own_index = lax.axis_index("seq")
    tok_dev = projected.shape[0]
    columns = projected.shape[2]
    heads_here = columns // HD
    per_dev = tok_dev // BLK
    blocks_all = owners * per_dev
    capacity = 2 * (tok_dev // owners)
    score_scale = 1.0 / math.sqrt(HD)
    target_owner = destination // tok_dev
    onehot = (target_owner[:, None] == jnp.arange(owners, dtype=jnp.int32)[None, :]).astype(
        jnp.int32
    )
    before = jnp.cumsum(onehot, axis=0) - onehot
    slot_rank = jnp.sum(before * onehot, axis=1)
    outgoing = (
        jnp.zeros((owners, capacity, 3, columns), projected.dtype)
        .at[target_owner, slot_rank]
        .set(projected)
    )
    slots = (
        jnp.full((owners, capacity), -1, jnp.int32)
        .at[target_owner, slot_rank]
        .set(destination % tok_dev)
    )
    incoming, landing = (
        lax.all_to_all(outgoing, "seq", split_axis=0, concat_axis=0, tiled=True),
        lax.all_to_all(slots, "seq", split_axis=0, concat_axis=0, tiled=True),
    )
    landing = landing.reshape(-1)
    landing = jnp.where(landing >= 0, landing, tok_dev)
    routed = (
        jnp.zeros((tok_dev, 3, columns), projected.dtype)
        .at[landing]
        .set(incoming.reshape(owners * capacity, 3, columns), mode="drop")
    )
    keyval = routed[:, 1:, :]
    fetched = {0: keyval}
    offsets = list(range(-RDEV, 0)) + list(range(1, RDEV + 1))
    for offset in offsets:
        fetched[offset] = from_behind(keyval, "seq", -offset)
    band_blocks = jnp.stack([fetched[offset] for offset in range(-RDEV, RDEV + 1)])
    block_ids = own_index * per_dev + jnp.arange(per_dev, dtype=jnp.int32)
    local_pick = jnp.arange(per_dev, dtype=jnp.int32) + RDEV * per_dev
    window_pick = local_pick[:, None] + jnp.arange(-1, 2, dtype=jnp.int32)[None, :]
    chosen_rand = lax.dynamic_slice_in_dim(random_blocks, own_index * per_dev, per_dev, 0)
    away_dev = (chosen_rand // per_dev - own_index) % owners
    away_dev = jnp.where(away_dev > owners // 2, away_dev - owners, away_dev)
    rand_pick = (away_dev + RDEV) * per_dev + chosen_rand % per_dev
    block_picks = jnp.concatenate([window_pick, rand_pick], axis=1)
    gathered = jnp.take(band_blocks, block_picks, axis=0)
    near_keys = gathered[:, :, :, 0, :].reshape(per_dev, (3 + R) * BLK, heads_here, HD)
    near_values = gathered[:, :, :, 1, :].reshape(per_dev, (3 + R) * BLK, heads_here, HD)
    owner_dev = global_owner[0]
    global_rows = from_root(routed, "seq", owner_dev)
    glob_keys = global_rows[:, 1, :].reshape(tok_dev, heads_here, HD)
    glob_values = global_rows[:, 2, :].reshape(tok_dev, heads_here, HD)
    queries = routed[:, 0, :].reshape(per_dev, BLK, heads_here, HD)
    near_scores = (
        jnp.einsum("bqhd,bkhd->bhqk", queries, near_keys, preferred_element_type=jnp.float32)
        * score_scale
    )
    far_scores = (
        jnp.einsum("bqhd,khd->bhqk", queries, glob_keys, preferred_element_type=jnp.float32)
        * score_scale
    )
    bounds = jnp.cumsum(doc_lengths)
    query_pos = own_index * tok_dev + jnp.arange(tok_dev, dtype=jnp.int32)
    query_doc = segment_of(query_pos, bounds).reshape(per_dev, BLK)
    window_blocks = (block_ids[:, None] + jnp.arange(-1, 2, dtype=jnp.int32)[None, :]) % blocks_all
    key_pos = (
        window_blocks[:, :, None] * BLK + jnp.arange(BLK, dtype=jnp.int32)[None, None, :]
    ).reshape(-1)
    key_doc = segment_of(key_pos, bounds).reshape(per_dev, 3 * BLK)
    same_doc = query_doc[:, :, None] == key_doc[:, None, :]
    allowed = jnp.concatenate(
        [same_doc, jnp.ones((per_dev, BLK, R * BLK), dtype=jnp.bool_)], axis=2
    )
    near_scores = jnp.where(allowed[:, None], near_scores, big_negative)
    row_peak = jnp.maximum(jnp.max(near_scores, axis=3), jnp.max(far_scores, axis=3))
    near_exp = jnp.exp(near_scores - row_peak[..., None])
    far_exp = jnp.exp(far_scores - row_peak[..., None])
    denominator = jnp.sum(near_exp, axis=3) + jnp.sum(far_exp, axis=3)
    mixed_sum = jnp.einsum(
        "bhqk,bkhd->bqhd",
        near_exp.astype(jnp.bfloat16),
        near_values,
        preferred_element_type=jnp.float32,
    )
    mixed_sum = mixed_sum + jnp.einsum(
        "bhqk,khd->bqhd",
        far_exp.astype(jnp.bfloat16),
        glob_values,
        preferred_element_type=jnp.float32,
    )
    sparse = (mixed_sum / jnp.transpose(denominator, (0, 2, 1))[..., None]).reshape(
        tok_dev, columns
    )
    sparse = sparse.astype(jnp.bfloat16)
    glob_queries = global_rows[:, 0, :].reshape(tok_dev, heads_here, HD)
    local_keys = routed[:, 1, :].reshape(tok_dev, heads_here, HD)
    local_values = routed[:, 2, :].reshape(tok_dev, heads_here, HD).astype(jnp.float32)
    all_scores = (
        jnp.einsum("qhd,khd->hqk", glob_queries, local_keys, preferred_element_type=jnp.float32)
        * score_scale
    )
    local_peak = jnp.max(all_scores, axis=2)
    weights = jnp.exp(all_scores - local_peak[..., None])
    part_total = jnp.sum(weights, axis=2)
    part_accum = jnp.einsum("hqk,khd->hqd", weights, local_values, precision=lax.Precision.HIGHEST)
    peak_all, total_all, accum_all = combined_all(
        (local_peak, part_total, part_accum), "seq", combine_parts
    )
    glob_out = jnp.transpose(accum_all / total_all[..., None], (1, 0, 2)).reshape(tok_dev, columns)
    glob_out = glob_out.astype(jnp.bfloat16)
    attn_rows = jnp.where(own_index == owner_dev, glob_out, sparse)
    return lax.psum_scatter(
        jnp.dot(attn_rows, out_weight, preferred_element_type=jnp.float32).astype(jnp.bfloat16),
        "head",
        scatter_dimension=0,
        tiled=True,
    )


def gathered_plan(projected, destination, doc_lengths, random_blocks, global_owner, out_weight):
    owners = lax.axis_size("seq")
    own_index = lax.axis_index("seq")
    tok_dev = projected.shape[0]
    columns = projected.shape[2]
    heads_here = columns // HD
    tokens = owners * tok_dev
    blocks_all = tokens // BLK
    score_scale = 1.0 / math.sqrt(HD)
    capacity = 2 * (tok_dev // owners)
    arrival_dest = lax.all_gather(destination, "seq", tiled=True)
    keyval = lax.all_gather(projected[:, 1:, :], "seq", tiled=True)
    target_all = arrival_dest.reshape(owners, tok_dev) // tok_dev
    onehot = (target_all[:, :, None] == jnp.arange(owners, dtype=jnp.int32)).astype(jnp.int32)
    slot_all = jnp.sum((jnp.cumsum(onehot, axis=1) - onehot) * onehot, axis=2)
    target = destination // tok_dev
    mine = (target[:, None] == jnp.arange(owners, dtype=jnp.int32)[None, :]).astype(jnp.int32)
    slot = jnp.sum((jnp.cumsum(mine, axis=0) - mine) * mine, axis=1)
    send_col = target * capacity + slot
    send_pick = (
        jnp.arange(owners * capacity, dtype=jnp.int32)[:, None] == send_col[None, :]
    ).astype(projected.dtype)
    outgoing = jnp.dot(send_pick, projected[:, 0, :], preferred_element_type=jnp.float32)
    outgoing = outgoing.astype(projected.dtype).reshape(owners, capacity, columns)
    incoming = lax.all_to_all(outgoing, "seq", split_axis=0, concat_axis=0, tiled=True)
    source = jnp.arange(tokens, dtype=jnp.int32) // tok_dev
    land_col = source * capacity + slot_all.reshape(-1)
    flat_in = incoming.reshape(owners * capacity, columns)
    keys = keyval[:, 0, :].reshape(tokens, heads_here, HD)
    values = keyval[:, 1, :].reshape(tokens, heads_here, HD)
    bounds = jnp.cumsum(doc_lengths)
    key_block = arrival_dest // BLK
    key_doc = segment_of(arrival_dest, bounds)
    glob_start = global_owner[0] * tok_dev
    in_glob = (arrival_dest >= glob_start) & (arrival_dest < glob_start + tok_dev)
    holds_glob = own_index == global_owner[0]

    def attend(local_rows):
        rows = local_rows.shape[0]
        my_pos = own_index * tok_dev + local_rows
        hit = arrival_dest[None, :] == my_pos[:, None]
        col_of_pos = jnp.sum(jnp.where(hit, land_col[None, :], 0), axis=1)
        land_pick = (
            col_of_pos[:, None] == jnp.arange(owners * capacity, dtype=jnp.int32)[None, :]
        ).astype(projected.dtype)
        queries = jnp.dot(land_pick, flat_in, preferred_element_type=jnp.float32)
        queries = queries.astype(projected.dtype).reshape(rows, heads_here, HD)
        scores = (
            jnp.einsum("qhd,khd->hqk", queries, keys, preferred_element_type=jnp.float32)
            * score_scale
        )
        query_block = my_pos // BLK
        query_doc = segment_of(my_pos, bounds)
        same_doc = query_doc[:, None] == key_doc[None, :]
        window = jnp.zeros((rows, tokens), jnp.int32)
        for step in (-1, 0, 1):
            near = (query_block + step) % blocks_all
            window = window + (key_block[None, :] == near[:, None]).astype(jnp.int32)
        window = jnp.where(same_doc, window, 0)
        chosen = random_blocks[query_block]
        drawn = jnp.zeros((rows, tokens), jnp.int32)
        for r in range(chosen.shape[1]):
            drawn = drawn + (key_block[None, :] == chosen[:, r][:, None]).astype(jnp.int32)
        count = window + drawn + in_glob[None, :].astype(jnp.int32)
        count = jnp.where(holds_glob, 1, count)
        live = count > 0
        near_scores = jnp.where(live[None], scores, big_negative)
        row_peak = jnp.max(near_scores, axis=2)
        near_exp = jnp.exp(near_scores - row_peak[..., None])
        count_f = count.astype(jnp.float32)[None]
        denominator = jnp.sum(near_exp * count_f, axis=2)
        rounded = jnp.where(
            holds_glob, near_exp, near_exp.astype(jnp.bfloat16).astype(jnp.float32)
        )
        weighted = rounded * count_f
        weight_hi = weighted.astype(jnp.bfloat16)
        weight_lo = (weighted - weight_hi.astype(jnp.float32)).astype(jnp.bfloat16)
        mixed_sum = jnp.einsum(
            "hqk,khd->qhd", weight_hi, values, preferred_element_type=jnp.float32
        )
        mixed_sum = mixed_sum + jnp.einsum(
            "hqk,khd->qhd", weight_lo, values, preferred_element_type=jnp.float32
        )
        attn_rows = (mixed_sum / jnp.transpose(denominator)[..., None]).reshape(rows, columns)
        return attn_rows.astype(jnp.bfloat16)

    def project(local_rows):
        out = jnp.dot(attend(local_rows), out_weight, preferred_element_type=jnp.float32)
        return lax.optimization_barrier(out)

    members = lax.axis_size("head")
    if members & (members - 1):
        return head_sum(project(jnp.arange(tok_dev, dtype=jnp.int32)))
    me = lax.axis_index("head")
    rows_per = tok_dev // members
    stages = members.bit_length() - 1
    received = []
    for stage in range(stages + 1):
        if stage < stages:
            ahead = jnp.arange(members >> (stage + 1), dtype=jnp.int32)
            flip = ((me >> stage) & 1) ^ 1
            blocks = (ahead << (stage + 1)) | (flip << stage) | (me & ((1 << stage) - 1))
        else:
            blocks = jnp.reshape(me, (1,)).astype(jnp.int32)
        local_rows = (
            blocks[:, None] * rows_per + jnp.arange(rows_per, dtype=jnp.int32)[None, :]
        ).reshape(-1)
        part = project(local_rows).reshape(blocks.shape[0], rows_per, -1)
        for done, got in received:
            part = part + jnp.take(got, blocks >> (done + 1), axis=0)
        if stage == stages:
            return part.reshape(rows_per, -1).astype(jnp.bfloat16)
        pairs = [(i, i ^ (1 << stage)) for i in range(members)]
        got = lax.ppermute(part.astype(jnp.bfloat16), "head", pairs)
        received.append((stage, got.astype(jnp.float32)))


def head_sum(partial):
    members = lax.axis_size("head")
    if members & (members - 1):
        return lax.psum_scatter(
            partial.astype(jnp.bfloat16), "head", scatter_dimension=0, tiled=True
        )
    me = lax.axis_index("head")
    rows = partial.shape[0] // members
    partial = partial.reshape(members, rows, partial.shape[1])
    bit = 1
    while bit < members:
        pairs = partial.reshape(partial.shape[0] // 2, 2, rows, partial.shape[2])
        upper = (me & bit) != 0
        keep = jnp.where(upper, pairs[:, 1], pairs[:, 0])
        send = jnp.where(upper, pairs[:, 0], pairs[:, 1]).astype(jnp.bfloat16)
        got = lax.ppermute(send, "head", [(i, i ^ bit) for i in range(members)])
        partial = keep + got.astype(jnp.float32)
        bit *= 2
    partial = partial.reshape(rows, partial.shape[2])
    return partial.astype(jnp.bfloat16)


GATHER_LIMIT = 16 * 2**20


def shards(projected, destination, doc_lengths, random_blocks, global_owner, out_weight):
    gathered_bytes = lax.axis_size("seq") * projected.size * projected.dtype.itemsize
    if gathered_bytes <= GATHER_LIMIT:
        return gathered_plan(
            projected, destination, doc_lengths, random_blocks, global_owner, out_weight
        )
    return shards_ring(projected, destination, doc_lengths, random_blocks, global_owner, out_weight)


def solution(mesh):
    in_specs = (P("seq", None, "head"), P("seq"), P(), P(), P(), P("head", None))
    out_specs = P(("seq", "head"), None)
    return jax.shard_map(shards, mesh=mesh, in_specs=in_specs, out_specs=out_specs, check_vma=False)
```

```python
import math

import jax
import jax.numpy as jnp
from jax import lax
from jax.experimental.layout import Layout, with_layout_constraint
from jax.sharding import PartitionSpec as P

HD = 128
BLK = 128
R = 3
RDEV = 2


big_negative = -1e30


def from_behind(block, axis, distance):
    devices = range(lax.axis_size(axis))
    route = [((i - distance) % len(devices), i) for i in devices]
    return lax.ppermute(block, axis, route)


def from_root(x, axis, root):
    mine = lax.axis_index(axis) == root
    return lax.psum(jnp.where(mine, x, jnp.zeros_like(x)), axis)


def combined_all(x, axis, combine):
    everything = jax.tree.map(lambda part: lax.all_gather(part, axis), x)
    first = jax.tree.map(lambda part: part[0], everything)

    def step(k, so_far):
        return combine(so_far, jax.tree.map(lambda part: part[k], everything))

    return lax.fori_loop(1, lax.axis_size(axis), step, first)


def segment_of(positions, bounds):
    return jnp.sum((bounds[None, :] <= positions[:, None]).astype(jnp.int32), axis=1)


def combine_parts(left_part, right_part):
    top_left, total_left, accum_left = left_part
    top_right, total_right, accum_right = right_part
    row_peak = jnp.maximum(top_left, top_right)
    factor_left = jnp.exp(top_left - row_peak)
    factor_right = jnp.exp(top_right - row_peak)
    return (
        row_peak,
        total_left * factor_left + total_right * factor_right,
        accum_left * factor_left[:, :, None] + accum_right * factor_right[:, :, None],
    )


def shards_ring(projected, destination, doc_lengths, random_blocks, global_owner, out_weight):
    owners = lax.axis_size("seq")
    own_index = lax.axis_index("seq")
    tok_dev = projected.shape[0]
    columns = projected.shape[2]
    heads_here = columns // HD
    per_dev = tok_dev // BLK
    blocks_all = owners * per_dev
    capacity = 2 * (tok_dev // owners)
    score_scale = 1.0 / math.sqrt(HD)
    target_owner = destination // tok_dev
    onehot = (target_owner[:, None] == jnp.arange(owners, dtype=jnp.int32)[None, :]).astype(
        jnp.int32
    )
    before = jnp.cumsum(onehot, axis=0) - onehot
    slot_rank = jnp.sum(before * onehot, axis=1)
    outgoing = (
        jnp.zeros((owners, capacity, 3, columns), projected.dtype)
        .at[target_owner, slot_rank]
        .set(projected)
    )
    slots = (
        jnp.full((owners, capacity), -1, jnp.int32)
        .at[target_owner, slot_rank]
        .set(destination % tok_dev)
    )
    incoming, landing = (
        lax.all_to_all(outgoing, "seq", split_axis=0, concat_axis=0, tiled=True),
        lax.all_to_all(slots, "seq", split_axis=0, concat_axis=0, tiled=True),
    )
    landing = landing.reshape(-1)
    landing = jnp.where(landing >= 0, landing, tok_dev)
    routed = (
        jnp.zeros((tok_dev, 3, columns), projected.dtype)
        .at[landing]
        .set(incoming.reshape(owners * capacity, 3, columns), mode="drop")
    )
    keyval = routed[:, 1:, :]
    fetched = {0: keyval}
    offsets = list(range(-RDEV, 0)) + list(range(1, RDEV + 1))
    for offset in offsets:
        fetched[offset] = from_behind(keyval, "seq", -offset)
    band_blocks = jnp.stack([fetched[offset] for offset in range(-RDEV, RDEV + 1)])
    block_ids = own_index * per_dev + jnp.arange(per_dev, dtype=jnp.int32)
    local_pick = jnp.arange(per_dev, dtype=jnp.int32) + RDEV * per_dev
    window_pick = local_pick[:, None] + jnp.arange(-1, 2, dtype=jnp.int32)[None, :]
    chosen_rand = lax.dynamic_slice_in_dim(random_blocks, own_index * per_dev, per_dev, 0)
    away_dev = (chosen_rand // per_dev - own_index) % owners
    away_dev = jnp.where(away_dev > owners // 2, away_dev - owners, away_dev)
    rand_pick = (away_dev + RDEV) * per_dev + chosen_rand % per_dev
    block_picks = jnp.concatenate([window_pick, rand_pick], axis=1)
    gathered = jnp.take(band_blocks, block_picks, axis=0)
    near_keys = gathered[:, :, :, 0, :].reshape(per_dev, (3 + R) * BLK, heads_here, HD)
    near_values = gathered[:, :, :, 1, :].reshape(per_dev, (3 + R) * BLK, heads_here, HD)
    owner_dev = global_owner[0]
    global_rows = from_root(routed, "seq", owner_dev)
    glob_keys = global_rows[:, 1, :].reshape(tok_dev, heads_here, HD)
    glob_values = global_rows[:, 2, :].reshape(tok_dev, heads_here, HD)
    queries = routed[:, 0, :].reshape(per_dev, BLK, heads_here, HD)
    near_scores = (
        jnp.einsum("bqhd,bkhd->bhqk", queries, near_keys, preferred_element_type=jnp.float32)
        * score_scale
    )
    far_scores = (
        jnp.einsum("bqhd,khd->bhqk", queries, glob_keys, preferred_element_type=jnp.float32)
        * score_scale
    )
    bounds = jnp.cumsum(doc_lengths)
    query_pos = own_index * tok_dev + jnp.arange(tok_dev, dtype=jnp.int32)
    query_doc = segment_of(query_pos, bounds).reshape(per_dev, BLK)
    window_blocks = (block_ids[:, None] + jnp.arange(-1, 2, dtype=jnp.int32)[None, :]) % blocks_all
    key_pos = (
        window_blocks[:, :, None] * BLK + jnp.arange(BLK, dtype=jnp.int32)[None, None, :]
    ).reshape(-1)
    key_doc = segment_of(key_pos, bounds).reshape(per_dev, 3 * BLK)
    same_doc = query_doc[:, :, None] == key_doc[:, None, :]
    allowed = jnp.concatenate(
        [same_doc, jnp.ones((per_dev, BLK, R * BLK), dtype=jnp.bool_)], axis=2
    )
    near_scores = jnp.where(allowed[:, None], near_scores, big_negative)
    row_peak = jnp.maximum(jnp.max(near_scores, axis=3), jnp.max(far_scores, axis=3))
    near_exp = jnp.exp(near_scores - row_peak[..., None])
    far_exp = jnp.exp(far_scores - row_peak[..., None])
    denominator = jnp.sum(near_exp, axis=3) + jnp.sum(far_exp, axis=3)
    mixed_sum = jnp.einsum(
        "bhqk,bkhd->bqhd",
        near_exp.astype(jnp.bfloat16),
        near_values,
        preferred_element_type=jnp.float32,
    )
    mixed_sum = mixed_sum + jnp.einsum(
        "bhqk,khd->bqhd",
        far_exp.astype(jnp.bfloat16),
        glob_values,
        preferred_element_type=jnp.float32,
    )
    sparse = (mixed_sum / jnp.transpose(denominator, (0, 2, 1))[..., None]).reshape(
        tok_dev, columns
    )
    sparse = sparse.astype(jnp.bfloat16)
    glob_queries = global_rows[:, 0, :].reshape(tok_dev, heads_here, HD)
    local_keys = routed[:, 1, :].reshape(tok_dev, heads_here, HD)
    local_values = routed[:, 2, :].reshape(tok_dev, heads_here, HD).astype(jnp.float32)
    all_scores = (
        jnp.einsum("qhd,khd->hqk", glob_queries, local_keys, preferred_element_type=jnp.float32)
        * score_scale
    )
    local_peak = jnp.max(all_scores, axis=2)
    weights = jnp.exp(all_scores - local_peak[..., None])
    part_total = jnp.sum(weights, axis=2)
    part_accum = jnp.einsum("hqk,khd->hqd", weights, local_values, precision=lax.Precision.HIGHEST)
    peak_all, total_all, accum_all = combined_all(
        (local_peak, part_total, part_accum), "seq", combine_parts
    )
    glob_out = jnp.transpose(accum_all / total_all[..., None], (1, 0, 2)).reshape(tok_dev, columns)
    glob_out = glob_out.astype(jnp.bfloat16)
    attn_rows = jnp.where(own_index == owner_dev, glob_out, sparse)
    return lax.psum_scatter(
        jnp.dot(attn_rows, out_weight, preferred_element_type=jnp.float32).astype(jnp.bfloat16),
        "head",
        scatter_dimension=0,
        tiled=True,
    )


def gathered_plan(projected, destination, doc_lengths, random_blocks, global_owner, out_weight):
    owners = lax.axis_size("seq")
    own_index = lax.axis_index("seq")
    tok_dev = projected.shape[0]
    columns = projected.shape[2]
    heads_here = columns // HD
    tokens = owners * tok_dev
    blocks_all = tokens // BLK
    score_scale = 1.0 / math.sqrt(HD)
    capacity = 2 * (tok_dev // owners)
    arrival_dest = lax.all_gather(destination, "seq", tiled=True)
    keyval = lax.all_gather(projected[:, 1:, :], "seq", tiled=True)
    keyval = with_layout_constraint(keyval, Layout((1, 0, 2)))
    target_all = arrival_dest.reshape(owners, tok_dev) // tok_dev
    onehot = (target_all[:, :, None] == jnp.arange(owners, dtype=jnp.int32)).astype(jnp.int32)
    slot_all = jnp.sum((jnp.cumsum(onehot, axis=1) - onehot) * onehot, axis=2)
    target = destination // tok_dev
    mine = (target[:, None] == jnp.arange(owners, dtype=jnp.int32)[None, :]).astype(jnp.int32)
    slot = jnp.sum((jnp.cumsum(mine, axis=0) - mine) * mine, axis=1)
    send_col = target * capacity + slot
    send_pick = (
        jnp.arange(owners * capacity, dtype=jnp.int32)[:, None] == send_col[None, :]
    ).astype(projected.dtype)
    outgoing = jnp.dot(send_pick, projected[:, 0, :], preferred_element_type=jnp.float32)
    outgoing = outgoing.astype(projected.dtype).reshape(owners, capacity, columns)
    incoming = lax.all_to_all(outgoing, "seq", split_axis=0, concat_axis=0, tiled=True)
    my_pos = own_index * tok_dev + jnp.arange(tok_dev, dtype=jnp.int32)
    source = jnp.arange(tokens, dtype=jnp.int32) // tok_dev
    land_col = (source * capacity + slot_all.reshape(-1))[None, :]
    hit = arrival_dest[None, :] == my_pos[:, None]
    col_of_pos = jnp.sum(jnp.where(hit, land_col, 0), axis=1)
    land_pick = (
        col_of_pos[:, None] == jnp.arange(owners * capacity, dtype=jnp.int32)[None, :]
    ).astype(projected.dtype)
    queries = jnp.dot(
        land_pick, incoming.reshape(owners * capacity, columns), preferred_element_type=jnp.float32
    )
    queries = queries.astype(projected.dtype).reshape(tok_dev, heads_here, HD)
    keys = keyval[:, 0, :].reshape(tokens, heads_here, HD)
    values = keyval[:, 1, :].reshape(tokens, heads_here, HD)
    scores = (
        jnp.einsum("qhd,khd->hqk", queries, keys, preferred_element_type=jnp.float32)
        * score_scale
    )
    bounds = jnp.cumsum(doc_lengths)
    key_block = arrival_dest // BLK
    key_doc = segment_of(arrival_dest, bounds)
    query_block = my_pos // BLK
    query_doc = segment_of(my_pos, bounds)
    same_doc = query_doc[:, None] == key_doc[None, :]
    window = jnp.zeros((tok_dev, tokens), jnp.int32)
    for step in (-1, 0, 1):
        near = (query_block + step) % blocks_all
        window = window + (key_block[None, :] == near[:, None]).astype(jnp.int32)
    window = jnp.where(same_doc, window, 0)
    chosen = random_blocks[query_block]
    drawn = jnp.zeros((tok_dev, tokens), jnp.int32)
    for r in range(chosen.shape[1]):
        drawn = drawn + (key_block[None, :] == chosen[:, r][:, None]).astype(jnp.int32)
    glob_start = global_owner[0] * tok_dev
    in_glob = (arrival_dest >= glob_start) & (arrival_dest < glob_start + tok_dev)
    holds_glob = own_index == global_owner[0]
    count = window + drawn + in_glob[None, :].astype(jnp.int32)
    count = jnp.where(holds_glob, 1, count)
    live = count > 0
    near_scores = jnp.where(live[None], scores, big_negative)
    row_peak = jnp.max(near_scores, axis=2)
    near_exp = jnp.exp(near_scores - row_peak[..., None])
    count_f = count.astype(jnp.float32)[None]
    denominator = jnp.sum(near_exp * count_f, axis=2)
    rounded = jnp.where(holds_glob, near_exp, near_exp.astype(jnp.bfloat16).astype(jnp.float32))
    weighted = rounded * count_f
    weight_hi = weighted.astype(jnp.bfloat16)
    weight_lo = (weighted - weight_hi.astype(jnp.float32)).astype(jnp.bfloat16)
    mixed_sum = jnp.einsum("hqk,khd->qhd", weight_hi, values, preferred_element_type=jnp.float32)
    mixed_sum = mixed_sum + jnp.einsum(
        "hqk,khd->qhd", weight_lo, values, preferred_element_type=jnp.float32
    )
    attn_rows = (mixed_sum / jnp.transpose(denominator)[..., None]).reshape(tok_dev, columns)
    attn_rows = attn_rows.astype(jnp.bfloat16)
    projected_rows = jnp.dot(attn_rows, out_weight, preferred_element_type=jnp.float32)
    return head_sum(lax.optimization_barrier(projected_rows))


def head_sum(partial):
    members = lax.axis_size("head")
    if members & (members - 1):
        return lax.psum_scatter(
            partial.astype(jnp.bfloat16), "head", scatter_dimension=0, tiled=True
        )
    me = lax.axis_index("head")
    rows = partial.shape[0] // members
    partial = partial.reshape(members, rows, partial.shape[1])
    bit = 1
    while bit < members:
        pairs = partial.reshape(partial.shape[0] // 2, 2, rows, partial.shape[2])
        upper = (me & bit) != 0
        keep = jnp.where(upper, pairs[:, 1], pairs[:, 0])
        send = jnp.where(upper, pairs[:, 0], pairs[:, 1]).astype(jnp.bfloat16)
        got = lax.ppermute(send, "head", [(i, i ^ bit) for i in range(members)])
        partial = keep + got.astype(jnp.float32)
        bit *= 2
    partial = partial.reshape(rows, partial.shape[2])
    return partial.astype(jnp.bfloat16)


GATHER_LIMIT = 16 * 2**20


def shards(projected, destination, doc_lengths, random_blocks, global_owner, out_weight):
    gathered_bytes = lax.axis_size("seq") * projected.size * projected.dtype.itemsize
    if gathered_bytes <= GATHER_LIMIT:
        return gathered_plan(
            projected, destination, doc_lengths, random_blocks, global_owner, out_weight
        )
    return shards_ring(projected, destination, doc_lengths, random_blocks, global_owner, out_weight)


def solution(mesh):
    in_specs = (P("seq", None, "head"), P("seq"), P(), P(), P(), P("head", None))
    out_specs = P(("seq", "head"), None)
    return jax.shard_map(shards, mesh=mesh, in_specs=in_specs, out_specs=out_specs, check_vma=False)
```

```python
import math

import jax
import jax.numpy as jnp
from jax import lax
from jax.experimental import pallas as pl
from jax.experimental.pallas import tpu as pltpu
from jax.sharding import PartitionSpec as P

HD = 128
BLK = 128
R = 3
RDEV = 2


big_negative = -1e30


def from_behind(block, axis, distance):
    devices = range(lax.axis_size(axis))
    route = [((i - distance) % len(devices), i) for i in devices]
    return lax.ppermute(block, axis, route)


def from_root(x, axis, root):
    mine = lax.axis_index(axis) == root
    return lax.psum(jnp.where(mine, x, jnp.zeros_like(x)), axis)


def combined_all(x, axis, combine):
    everything = jax.tree.map(lambda part: lax.all_gather(part, axis), x)
    first = jax.tree.map(lambda part: part[0], everything)

    def step(k, so_far):
        return combine(so_far, jax.tree.map(lambda part: part[k], everything))

    return lax.fori_loop(1, lax.axis_size(axis), step, first)


def segment_of(positions, bounds):
    return jnp.sum((bounds[None, :] <= positions[:, None]).astype(jnp.int32), axis=1)


def combine_parts(left_part, right_part):
    top_left, total_left, accum_left = left_part
    top_right, total_right, accum_right = right_part
    row_peak = jnp.maximum(top_left, top_right)
    factor_left = jnp.exp(top_left - row_peak)
    factor_right = jnp.exp(top_right - row_peak)
    return (
        row_peak,
        total_left * factor_left + total_right * factor_right,
        accum_left * factor_left[:, :, None] + accum_right * factor_right[:, :, None],
    )


def shards_ring(projected, destination, doc_lengths, random_blocks, global_owner, out_weight):
    owners = lax.axis_size("seq")
    own_index = lax.axis_index("seq")
    tok_dev = projected.shape[0]
    columns = projected.shape[2]
    heads_here = columns // HD
    per_dev = tok_dev // BLK
    blocks_all = owners * per_dev
    capacity = 2 * (tok_dev // owners)
    score_scale = 1.0 / math.sqrt(HD)
    target_owner = destination // tok_dev
    onehot = (target_owner[:, None] == jnp.arange(owners, dtype=jnp.int32)[None, :]).astype(
        jnp.int32
    )
    before = jnp.cumsum(onehot, axis=0) - onehot
    slot_rank = jnp.sum(before * onehot, axis=1)
    outgoing = (
        jnp.zeros((owners, capacity, 3, columns), projected.dtype)
        .at[target_owner, slot_rank]
        .set(projected)
    )
    slots = (
        jnp.full((owners, capacity), -1, jnp.int32)
        .at[target_owner, slot_rank]
        .set(destination % tok_dev)
    )
    incoming, landing = (
        lax.all_to_all(outgoing, "seq", split_axis=0, concat_axis=0, tiled=True),
        lax.all_to_all(slots, "seq", split_axis=0, concat_axis=0, tiled=True),
    )
    landing = landing.reshape(-1)
    landing = jnp.where(landing >= 0, landing, tok_dev)
    routed = (
        jnp.zeros((tok_dev, 3, columns), projected.dtype)
        .at[landing]
        .set(incoming.reshape(owners * capacity, 3, columns), mode="drop")
    )
    keyval = routed[:, 1:, :]
    fetched = {0: keyval}
    offsets = list(range(-RDEV, 0)) + list(range(1, RDEV + 1))
    for offset in offsets:
        fetched[offset] = from_behind(keyval, "seq", -offset)
    band_blocks = jnp.stack([fetched[offset] for offset in range(-RDEV, RDEV + 1)])
    block_ids = own_index * per_dev + jnp.arange(per_dev, dtype=jnp.int32)
    local_pick = jnp.arange(per_dev, dtype=jnp.int32) + RDEV * per_dev
    window_pick = local_pick[:, None] + jnp.arange(-1, 2, dtype=jnp.int32)[None, :]
    chosen_rand = lax.dynamic_slice_in_dim(random_blocks, own_index * per_dev, per_dev, 0)
    away_dev = (chosen_rand // per_dev - own_index) % owners
    away_dev = jnp.where(away_dev > owners // 2, away_dev - owners, away_dev)
    rand_pick = (away_dev + RDEV) * per_dev + chosen_rand % per_dev
    block_picks = jnp.concatenate([window_pick, rand_pick], axis=1)
    gathered = jnp.take(band_blocks, block_picks, axis=0)
    near_keys = gathered[:, :, :, 0, :].reshape(per_dev, (3 + R) * BLK, heads_here, HD)
    near_values = gathered[:, :, :, 1, :].reshape(per_dev, (3 + R) * BLK, heads_here, HD)
    owner_dev = global_owner[0]
    global_rows = from_root(routed, "seq", owner_dev)
    glob_keys = global_rows[:, 1, :].reshape(tok_dev, heads_here, HD)
    glob_values = global_rows[:, 2, :].reshape(tok_dev, heads_here, HD)
    queries = routed[:, 0, :].reshape(per_dev, BLK, heads_here, HD)
    near_scores = (
        jnp.einsum("bqhd,bkhd->bhqk", queries, near_keys, preferred_element_type=jnp.float32)
        * score_scale
    )
    far_scores = (
        jnp.einsum("bqhd,khd->bhqk", queries, glob_keys, preferred_element_type=jnp.float32)
        * score_scale
    )
    bounds = jnp.cumsum(doc_lengths)
    query_pos = own_index * tok_dev + jnp.arange(tok_dev, dtype=jnp.int32)
    query_doc = segment_of(query_pos, bounds).reshape(per_dev, BLK)
    window_blocks = (block_ids[:, None] + jnp.arange(-1, 2, dtype=jnp.int32)[None, :]) % blocks_all
    key_pos = (
        window_blocks[:, :, None] * BLK + jnp.arange(BLK, dtype=jnp.int32)[None, None, :]
    ).reshape(-1)
    key_doc = segment_of(key_pos, bounds).reshape(per_dev, 3 * BLK)
    same_doc = query_doc[:, :, None] == key_doc[:, None, :]
    allowed = jnp.concatenate(
        [same_doc, jnp.ones((per_dev, BLK, R * BLK), dtype=jnp.bool_)], axis=2
    )
    near_scores = jnp.where(allowed[:, None], near_scores, big_negative)
    row_peak = jnp.maximum(jnp.max(near_scores, axis=3), jnp.max(far_scores, axis=3))
    near_exp = jnp.exp(near_scores - row_peak[..., None])
    far_exp = jnp.exp(far_scores - row_peak[..., None])
    denominator = jnp.sum(near_exp, axis=3) + jnp.sum(far_exp, axis=3)
    mixed_sum = jnp.einsum(
        "bhqk,bkhd->bqhd",
        near_exp.astype(jnp.bfloat16),
        near_values,
        preferred_element_type=jnp.float32,
    )
    mixed_sum = mixed_sum + jnp.einsum(
        "bhqk,khd->bqhd",
        far_exp.astype(jnp.bfloat16),
        glob_values,
        preferred_element_type=jnp.float32,
    )
    sparse = (mixed_sum / jnp.transpose(denominator, (0, 2, 1))[..., None]).reshape(
        tok_dev, columns
    )
    sparse = sparse.astype(jnp.bfloat16)
    glob_queries = global_rows[:, 0, :].reshape(tok_dev, heads_here, HD)
    local_keys = routed[:, 1, :].reshape(tok_dev, heads_here, HD)
    local_values = routed[:, 2, :].reshape(tok_dev, heads_here, HD).astype(jnp.float32)
    all_scores = (
        jnp.einsum("qhd,khd->hqk", glob_queries, local_keys, preferred_element_type=jnp.float32)
        * score_scale
    )
    local_peak = jnp.max(all_scores, axis=2)
    weights = jnp.exp(all_scores - local_peak[..., None])
    part_total = jnp.sum(weights, axis=2)
    part_accum = jnp.einsum("hqk,khd->hqd", weights, local_values, precision=lax.Precision.HIGHEST)
    peak_all, total_all, accum_all = combined_all(
        (local_peak, part_total, part_accum), "seq", combine_parts
    )
    glob_out = jnp.transpose(accum_all / total_all[..., None], (1, 0, 2)).reshape(tok_dev, columns)
    glob_out = glob_out.astype(jnp.bfloat16)
    attn_rows = jnp.where(own_index == owner_dev, glob_out, sparse)
    return lax.psum_scatter(
        jnp.dot(attn_rows, out_weight, preferred_element_type=jnp.float32).astype(jnp.bfloat16),
        "head",
        scatter_dimension=0,
        tiled=True,
    )


def attend_body(q_ref, k_ref, v_ref, count_ref, flag_ref, out_ref):
    scores = lax.dot_general(
        q_ref[...], k_ref[...], (((1,), (1,)), ((), ())), preferred_element_type=jnp.float32
    ) * (1.0 / math.sqrt(HD))
    count = count_ref[...]
    near_scores = jnp.where(count > 0, scores, big_negative)
    row_peak = jnp.max(near_scores, axis=1, keepdims=True)
    near_exp = jnp.exp(near_scores - row_peak)
    denominator = jnp.sum(near_exp * count, axis=1, keepdims=True)
    exact = flag_ref[0:1, 0:1] > 0
    rounded = jnp.where(exact, near_exp, near_exp.astype(jnp.bfloat16).astype(jnp.float32))
    weighted = rounded * count
    weight_hi = weighted.astype(jnp.bfloat16)
    weight_lo = (weighted - weight_hi.astype(jnp.float32)).astype(jnp.bfloat16)
    values = v_ref[...]
    mixed_sum = jnp.dot(weight_hi, values, preferred_element_type=jnp.float32)
    mixed_sum = mixed_sum + jnp.dot(weight_lo, values, preferred_element_type=jnp.float32)
    out_ref[...] = (mixed_sum / denominator).astype(out_ref.dtype)


def attend_all(queries, keys, values, count, flag):
    rows, columns = queries.shape
    tokens = keys.shape[0]
    heads = columns // HD
    flops = heads * rows * tokens * HD * 2 * 3
    return pl.pallas_call(
        attend_body,
        grid=(heads,),
        in_specs=[
            pl.BlockSpec((rows, HD), lambda h: (0, h)),
            pl.BlockSpec((tokens, HD), lambda h: (0, h)),
            pl.BlockSpec((tokens, HD), lambda h: (0, h)),
            pl.BlockSpec((rows, tokens), lambda h: (0, 0)),
            pl.BlockSpec((8, 128), lambda h: (0, 0)),
        ],
        out_specs=pl.BlockSpec((rows, HD), lambda h: (0, h)),
        out_shape=jax.ShapeDtypeStruct((rows, columns), jnp.bfloat16),
        cost_estimate=pl.CostEstimate(
            flops=flops,
            transcendentals=heads * rows * tokens,
            bytes_accessed=2 * tokens * columns * 2 + rows * tokens * 4 + 2 * rows * columns * 2,
        ),
    )(queries, keys, values, count, flag)


def gathered_plan(projected, destination, doc_lengths, random_blocks, global_owner, out_weight):
    owners = lax.axis_size("seq")
    own_index = lax.axis_index("seq")
    tok_dev = projected.shape[0]
    columns = projected.shape[2]
    heads_here = columns // HD
    tokens = owners * tok_dev
    blocks_all = tokens // BLK
    score_scale = 1.0 / math.sqrt(HD)
    capacity = 2 * (tok_dev // owners)
    arrival_dest = lax.all_gather(destination, "seq", tiled=True)
    keyval = lax.all_gather(projected[:, 1:, :], "seq", tiled=True)
    target_all = arrival_dest.reshape(owners, tok_dev) // tok_dev
    onehot = (target_all[:, :, None] == jnp.arange(owners, dtype=jnp.int32)).astype(jnp.int32)
    slot_all = jnp.sum((jnp.cumsum(onehot, axis=1) - onehot) * onehot, axis=2)
    target = destination // tok_dev
    mine = (target[:, None] == jnp.arange(owners, dtype=jnp.int32)[None, :]).astype(jnp.int32)
    slot = jnp.sum((jnp.cumsum(mine, axis=0) - mine) * mine, axis=1)
    send_col = target * capacity + slot
    send_pick = (
        jnp.arange(owners * capacity, dtype=jnp.int32)[:, None] == send_col[None, :]
    ).astype(projected.dtype)
    outgoing = jnp.dot(send_pick, projected[:, 0, :], preferred_element_type=jnp.float32)
    outgoing = outgoing.astype(projected.dtype).reshape(owners, capacity, columns)
    incoming = lax.all_to_all(outgoing, "seq", split_axis=0, concat_axis=0, tiled=True)
    my_pos = own_index * tok_dev + jnp.arange(tok_dev, dtype=jnp.int32)
    source = jnp.arange(tokens, dtype=jnp.int32) // tok_dev
    land_col = (source * capacity + slot_all.reshape(-1))[None, :]
    hit = arrival_dest[None, :] == my_pos[:, None]
    col_of_pos = jnp.sum(jnp.where(hit, land_col, 0), axis=1)
    land_pick = (
        col_of_pos[:, None] == jnp.arange(owners * capacity, dtype=jnp.int32)[None, :]
    ).astype(projected.dtype)
    queries = jnp.dot(
        land_pick, incoming.reshape(owners * capacity, columns), preferred_element_type=jnp.float32
    )
    queries = queries.astype(projected.dtype).reshape(tok_dev, heads_here, HD)
    keys = keyval[:, 0, :].reshape(tokens, heads_here, HD)
    values = keyval[:, 1, :].reshape(tokens, heads_here, HD)
    bounds = jnp.cumsum(doc_lengths)
    key_block = arrival_dest // BLK
    key_doc = segment_of(arrival_dest, bounds)
    query_block = my_pos // BLK
    query_doc = segment_of(my_pos, bounds)
    same_doc = query_doc[:, None] == key_doc[None, :]
    window = jnp.zeros((tok_dev, tokens), jnp.int32)
    for step in (-1, 0, 1):
        near = (query_block + step) % blocks_all
        window = window + (key_block[None, :] == near[:, None]).astype(jnp.int32)
    window = jnp.where(same_doc, window, 0)
    chosen = random_blocks[query_block]
    drawn = jnp.zeros((tok_dev, tokens), jnp.int32)
    for r in range(chosen.shape[1]):
        drawn = drawn + (key_block[None, :] == chosen[:, r][:, None]).astype(jnp.int32)
    glob_start = global_owner[0] * tok_dev
    in_glob = (arrival_dest >= glob_start) & (arrival_dest < glob_start + tok_dev)
    holds_glob = own_index == global_owner[0]
    count = window + drawn + in_glob[None, :].astype(jnp.int32)
    count = jnp.where(holds_glob, 1, count)
    attn_rows = attend_all(
        queries.reshape(tok_dev, columns),
        keyval[:, 0, :],
        keyval[:, 1, :],
        count.astype(jnp.float32),
        jnp.full((8, 128), holds_glob.astype(jnp.float32)),
    )
    projected_rows = jnp.dot(attn_rows, out_weight, preferred_element_type=jnp.float32)
    return head_sum(lax.optimization_barrier(projected_rows))


def head_sum(partial):
    members = lax.axis_size("head")
    if members & (members - 1):
        return lax.psum_scatter(
            partial.astype(jnp.bfloat16), "head", scatter_dimension=0, tiled=True
        )
    me = lax.axis_index("head")
    rows = partial.shape[0] // members
    partial = partial.reshape(members, rows, partial.shape[1])
    bit = 1
    while bit < members:
        pairs = partial.reshape(partial.shape[0] // 2, 2, rows, partial.shape[2])
        upper = (me & bit) != 0
        keep = jnp.where(upper, pairs[:, 1], pairs[:, 0])
        send = jnp.where(upper, pairs[:, 0], pairs[:, 1]).astype(jnp.bfloat16)
        got = lax.ppermute(send, "head", [(i, i ^ bit) for i in range(members)])
        partial = keep + got.astype(jnp.float32)
        bit *= 2
    partial = partial.reshape(rows, partial.shape[2])
    return partial.astype(jnp.bfloat16)


GATHER_LIMIT = 16 * 2**20


def shards(projected, destination, doc_lengths, random_blocks, global_owner, out_weight):
    gathered_bytes = lax.axis_size("seq") * projected.size * projected.dtype.itemsize
    if gathered_bytes <= GATHER_LIMIT:
        return gathered_plan(
            projected, destination, doc_lengths, random_blocks, global_owner, out_weight
        )
    return shards_ring(projected, destination, doc_lengths, random_blocks, global_owner, out_weight)


def solution(mesh):
    in_specs = (P("seq", None, "head"), P("seq"), P(), P(), P(), P("head", None))
    out_specs = P(("seq", "head"), None)
    return jax.shard_map(shards, mesh=mesh, in_specs=in_specs, out_specs=out_specs, check_vma=False)
```

```python
import math

import jax
import jax.numpy as jnp
from jax import lax
from jax.sharding import PartitionSpec as P

HD = 128
BLK = 128
R = 3
RDEV = 2


big_negative = -1e30


def from_behind(block, axis, distance):
    devices = range(lax.axis_size(axis))
    route = [((i - distance) % len(devices), i) for i in devices]
    return lax.ppermute(block, axis, route)


def from_root(x, axis, root):
    mine = lax.axis_index(axis) == root
    return lax.psum(jnp.where(mine, x, jnp.zeros_like(x)), axis)


def combined_all(x, axis, combine):
    everything = jax.tree.map(lambda part: lax.all_gather(part, axis), x)
    first = jax.tree.map(lambda part: part[0], everything)

    def step(k, so_far):
        return combine(so_far, jax.tree.map(lambda part: part[k], everything))

    return lax.fori_loop(1, lax.axis_size(axis), step, first)


def segment_of(positions, bounds):
    return jnp.sum((bounds[None, :] <= positions[:, None]).astype(jnp.int32), axis=1)


def combine_parts(left_part, right_part):
    top_left, total_left, accum_left = left_part
    top_right, total_right, accum_right = right_part
    row_peak = jnp.maximum(top_left, top_right)
    factor_left = jnp.exp(top_left - row_peak)
    factor_right = jnp.exp(top_right - row_peak)
    return (
        row_peak,
        total_left * factor_left + total_right * factor_right,
        accum_left * factor_left[:, :, None] + accum_right * factor_right[:, :, None],
    )


def shards_ring(projected, destination, doc_lengths, random_blocks, global_owner, out_weight):
    owners = lax.axis_size("seq")
    own_index = lax.axis_index("seq")
    tok_dev = projected.shape[0]
    columns = projected.shape[2]
    heads_here = columns // HD
    per_dev = tok_dev // BLK
    blocks_all = owners * per_dev
    capacity = 2 * (tok_dev // owners)
    score_scale = 1.0 / math.sqrt(HD)
    target_owner = destination // tok_dev
    onehot = (target_owner[:, None] == jnp.arange(owners, dtype=jnp.int32)[None, :]).astype(
        jnp.int32
    )
    before = jnp.cumsum(onehot, axis=0) - onehot
    slot_rank = jnp.sum(before * onehot, axis=1)
    outgoing = (
        jnp.zeros((owners, capacity, 3, columns), projected.dtype)
        .at[target_owner, slot_rank]
        .set(projected)
    )
    slots = (
        jnp.full((owners, capacity), -1, jnp.int32)
        .at[target_owner, slot_rank]
        .set(destination % tok_dev)
    )
    incoming, landing = (
        lax.all_to_all(outgoing, "seq", split_axis=0, concat_axis=0, tiled=True),
        lax.all_to_all(slots, "seq", split_axis=0, concat_axis=0, tiled=True),
    )
    landing = landing.reshape(-1)
    landing = jnp.where(landing >= 0, landing, tok_dev)
    routed = (
        jnp.zeros((tok_dev, 3, columns), projected.dtype)
        .at[landing]
        .set(incoming.reshape(owners * capacity, 3, columns), mode="drop")
    )
    keyval = routed[:, 1:, :]
    fetched = {0: keyval}
    offsets = list(range(-RDEV, 0)) + list(range(1, RDEV + 1))
    for offset in offsets:
        fetched[offset] = from_behind(keyval, "seq", -offset)
    band_blocks = jnp.stack([fetched[offset] for offset in range(-RDEV, RDEV + 1)])
    block_ids = own_index * per_dev + jnp.arange(per_dev, dtype=jnp.int32)
    local_pick = jnp.arange(per_dev, dtype=jnp.int32) + RDEV * per_dev
    window_pick = local_pick[:, None] + jnp.arange(-1, 2, dtype=jnp.int32)[None, :]
    chosen_rand = lax.dynamic_slice_in_dim(random_blocks, own_index * per_dev, per_dev, 0)
    away_dev = (chosen_rand // per_dev - own_index) % owners
    away_dev = jnp.where(away_dev > owners // 2, away_dev - owners, away_dev)
    rand_pick = (away_dev + RDEV) * per_dev + chosen_rand % per_dev
    block_picks = jnp.concatenate([window_pick, rand_pick], axis=1)
    gathered = jnp.take(band_blocks, block_picks, axis=0)
    near_keys = gathered[:, :, :, 0, :].reshape(per_dev, (3 + R) * BLK, heads_here, HD)
    near_values = gathered[:, :, :, 1, :].reshape(per_dev, (3 + R) * BLK, heads_here, HD)
    owner_dev = global_owner[0]
    global_rows = from_root(routed, "seq", owner_dev)
    glob_keys = global_rows[:, 1, :].reshape(tok_dev, heads_here, HD)
    glob_values = global_rows[:, 2, :].reshape(tok_dev, heads_here, HD)
    queries = routed[:, 0, :].reshape(per_dev, BLK, heads_here, HD)
    near_scores = (
        jnp.einsum("bqhd,bkhd->bhqk", queries, near_keys, preferred_element_type=jnp.float32)
        * score_scale
    )
    far_scores = (
        jnp.einsum("bqhd,khd->bhqk", queries, glob_keys, preferred_element_type=jnp.float32)
        * score_scale
    )
    bounds = jnp.cumsum(doc_lengths)
    query_pos = own_index * tok_dev + jnp.arange(tok_dev, dtype=jnp.int32)
    query_doc = segment_of(query_pos, bounds).reshape(per_dev, BLK)
    window_blocks = (block_ids[:, None] + jnp.arange(-1, 2, dtype=jnp.int32)[None, :]) % blocks_all
    key_pos = (
        window_blocks[:, :, None] * BLK + jnp.arange(BLK, dtype=jnp.int32)[None, None, :]
    ).reshape(-1)
    key_doc = segment_of(key_pos, bounds).reshape(per_dev, 3 * BLK)
    same_doc = query_doc[:, :, None] == key_doc[:, None, :]
    allowed = jnp.concatenate(
        [same_doc, jnp.ones((per_dev, BLK, R * BLK), dtype=jnp.bool_)], axis=2
    )
    near_scores = jnp.where(allowed[:, None], near_scores, big_negative)
    row_peak = jnp.maximum(jnp.max(near_scores, axis=3), jnp.max(far_scores, axis=3))
    near_exp = jnp.exp(near_scores - row_peak[..., None])
    far_exp = jnp.exp(far_scores - row_peak[..., None])
    denominator = jnp.sum(near_exp, axis=3) + jnp.sum(far_exp, axis=3)
    mixed_sum = jnp.einsum(
        "bhqk,bkhd->bqhd",
        near_exp.astype(jnp.bfloat16),
        near_values,
        preferred_element_type=jnp.float32,
    )
    mixed_sum = mixed_sum + jnp.einsum(
        "bhqk,khd->bqhd",
        far_exp.astype(jnp.bfloat16),
        glob_values,
        preferred_element_type=jnp.float32,
    )
    sparse = (mixed_sum / jnp.transpose(denominator, (0, 2, 1))[..., None]).reshape(
        tok_dev, columns
    )
    sparse = sparse.astype(jnp.bfloat16)
    glob_queries = global_rows[:, 0, :].reshape(tok_dev, heads_here, HD)
    local_keys = routed[:, 1, :].reshape(tok_dev, heads_here, HD)
    local_values = routed[:, 2, :].reshape(tok_dev, heads_here, HD).astype(jnp.float32)
    all_scores = (
        jnp.einsum("qhd,khd->hqk", glob_queries, local_keys, preferred_element_type=jnp.float32)
        * score_scale
    )
    local_peak = jnp.max(all_scores, axis=2)
    weights = jnp.exp(all_scores - local_peak[..., None])
    part_total = jnp.sum(weights, axis=2)
    part_accum = jnp.einsum("hqk,khd->hqd", weights, local_values, precision=lax.Precision.HIGHEST)
    peak_all, total_all, accum_all = combined_all(
        (local_peak, part_total, part_accum), "seq", combine_parts
    )
    glob_out = jnp.transpose(accum_all / total_all[..., None], (1, 0, 2)).reshape(tok_dev, columns)
    glob_out = glob_out.astype(jnp.bfloat16)
    attn_rows = jnp.where(own_index == owner_dev, glob_out, sparse)
    return lax.psum_scatter(
        jnp.dot(attn_rows, out_weight, preferred_element_type=jnp.float32).astype(jnp.bfloat16),
        "head",
        scatter_dimension=0,
        tiled=True,
    )


def ring_gather(block, own_index, owners):
    if owners % 2:
        ring = list(range(owners))
    else:
        half = owners // 2
        ring = [2 * i for i in range(half)] + [2 * i + 1 for i in reversed(range(half))]
    place = [0] * owners
    for i, s in enumerate(ring):
        place[s] = i
    right = [(ring[i], ring[(i + 1) % owners]) for i in range(owners)]
    left = [(ring[i], ring[(i - 1) % owners]) for i in range(owners)]
    pieces = {0: block}
    moving_right = block
    moving_left = block
    for step in range(1, owners // 2 + 1):
        moving_right = lax.ppermute(moving_right, "seq", right)
        pieces[-step] = moving_right
        if step <= (owners - 1) // 2:
            moving_left = lax.ppermute(moving_left, "seq", left)
            pieces[step] = moving_left
    offsets = sorted(pieces)
    stacked = jnp.concatenate([pieces[k] for k in offsets], axis=0)
    where = jnp.asarray(place, jnp.int32)[own_index]
    order = jnp.asarray(ring, jnp.int32)[(where + jnp.asarray(offsets, jnp.int32)) % owners]
    return stacked, order


def gathered_plan(projected, destination, doc_lengths, random_blocks, global_owner, out_weight):
    owners = lax.axis_size("seq")
    own_index = lax.axis_index("seq")
    tok_dev = projected.shape[0]
    columns = projected.shape[2]
    heads_here = columns // HD
    tokens = owners * tok_dev
    blocks_all = tokens // BLK
    score_scale = 1.0 / math.sqrt(HD)
    capacity = 2 * (tok_dev // owners)
    arrival_dest = lax.all_gather(destination, "seq", tiled=True)
    keyval, key_order = ring_gather(projected[:, 1:, :], own_index, owners)
    key_dest = arrival_dest.reshape(owners, tok_dev)[key_order].reshape(-1)
    target_all = arrival_dest.reshape(owners, tok_dev) // tok_dev
    onehot = (target_all[:, :, None] == jnp.arange(owners, dtype=jnp.int32)).astype(jnp.int32)
    slot_all = jnp.sum((jnp.cumsum(onehot, axis=1) - onehot) * onehot, axis=2)
    target = destination // tok_dev
    mine = (target[:, None] == jnp.arange(owners, dtype=jnp.int32)[None, :]).astype(jnp.int32)
    slot = jnp.sum((jnp.cumsum(mine, axis=0) - mine) * mine, axis=1)
    send_col = target * capacity + slot
    send_pick = (
        jnp.arange(owners * capacity, dtype=jnp.int32)[:, None] == send_col[None, :]
    ).astype(projected.dtype)
    outgoing = jnp.dot(send_pick, projected[:, 0, :], preferred_element_type=jnp.float32)
    outgoing = outgoing.astype(projected.dtype).reshape(owners, capacity, columns)
    incoming = lax.all_to_all(outgoing, "seq", split_axis=0, concat_axis=0, tiled=True)
    my_pos = own_index * tok_dev + jnp.arange(tok_dev, dtype=jnp.int32)
    source = jnp.arange(tokens, dtype=jnp.int32) // tok_dev
    land_col = (source * capacity + slot_all.reshape(-1))[None, :]
    hit = arrival_dest[None, :] == my_pos[:, None]
    col_of_pos = jnp.sum(jnp.where(hit, land_col, 0), axis=1)
    land_pick = (
        col_of_pos[:, None] == jnp.arange(owners * capacity, dtype=jnp.int32)[None, :]
    ).astype(projected.dtype)
    queries = jnp.dot(
        land_pick, incoming.reshape(owners * capacity, columns), preferred_element_type=jnp.float32
    )
    queries = queries.astype(projected.dtype).reshape(tok_dev, heads_here, HD)
    keys = keyval[:, 0, :].reshape(tokens, heads_here, HD)
    values = keyval[:, 1, :].reshape(tokens, heads_here, HD)
    scores = (
        jnp.einsum("qhd,khd->hqk", queries, keys, preferred_element_type=jnp.float32)
        * score_scale
    )
    bounds = jnp.cumsum(doc_lengths)
    key_block = key_dest // BLK
    key_doc = segment_of(key_dest, bounds)
    query_block = my_pos // BLK
    query_doc = segment_of(my_pos, bounds)
    same_doc = query_doc[:, None] == key_doc[None, :]
    window = jnp.zeros((tok_dev, tokens), jnp.int32)
    for step in (-1, 0, 1):
        near = (query_block + step) % blocks_all
        window = window + (key_block[None, :] == near[:, None]).astype(jnp.int32)
    window = jnp.where(same_doc, window, 0)
    chosen = random_blocks[query_block]
    drawn = jnp.zeros((tok_dev, tokens), jnp.int32)
    for r in range(chosen.shape[1]):
        drawn = drawn + (key_block[None, :] == chosen[:, r][:, None]).astype(jnp.int32)
    glob_start = global_owner[0] * tok_dev
    in_glob = (key_dest >= glob_start) & (key_dest < glob_start + tok_dev)
    holds_glob = own_index == global_owner[0]
    count = window + drawn + in_glob[None, :].astype(jnp.int32)
    count = jnp.where(holds_glob, 1, count)
    live = count > 0
    near_scores = jnp.where(live[None], scores, big_negative)
    row_peak = jnp.max(near_scores, axis=2)
    near_exp = jnp.exp(near_scores - row_peak[..., None])
    count_f = count.astype(jnp.float32)[None]
    denominator = jnp.sum(near_exp * count_f, axis=2)
    rounded = jnp.where(holds_glob, near_exp, near_exp.astype(jnp.bfloat16).astype(jnp.float32))
    weighted = rounded * count_f
    weight_hi = weighted.astype(jnp.bfloat16)
    weight_lo = (weighted - weight_hi.astype(jnp.float32)).astype(jnp.bfloat16)
    mixed_sum = jnp.einsum("hqk,khd->qhd", weight_hi, values, preferred_element_type=jnp.float32)
    mixed_sum = mixed_sum + jnp.einsum(
        "hqk,khd->qhd", weight_lo, values, preferred_element_type=jnp.float32
    )
    attn_rows = (mixed_sum / jnp.transpose(denominator)[..., None]).reshape(tok_dev, columns)
    attn_rows = attn_rows.astype(jnp.bfloat16)
    projected_rows = jnp.dot(attn_rows, out_weight, preferred_element_type=jnp.float32)
    return head_sum(lax.optimization_barrier(projected_rows))


def head_sum(partial):
    members = lax.axis_size("head")
    if members & (members - 1):
        return lax.psum_scatter(
            partial.astype(jnp.bfloat16), "head", scatter_dimension=0, tiled=True
        )
    me = lax.axis_index("head")
    rows = partial.shape[0] // members
    partial = partial.reshape(members, rows, partial.shape[1])
    bit = 1
    while bit < members:
        pairs = partial.reshape(partial.shape[0] // 2, 2, rows, partial.shape[2])
        upper = (me & bit) != 0
        keep = jnp.where(upper, pairs[:, 1], pairs[:, 0])
        send = jnp.where(upper, pairs[:, 0], pairs[:, 1]).astype(jnp.bfloat16)
        got = lax.ppermute(send, "head", [(i, i ^ bit) for i in range(members)])
        partial = keep + got.astype(jnp.float32)
        bit *= 2
    partial = partial.reshape(rows, partial.shape[2])
    return partial.astype(jnp.bfloat16)


GATHER_LIMIT = 16 * 2**20


def shards(projected, destination, doc_lengths, random_blocks, global_owner, out_weight):
    gathered_bytes = lax.axis_size("seq") * projected.size * projected.dtype.itemsize
    if gathered_bytes <= GATHER_LIMIT:
        return gathered_plan(
            projected, destination, doc_lengths, random_blocks, global_owner, out_weight
        )
    return shards_ring(projected, destination, doc_lengths, random_blocks, global_owner, out_weight)


def solution(mesh):
    in_specs = (P("seq", None, "head"), P("seq"), P(), P(), P(), P("head", None))
    out_specs = P(("seq", "head"), None)
    return jax.shard_map(shards, mesh=mesh, in_specs=in_specs, out_specs=out_specs, check_vma=False)
```

```python
import math

import jax
import jax.numpy as jnp
from jax import lax
from jax.sharding import PartitionSpec as P

HD = 128
BLK = 128
R = 3
RDEV = 2


big_negative = -1e30


def from_behind(block, axis, distance):
    devices = range(lax.axis_size(axis))
    route = [((i - distance) % len(devices), i) for i in devices]
    return lax.ppermute(block, axis, route)


def from_root(x, axis, root):
    mine = lax.axis_index(axis) == root
    return lax.psum(jnp.where(mine, x, jnp.zeros_like(x)), axis)


def combined_all(x, axis, combine):
    everything = jax.tree.map(lambda part: lax.all_gather(part, axis), x)
    first = jax.tree.map(lambda part: part[0], everything)

    def step(k, so_far):
        return combine(so_far, jax.tree.map(lambda part: part[k], everything))

    return lax.fori_loop(1, lax.axis_size(axis), step, first)


def segment_of(positions, bounds):
    return jnp.sum((bounds[None, :] <= positions[:, None]).astype(jnp.int32), axis=1)


def combine_parts(left_part, right_part):
    top_left, total_left, accum_left = left_part
    top_right, total_right, accum_right = right_part
    row_peak = jnp.maximum(top_left, top_right)
    factor_left = jnp.exp(top_left - row_peak)
    factor_right = jnp.exp(top_right - row_peak)
    return (
        row_peak,
        total_left * factor_left + total_right * factor_right,
        accum_left * factor_left[:, :, None] + accum_right * factor_right[:, :, None],
    )


def shards_ring(projected, destination, doc_lengths, random_blocks, global_owner, out_weight):
    owners = lax.axis_size("seq")
    own_index = lax.axis_index("seq")
    tok_dev = projected.shape[0]
    columns = projected.shape[2]
    heads_here = columns // HD
    per_dev = tok_dev // BLK
    blocks_all = owners * per_dev
    capacity = 2 * (tok_dev // owners)
    score_scale = 1.0 / math.sqrt(HD)
    target_owner = destination // tok_dev
    onehot = (target_owner[:, None] == jnp.arange(owners, dtype=jnp.int32)[None, :]).astype(
        jnp.int32
    )
    before = jnp.cumsum(onehot, axis=0) - onehot
    slot_rank = jnp.sum(before * onehot, axis=1)
    outgoing = (
        jnp.zeros((owners, capacity, 3, columns), projected.dtype)
        .at[target_owner, slot_rank]
        .set(projected)
    )
    slots = (
        jnp.full((owners, capacity), -1, jnp.int32)
        .at[target_owner, slot_rank]
        .set(destination % tok_dev)
    )
    incoming, landing = (
        lax.all_to_all(outgoing, "seq", split_axis=0, concat_axis=0, tiled=True),
        lax.all_to_all(slots, "seq", split_axis=0, concat_axis=0, tiled=True),
    )
    landing = landing.reshape(-1)
    landing = jnp.where(landing >= 0, landing, tok_dev)
    routed = (
        jnp.zeros((tok_dev, 3, columns), projected.dtype)
        .at[landing]
        .set(incoming.reshape(owners * capacity, 3, columns), mode="drop")
    )
    keyval = routed[:, 1:, :]
    fetched = {0: keyval}
    offsets = list(range(-RDEV, 0)) + list(range(1, RDEV + 1))
    for offset in offsets:
        fetched[offset] = from_behind(keyval, "seq", -offset)
    band_blocks = jnp.stack([fetched[offset] for offset in range(-RDEV, RDEV + 1)])
    block_ids = own_index * per_dev + jnp.arange(per_dev, dtype=jnp.int32)
    local_pick = jnp.arange(per_dev, dtype=jnp.int32) + RDEV * per_dev
    window_pick = local_pick[:, None] + jnp.arange(-1, 2, dtype=jnp.int32)[None, :]
    chosen_rand = lax.dynamic_slice_in_dim(random_blocks, own_index * per_dev, per_dev, 0)
    away_dev = (chosen_rand // per_dev - own_index) % owners
    away_dev = jnp.where(away_dev > owners // 2, away_dev - owners, away_dev)
    rand_pick = (away_dev + RDEV) * per_dev + chosen_rand % per_dev
    block_picks = jnp.concatenate([window_pick, rand_pick], axis=1)
    gathered = jnp.take(band_blocks, block_picks, axis=0)
    near_keys = gathered[:, :, :, 0, :].reshape(per_dev, (3 + R) * BLK, heads_here, HD)
    near_values = gathered[:, :, :, 1, :].reshape(per_dev, (3 + R) * BLK, heads_here, HD)
    owner_dev = global_owner[0]
    global_rows = from_root(routed, "seq", owner_dev)
    glob_keys = global_rows[:, 1, :].reshape(tok_dev, heads_here, HD)
    glob_values = global_rows[:, 2, :].reshape(tok_dev, heads_here, HD)
    queries = routed[:, 0, :].reshape(per_dev, BLK, heads_here, HD)
    near_scores = (
        jnp.einsum("bqhd,bkhd->bhqk", queries, near_keys, preferred_element_type=jnp.float32)
        * score_scale
    )
    far_scores = (
        jnp.einsum("bqhd,khd->bhqk", queries, glob_keys, preferred_element_type=jnp.float32)
        * score_scale
    )
    bounds = jnp.cumsum(doc_lengths)
    query_pos = own_index * tok_dev + jnp.arange(tok_dev, dtype=jnp.int32)
    query_doc = segment_of(query_pos, bounds).reshape(per_dev, BLK)
    window_blocks = (block_ids[:, None] + jnp.arange(-1, 2, dtype=jnp.int32)[None, :]) % blocks_all
    key_pos = (
        window_blocks[:, :, None] * BLK + jnp.arange(BLK, dtype=jnp.int32)[None, None, :]
    ).reshape(-1)
    key_doc = segment_of(key_pos, bounds).reshape(per_dev, 3 * BLK)
    same_doc = query_doc[:, :, None] == key_doc[:, None, :]
    allowed = jnp.concatenate(
        [same_doc, jnp.ones((per_dev, BLK, R * BLK), dtype=jnp.bool_)], axis=2
    )
    near_scores = jnp.where(allowed[:, None], near_scores, big_negative)
    row_peak = jnp.maximum(jnp.max(near_scores, axis=3), jnp.max(far_scores, axis=3))
    near_exp = jnp.exp(near_scores - row_peak[..., None])
    far_exp = jnp.exp(far_scores - row_peak[..., None])
    denominator = jnp.sum(near_exp, axis=3) + jnp.sum(far_exp, axis=3)
    mixed_sum = jnp.einsum(
        "bhqk,bkhd->bqhd",
        near_exp.astype(jnp.bfloat16),
        near_values,
        preferred_element_type=jnp.float32,
    )
    mixed_sum = mixed_sum + jnp.einsum(
        "bhqk,khd->bqhd",
        far_exp.astype(jnp.bfloat16),
        glob_values,
        preferred_element_type=jnp.float32,
    )
    sparse = (mixed_sum / jnp.transpose(denominator, (0, 2, 1))[..., None]).reshape(
        tok_dev, columns
    )
    sparse = sparse.astype(jnp.bfloat16)
    glob_queries = global_rows[:, 0, :].reshape(tok_dev, heads_here, HD)
    local_keys = routed[:, 1, :].reshape(tok_dev, heads_here, HD)
    local_values = routed[:, 2, :].reshape(tok_dev, heads_here, HD).astype(jnp.float32)
    all_scores = (
        jnp.einsum("qhd,khd->hqk", glob_queries, local_keys, preferred_element_type=jnp.float32)
        * score_scale
    )
    local_peak = jnp.max(all_scores, axis=2)
    weights = jnp.exp(all_scores - local_peak[..., None])
    part_total = jnp.sum(weights, axis=2)
    part_accum = jnp.einsum("hqk,khd->hqd", weights, local_values, precision=lax.Precision.HIGHEST)
    peak_all, total_all, accum_all = combined_all(
        (local_peak, part_total, part_accum), "seq", combine_parts
    )
    glob_out = jnp.transpose(accum_all / total_all[..., None], (1, 0, 2)).reshape(tok_dev, columns)
    glob_out = glob_out.astype(jnp.bfloat16)
    attn_rows = jnp.where(own_index == owner_dev, glob_out, sparse)
    return lax.psum_scatter(
        jnp.dot(attn_rows, out_weight, preferred_element_type=jnp.float32).astype(jnp.bfloat16),
        "head",
        scatter_dimension=0,
        tiled=True,
    )


def ring_gather(block, own_index, owners):
    if owners % 2:
        ring = list(range(owners))
    else:
        half = owners // 2
        ring = [2 * i for i in range(half)] + [2 * i + 1 for i in reversed(range(half))]
    place = [0] * owners
    for i, s in enumerate(ring):
        place[s] = i
    right = [(ring[i], ring[(i + 1) % owners]) for i in range(owners)]
    left = [(ring[i], ring[(i - 1) % owners]) for i in range(owners)]
    pieces = {0: block}
    moving_right = block
    moving_left = block
    for step in range(1, owners // 2 + 1):
        moving_right = jax.tree.map(lambda x: lax.ppermute(x, "seq", right), moving_right)
        pieces[-step] = moving_right
        if step <= (owners - 1) // 2:
            moving_left = jax.tree.map(lambda x: lax.ppermute(x, "seq", left), moving_left)
            pieces[step] = moving_left
    offsets = sorted(pieces)
    stacked = jax.tree.map(
        lambda *parts: jnp.concatenate(parts, axis=0), *[pieces[k] for k in offsets]
    )
    where = jnp.asarray(place, jnp.int32)[own_index]
    order = jnp.asarray(ring, jnp.int32)[(where + jnp.asarray(offsets, jnp.int32)) % owners]
    return stacked, order


def gathered_plan(projected, destination, doc_lengths, random_blocks, global_owner, out_weight):
    owners = lax.axis_size("seq")
    own_index = lax.axis_index("seq")
    tok_dev = projected.shape[0]
    columns = projected.shape[2]
    heads_here = columns // HD
    tokens = owners * tok_dev
    blocks_all = tokens // BLK
    score_scale = 1.0 / math.sqrt(HD)
    capacity = 2 * (tok_dev // owners)
    (keyval, key_dest), key_order = ring_gather(
        (projected[:, 1:, :], destination), own_index, owners
    )
    arrival_dest = key_dest
    target_all = arrival_dest.reshape(owners, tok_dev) // tok_dev
    onehot = (target_all[:, :, None] == jnp.arange(owners, dtype=jnp.int32)).astype(jnp.int32)
    slot_all = jnp.sum((jnp.cumsum(onehot, axis=1) - onehot) * onehot, axis=2)
    target = destination // tok_dev
    mine = (target[:, None] == jnp.arange(owners, dtype=jnp.int32)[None, :]).astype(jnp.int32)
    slot = jnp.sum((jnp.cumsum(mine, axis=0) - mine) * mine, axis=1)
    send_col = target * capacity + slot
    send_pick = (
        jnp.arange(owners * capacity, dtype=jnp.int32)[:, None] == send_col[None, :]
    ).astype(projected.dtype)
    outgoing = jnp.dot(send_pick, projected[:, 0, :], preferred_element_type=jnp.float32)
    outgoing = outgoing.astype(projected.dtype).reshape(owners, capacity, columns)
    incoming = lax.all_to_all(outgoing, "seq", split_axis=0, concat_axis=0, tiled=True)
    my_pos = own_index * tok_dev + jnp.arange(tok_dev, dtype=jnp.int32)
    source = jnp.repeat(key_order, tok_dev)
    land_col = (source * capacity + slot_all.reshape(-1))[None, :]
    hit = arrival_dest[None, :] == my_pos[:, None]
    col_of_pos = jnp.sum(jnp.where(hit, land_col, 0), axis=1)
    land_pick = (
        col_of_pos[:, None] == jnp.arange(owners * capacity, dtype=jnp.int32)[None, :]
    ).astype(projected.dtype)
    queries = jnp.dot(
        land_pick, incoming.reshape(owners * capacity, columns), preferred_element_type=jnp.float32
    )
    queries = queries.astype(projected.dtype).reshape(tok_dev, heads_here, HD)
    keys = keyval[:, 0, :].reshape(tokens, heads_here, HD)
    values = keyval[:, 1, :].reshape(tokens, heads_here, HD)
    scores = (
        jnp.einsum("qhd,khd->hqk", queries, keys, preferred_element_type=jnp.float32)
        * score_scale
    )
    bounds = jnp.cumsum(doc_lengths)
    key_block = key_dest // BLK
    key_doc = segment_of(key_dest, bounds)
    query_block = my_pos // BLK
    query_doc = segment_of(my_pos, bounds)
    same_doc = query_doc[:, None] == key_doc[None, :]
    window = jnp.zeros((tok_dev, tokens), jnp.int32)
    for step in (-1, 0, 1):
        near = (query_block + step) % blocks_all
        window = window + (key_block[None, :] == near[:, None]).astype(jnp.int32)
    window = jnp.where(same_doc, window, 0)
    chosen = random_blocks[query_block]
    drawn = jnp.zeros((tok_dev, tokens), jnp.int32)
    for r in range(chosen.shape[1]):
        drawn = drawn + (key_block[None, :] == chosen[:, r][:, None]).astype(jnp.int32)
    glob_start = global_owner[0] * tok_dev
    in_glob = (key_dest >= glob_start) & (key_dest < glob_start + tok_dev)
    holds_glob = own_index == global_owner[0]
    count = window + drawn + in_glob[None, :].astype(jnp.int32)
    count = jnp.where(holds_glob, 1, count)
    live = count > 0
    near_scores = jnp.where(live[None], scores, big_negative)
    row_peak = jnp.max(near_scores, axis=2)
    near_exp = jnp.exp(near_scores - row_peak[..., None])
    count_f = count.astype(jnp.float32)[None]
    denominator = jnp.sum(near_exp * count_f, axis=2)
    rounded = jnp.where(holds_glob, near_exp, near_exp.astype(jnp.bfloat16).astype(jnp.float32))
    weighted = rounded * count_f
    weight_hi = weighted.astype(jnp.bfloat16)
    weight_lo = (weighted - weight_hi.astype(jnp.float32)).astype(jnp.bfloat16)
    mixed_sum = jnp.einsum("hqk,khd->qhd", weight_hi, values, preferred_element_type=jnp.float32)
    mixed_sum = mixed_sum + jnp.einsum(
        "hqk,khd->qhd", weight_lo, values, preferred_element_type=jnp.float32
    )
    attn_rows = (mixed_sum / jnp.transpose(denominator)[..., None]).reshape(tok_dev, columns)
    attn_rows = attn_rows.astype(jnp.bfloat16)
    projected_rows = jnp.dot(attn_rows, out_weight, preferred_element_type=jnp.float32)
    return head_sum(lax.optimization_barrier(projected_rows))


def head_sum(partial):
    members = lax.axis_size("head")
    if members & (members - 1):
        return lax.psum_scatter(
            partial.astype(jnp.bfloat16), "head", scatter_dimension=0, tiled=True
        )
    me = lax.axis_index("head")
    rows = partial.shape[0] // members
    partial = partial.reshape(members, rows, partial.shape[1])
    bit = 1
    while bit < members:
        pairs = partial.reshape(partial.shape[0] // 2, 2, rows, partial.shape[2])
        upper = (me & bit) != 0
        keep = jnp.where(upper, pairs[:, 1], pairs[:, 0])
        send = jnp.where(upper, pairs[:, 0], pairs[:, 1]).astype(jnp.bfloat16)
        got = lax.ppermute(send, "head", [(i, i ^ bit) for i in range(members)])
        partial = keep + got.astype(jnp.float32)
        bit *= 2
    partial = partial.reshape(rows, partial.shape[2])
    return partial.astype(jnp.bfloat16)


GATHER_LIMIT = 16 * 2**20


def shards(projected, destination, doc_lengths, random_blocks, global_owner, out_weight):
    gathered_bytes = lax.axis_size("seq") * projected.size * projected.dtype.itemsize
    if gathered_bytes <= GATHER_LIMIT:
        return gathered_plan(
            projected, destination, doc_lengths, random_blocks, global_owner, out_weight
        )
    return shards_ring(projected, destination, doc_lengths, random_blocks, global_owner, out_weight)


def solution(mesh):
    in_specs = (P("seq", None, "head"), P("seq"), P(), P(), P(), P("head", None))
    out_specs = P(("seq", "head"), None)
    return jax.shard_map(shards, mesh=mesh, in_specs=in_specs, out_specs=out_specs, check_vma=False)
```

```python
import math

import jax
import jax.numpy as jnp
from jax import lax
from jax.sharding import PartitionSpec as P

HD = 128
BLK = 128
R = 3
RDEV = 2


big_negative = -1e30


def from_behind(block, axis, distance):
    devices = range(lax.axis_size(axis))
    route = [((i - distance) % len(devices), i) for i in devices]
    return lax.ppermute(block, axis, route)


def from_root(x, axis, root):
    mine = lax.axis_index(axis) == root
    return lax.psum(jnp.where(mine, x, jnp.zeros_like(x)), axis)


def combined_all(x, axis, combine):
    everything = jax.tree.map(lambda part: lax.all_gather(part, axis), x)
    first = jax.tree.map(lambda part: part[0], everything)

    def step(k, so_far):
        return combine(so_far, jax.tree.map(lambda part: part[k], everything))

    return lax.fori_loop(1, lax.axis_size(axis), step, first)


def segment_of(positions, bounds):
    return jnp.sum((bounds[None, :] <= positions[:, None]).astype(jnp.int32), axis=1)


def combine_parts(left_part, right_part):
    top_left, total_left, accum_left = left_part
    top_right, total_right, accum_right = right_part
    row_peak = jnp.maximum(top_left, top_right)
    factor_left = jnp.exp(top_left - row_peak)
    factor_right = jnp.exp(top_right - row_peak)
    return (
        row_peak,
        total_left * factor_left + total_right * factor_right,
        accum_left * factor_left[:, :, None] + accum_right * factor_right[:, :, None],
    )


def shards_ring(projected, destination, doc_lengths, random_blocks, global_owner, out_weight):
    owners = lax.axis_size("seq")
    own_index = lax.axis_index("seq")
    tok_dev = projected.shape[0]
    columns = projected.shape[2]
    heads_here = columns // HD
    per_dev = tok_dev // BLK
    blocks_all = owners * per_dev
    capacity = 2 * (tok_dev // owners)
    score_scale = 1.0 / math.sqrt(HD)
    target_owner = destination // tok_dev
    onehot = (target_owner[:, None] == jnp.arange(owners, dtype=jnp.int32)[None, :]).astype(
        jnp.int32
    )
    before = jnp.cumsum(onehot, axis=0) - onehot
    slot_rank = jnp.sum(before * onehot, axis=1)
    outgoing = (
        jnp.zeros((owners, capacity, 3, columns), projected.dtype)
        .at[target_owner, slot_rank]
        .set(projected)
    )
    slots = (
        jnp.full((owners, capacity), -1, jnp.int32)
        .at[target_owner, slot_rank]
        .set(destination % tok_dev)
    )
    incoming, landing = (
        lax.all_to_all(outgoing, "seq", split_axis=0, concat_axis=0, tiled=True),
        lax.all_to_all(slots, "seq", split_axis=0, concat_axis=0, tiled=True),
    )
    landing = landing.reshape(-1)
    landing = jnp.where(landing >= 0, landing, tok_dev)
    routed = (
        jnp.zeros((tok_dev, 3, columns), projected.dtype)
        .at[landing]
        .set(incoming.reshape(owners * capacity, 3, columns), mode="drop")
    )
    keyval = routed[:, 1:, :]
    fetched = {0: keyval}
    offsets = list(range(-RDEV, 0)) + list(range(1, RDEV + 1))
    for offset in offsets:
        fetched[offset] = from_behind(keyval, "seq", -offset)
    band_blocks = jnp.stack([fetched[offset] for offset in range(-RDEV, RDEV + 1)])
    block_ids = own_index * per_dev + jnp.arange(per_dev, dtype=jnp.int32)
    local_pick = jnp.arange(per_dev, dtype=jnp.int32) + RDEV * per_dev
    window_pick = local_pick[:, None] + jnp.arange(-1, 2, dtype=jnp.int32)[None, :]
    chosen_rand = lax.dynamic_slice_in_dim(random_blocks, own_index * per_dev, per_dev, 0)
    away_dev = (chosen_rand // per_dev - own_index) % owners
    away_dev = jnp.where(away_dev > owners // 2, away_dev - owners, away_dev)
    rand_pick = (away_dev + RDEV) * per_dev + chosen_rand % per_dev
    block_picks = jnp.concatenate([window_pick, rand_pick], axis=1)
    gathered = jnp.take(band_blocks, block_picks, axis=0)
    near_keys = gathered[:, :, :, 0, :].reshape(per_dev, (3 + R) * BLK, heads_here, HD)
    near_values = gathered[:, :, :, 1, :].reshape(per_dev, (3 + R) * BLK, heads_here, HD)
    owner_dev = global_owner[0]
    global_rows = from_root(routed, "seq", owner_dev)
    glob_keys = global_rows[:, 1, :].reshape(tok_dev, heads_here, HD)
    glob_values = global_rows[:, 2, :].reshape(tok_dev, heads_here, HD)
    queries = routed[:, 0, :].reshape(per_dev, BLK, heads_here, HD)
    near_scores = (
        jnp.einsum("bqhd,bkhd->bhqk", queries, near_keys, preferred_element_type=jnp.float32)
        * score_scale
    )
    far_scores = (
        jnp.einsum("bqhd,khd->bhqk", queries, glob_keys, preferred_element_type=jnp.float32)
        * score_scale
    )
    bounds = jnp.cumsum(doc_lengths)
    query_pos = own_index * tok_dev + jnp.arange(tok_dev, dtype=jnp.int32)
    query_doc = segment_of(query_pos, bounds).reshape(per_dev, BLK)
    window_blocks = (block_ids[:, None] + jnp.arange(-1, 2, dtype=jnp.int32)[None, :]) % blocks_all
    key_pos = (
        window_blocks[:, :, None] * BLK + jnp.arange(BLK, dtype=jnp.int32)[None, None, :]
    ).reshape(-1)
    key_doc = segment_of(key_pos, bounds).reshape(per_dev, 3 * BLK)
    same_doc = query_doc[:, :, None] == key_doc[:, None, :]
    allowed = jnp.concatenate(
        [same_doc, jnp.ones((per_dev, BLK, R * BLK), dtype=jnp.bool_)], axis=2
    )
    near_scores = jnp.where(allowed[:, None], near_scores, big_negative)
    row_peak = jnp.maximum(jnp.max(near_scores, axis=3), jnp.max(far_scores, axis=3))
    near_exp = jnp.exp(near_scores - row_peak[..., None])
    far_exp = jnp.exp(far_scores - row_peak[..., None])
    denominator = jnp.sum(near_exp, axis=3) + jnp.sum(far_exp, axis=3)
    mixed_sum = jnp.einsum(
        "bhqk,bkhd->bqhd",
        near_exp.astype(jnp.bfloat16),
        near_values,
        preferred_element_type=jnp.float32,
    )
    mixed_sum = mixed_sum + jnp.einsum(
        "bhqk,khd->bqhd",
        far_exp.astype(jnp.bfloat16),
        glob_values,
        preferred_element_type=jnp.float32,
    )
    sparse = (mixed_sum / jnp.transpose(denominator, (0, 2, 1))[..., None]).reshape(
        tok_dev, columns
    )
    sparse = sparse.astype(jnp.bfloat16)
    glob_queries = global_rows[:, 0, :].reshape(tok_dev, heads_here, HD)
    local_keys = routed[:, 1, :].reshape(tok_dev, heads_here, HD)
    local_values = routed[:, 2, :].reshape(tok_dev, heads_here, HD).astype(jnp.float32)
    all_scores = (
        jnp.einsum("qhd,khd->hqk", glob_queries, local_keys, preferred_element_type=jnp.float32)
        * score_scale
    )
    local_peak = jnp.max(all_scores, axis=2)
    weights = jnp.exp(all_scores - local_peak[..., None])
    part_total = jnp.sum(weights, axis=2)
    part_accum = jnp.einsum("hqk,khd->hqd", weights, local_values, precision=lax.Precision.HIGHEST)
    peak_all, total_all, accum_all = combined_all(
        (local_peak, part_total, part_accum), "seq", combine_parts
    )
    glob_out = jnp.transpose(accum_all / total_all[..., None], (1, 0, 2)).reshape(tok_dev, columns)
    glob_out = glob_out.astype(jnp.bfloat16)
    attn_rows = jnp.where(own_index == owner_dev, glob_out, sparse)
    return lax.psum_scatter(
        jnp.dot(attn_rows, out_weight, preferred_element_type=jnp.float32).astype(jnp.bfloat16),
        "head",
        scatter_dimension=0,
        tiled=True,
    )


def ring_gather(block, own_index, owners):
    if owners % 2:
        ring = list(range(owners))
    else:
        half = owners // 2
        ring = [2 * i for i in range(half)] + [2 * i + 1 for i in reversed(range(half))]
    place = [0] * owners
    for i, s in enumerate(ring):
        place[s] = i
    right = [(ring[i], ring[(i + 1) % owners]) for i in range(owners)]
    left = [(ring[i], ring[(i - 1) % owners]) for i in range(owners)]
    pieces = {0: block}
    moving_right = block
    moving_left = block
    for step in range(1, owners // 2 + 1):
        moving_right = jax.tree.map(lambda x: lax.ppermute(x, "seq", right), moving_right)
        pieces[-step] = moving_right
        if step <= (owners - 1) // 2:
            moving_left = jax.tree.map(lambda x: lax.ppermute(x, "seq", left), moving_left)
            pieces[step] = moving_left
    offsets = sorted(pieces)
    stacked = jax.tree.map(
        lambda *parts: jnp.concatenate(parts, axis=0), *[pieces[k] for k in offsets]
    )
    where = jnp.asarray(place, jnp.int32)[own_index]
    order = jnp.asarray(ring, jnp.int32)[(where + jnp.asarray(offsets, jnp.int32)) % owners]
    return stacked, order


def gathered_plan(projected, destination, doc_lengths, random_blocks, global_owner, out_weight):
    owners = lax.axis_size("seq")
    own_index = lax.axis_index("seq")
    tok_dev = projected.shape[0]
    columns = projected.shape[2]
    heads_here = columns // HD
    tokens = owners * tok_dev
    blocks_all = tokens // BLK
    score_scale = 1.0 / math.sqrt(HD)
    capacity = 2 * (tok_dev // owners)
    lanes = jnp.arange(128, dtype=jnp.int32)[None, :]
    dest_hi = jnp.where(lanes == 0, (destination // 32)[:, None], 0)
    dest_lo = jnp.where(lanes == 0, (destination % 32)[:, None], 0)
    tag = jnp.stack([dest_hi, dest_lo], axis=1).astype(projected.dtype)
    message = jnp.concatenate([projected[:, 1:, :], tag], axis=2)
    stacked, key_order = ring_gather(message, own_index, owners)
    key_dest = stacked[:, 0, columns].astype(jnp.int32) * 32 + stacked[:, 1, columns].astype(
        jnp.int32
    )
    keyval = stacked[:, :, :columns]
    arrival_dest = key_dest
    target_all = arrival_dest.reshape(owners, tok_dev) // tok_dev
    onehot = (target_all[:, :, None] == jnp.arange(owners, dtype=jnp.int32)).astype(jnp.int32)
    slot_all = jnp.sum((jnp.cumsum(onehot, axis=1) - onehot) * onehot, axis=2)
    target = destination // tok_dev
    mine = (target[:, None] == jnp.arange(owners, dtype=jnp.int32)[None, :]).astype(jnp.int32)
    slot = jnp.sum((jnp.cumsum(mine, axis=0) - mine) * mine, axis=1)
    send_col = target * capacity + slot
    send_pick = (
        jnp.arange(owners * capacity, dtype=jnp.int32)[:, None] == send_col[None, :]
    ).astype(projected.dtype)
    outgoing = jnp.dot(send_pick, projected[:, 0, :], preferred_element_type=jnp.float32)
    outgoing = outgoing.astype(projected.dtype).reshape(owners, capacity, columns)
    incoming = lax.all_to_all(outgoing, "seq", split_axis=0, concat_axis=0, tiled=True)
    my_pos = own_index * tok_dev + jnp.arange(tok_dev, dtype=jnp.int32)
    source = jnp.repeat(key_order, tok_dev)
    land_col = (source * capacity + slot_all.reshape(-1))[None, :]
    hit = arrival_dest[None, :] == my_pos[:, None]
    col_of_pos = jnp.sum(jnp.where(hit, land_col, 0), axis=1)
    land_pick = (
        col_of_pos[:, None] == jnp.arange(owners * capacity, dtype=jnp.int32)[None, :]
    ).astype(projected.dtype)
    queries = jnp.dot(
        land_pick, incoming.reshape(owners * capacity, columns), preferred_element_type=jnp.float32
    )
    queries = queries.astype(projected.dtype).reshape(tok_dev, heads_here, HD)
    keys = keyval[:, 0, :].reshape(tokens, heads_here, HD)
    values = keyval[:, 1, :].reshape(tokens, heads_here, HD)
    scores = (
        jnp.einsum("qhd,khd->hqk", queries, keys, preferred_element_type=jnp.float32)
        * score_scale
    )
    bounds = jnp.cumsum(doc_lengths)
    key_block = key_dest // BLK
    key_doc = segment_of(key_dest, bounds)
    query_block = my_pos // BLK
    query_doc = segment_of(my_pos, bounds)
    same_doc = query_doc[:, None] == key_doc[None, :]
    window = jnp.zeros((tok_dev, tokens), jnp.int32)
    for step in (-1, 0, 1):
        near = (query_block + step) % blocks_all
        window = window + (key_block[None, :] == near[:, None]).astype(jnp.int32)
    window = jnp.where(same_doc, window, 0)
    chosen = random_blocks[query_block]
    drawn = jnp.zeros((tok_dev, tokens), jnp.int32)
    for r in range(chosen.shape[1]):
        drawn = drawn + (key_block[None, :] == chosen[:, r][:, None]).astype(jnp.int32)
    glob_start = global_owner[0] * tok_dev
    in_glob = (key_dest >= glob_start) & (key_dest < glob_start + tok_dev)
    holds_glob = own_index == global_owner[0]
    count = window + drawn + in_glob[None, :].astype(jnp.int32)
    count = jnp.where(holds_glob, 1, count)
    live = count > 0
    near_scores = jnp.where(live[None], scores, big_negative)
    row_peak = jnp.max(near_scores, axis=2)
    near_exp = jnp.exp(near_scores - row_peak[..., None])
    count_f = count.astype(jnp.float32)[None]
    denominator = jnp.sum(near_exp * count_f, axis=2)
    rounded = jnp.where(holds_glob, near_exp, near_exp.astype(jnp.bfloat16).astype(jnp.float32))
    weighted = rounded * count_f
    weight_hi = weighted.astype(jnp.bfloat16)
    weight_lo = (weighted - weight_hi.astype(jnp.float32)).astype(jnp.bfloat16)
    mixed_sum = jnp.einsum("hqk,khd->qhd", weight_hi, values, preferred_element_type=jnp.float32)
    mixed_sum = mixed_sum + jnp.einsum(
        "hqk,khd->qhd", weight_lo, values, preferred_element_type=jnp.float32
    )
    attn_rows = (mixed_sum / jnp.transpose(denominator)[..., None]).reshape(tok_dev, columns)
    attn_rows = attn_rows.astype(jnp.bfloat16)
    projected_rows = jnp.dot(attn_rows, out_weight, preferred_element_type=jnp.float32)
    return head_sum(lax.optimization_barrier(projected_rows))


def head_sum(partial):
    members = lax.axis_size("head")
    if members & (members - 1):
        return lax.psum_scatter(
            partial.astype(jnp.bfloat16), "head", scatter_dimension=0, tiled=True
        )
    me = lax.axis_index("head")
    rows = partial.shape[0] // members
    partial = partial.reshape(members, rows, partial.shape[1])
    bit = 1
    while bit < members:
        pairs = partial.reshape(partial.shape[0] // 2, 2, rows, partial.shape[2])
        upper = (me & bit) != 0
        keep = jnp.where(upper, pairs[:, 1], pairs[:, 0])
        send = jnp.where(upper, pairs[:, 0], pairs[:, 1]).astype(jnp.bfloat16)
        got = lax.ppermute(send, "head", [(i, i ^ bit) for i in range(members)])
        partial = keep + got.astype(jnp.float32)
        bit *= 2
    partial = partial.reshape(rows, partial.shape[2])
    return partial.astype(jnp.bfloat16)


GATHER_LIMIT = 16 * 2**20


def shards(projected, destination, doc_lengths, random_blocks, global_owner, out_weight):
    gathered_bytes = lax.axis_size("seq") * projected.size * projected.dtype.itemsize
    if gathered_bytes <= GATHER_LIMIT:
        return gathered_plan(
            projected, destination, doc_lengths, random_blocks, global_owner, out_weight
        )
    return shards_ring(projected, destination, doc_lengths, random_blocks, global_owner, out_weight)


def solution(mesh):
    in_specs = (P("seq", None, "head"), P("seq"), P(), P(), P(), P("head", None))
    out_specs = P(("seq", "head"), None)
    return jax.shard_map(shards, mesh=mesh, in_specs=in_specs, out_specs=out_specs, check_vma=False)
```

```python
import math

import jax
import jax.numpy as jnp
from jax import lax
from jax.sharding import PartitionSpec as P

HD = 128
BLK = 128
R = 3
RDEV = 2


big_negative = -1e30


def from_behind(block, axis, distance):
    devices = range(lax.axis_size(axis))
    route = [((i - distance) % len(devices), i) for i in devices]
    return lax.ppermute(block, axis, route)


def from_root(x, axis, root):
    mine = lax.axis_index(axis) == root
    return lax.psum(jnp.where(mine, x, jnp.zeros_like(x)), axis)


def combined_all(x, axis, combine):
    everything = jax.tree.map(lambda part: lax.all_gather(part, axis), x)
    first = jax.tree.map(lambda part: part[0], everything)

    def step(k, so_far):
        return combine(so_far, jax.tree.map(lambda part: part[k], everything))

    return lax.fori_loop(1, lax.axis_size(axis), step, first)


def segment_of(positions, bounds):
    return jnp.sum((bounds[None, :] <= positions[:, None]).astype(jnp.int32), axis=1)


def combine_parts(left_part, right_part):
    top_left, total_left, accum_left = left_part
    top_right, total_right, accum_right = right_part
    row_peak = jnp.maximum(top_left, top_right)
    factor_left = jnp.exp(top_left - row_peak)
    factor_right = jnp.exp(top_right - row_peak)
    return (
        row_peak,
        total_left * factor_left + total_right * factor_right,
        accum_left * factor_left[:, :, None] + accum_right * factor_right[:, :, None],
    )


def shards_ring(projected, destination, doc_lengths, random_blocks, global_owner, out_weight):
    owners = lax.axis_size("seq")
    own_index = lax.axis_index("seq")
    tok_dev = projected.shape[0]
    columns = projected.shape[2]
    heads_here = columns // HD
    per_dev = tok_dev // BLK
    blocks_all = owners * per_dev
    capacity = 2 * (tok_dev // owners)
    score_scale = 1.0 / math.sqrt(HD)
    target_owner = destination // tok_dev
    onehot = (target_owner[:, None] == jnp.arange(owners, dtype=jnp.int32)[None, :]).astype(
        jnp.int32
    )
    before = jnp.cumsum(onehot, axis=0) - onehot
    slot_rank = jnp.sum(before * onehot, axis=1)
    outgoing = (
        jnp.zeros((owners, capacity, 3, columns), projected.dtype)
        .at[target_owner, slot_rank]
        .set(projected)
    )
    slots = (
        jnp.full((owners, capacity), -1, jnp.int32)
        .at[target_owner, slot_rank]
        .set(destination % tok_dev)
    )
    incoming, landing = (
        lax.all_to_all(outgoing, "seq", split_axis=0, concat_axis=0, tiled=True),
        lax.all_to_all(slots, "seq", split_axis=0, concat_axis=0, tiled=True),
    )
    landing = landing.reshape(-1)
    landing = jnp.where(landing >= 0, landing, tok_dev)
    routed = (
        jnp.zeros((tok_dev, 3, columns), projected.dtype)
        .at[landing]
        .set(incoming.reshape(owners * capacity, 3, columns), mode="drop")
    )
    keyval = routed[:, 1:, :]
    fetched = {0: keyval}
    offsets = list(range(-RDEV, 0)) + list(range(1, RDEV + 1))
    for offset in offsets:
        fetched[offset] = from_behind(keyval, "seq", -offset)
    band_blocks = jnp.stack([fetched[offset] for offset in range(-RDEV, RDEV + 1)])
    block_ids = own_index * per_dev + jnp.arange(per_dev, dtype=jnp.int32)
    local_pick = jnp.arange(per_dev, dtype=jnp.int32) + RDEV * per_dev
    window_pick = local_pick[:, None] + jnp.arange(-1, 2, dtype=jnp.int32)[None, :]
    chosen_rand = lax.dynamic_slice_in_dim(random_blocks, own_index * per_dev, per_dev, 0)
    away_dev = (chosen_rand // per_dev - own_index) % owners
    away_dev = jnp.where(away_dev > owners // 2, away_dev - owners, away_dev)
    rand_pick = (away_dev + RDEV) * per_dev + chosen_rand % per_dev
    block_picks = jnp.concatenate([window_pick, rand_pick], axis=1)
    gathered = jnp.take(band_blocks, block_picks, axis=0)
    near_keys = gathered[:, :, :, 0, :].reshape(per_dev, (3 + R) * BLK, heads_here, HD)
    near_values = gathered[:, :, :, 1, :].reshape(per_dev, (3 + R) * BLK, heads_here, HD)
    owner_dev = global_owner[0]
    global_rows = from_root(routed, "seq", owner_dev)
    glob_keys = global_rows[:, 1, :].reshape(tok_dev, heads_here, HD)
    glob_values = global_rows[:, 2, :].reshape(tok_dev, heads_here, HD)
    queries = routed[:, 0, :].reshape(per_dev, BLK, heads_here, HD)
    near_scores = (
        jnp.einsum("bqhd,bkhd->bhqk", queries, near_keys, preferred_element_type=jnp.float32)
        * score_scale
    )
    far_scores = (
        jnp.einsum("bqhd,khd->bhqk", queries, glob_keys, preferred_element_type=jnp.float32)
        * score_scale
    )
    bounds = jnp.cumsum(doc_lengths)
    query_pos = own_index * tok_dev + jnp.arange(tok_dev, dtype=jnp.int32)
    query_doc = segment_of(query_pos, bounds).reshape(per_dev, BLK)
    window_blocks = (block_ids[:, None] + jnp.arange(-1, 2, dtype=jnp.int32)[None, :]) % blocks_all
    key_pos = (
        window_blocks[:, :, None] * BLK + jnp.arange(BLK, dtype=jnp.int32)[None, None, :]
    ).reshape(-1)
    key_doc = segment_of(key_pos, bounds).reshape(per_dev, 3 * BLK)
    same_doc = query_doc[:, :, None] == key_doc[:, None, :]
    allowed = jnp.concatenate(
        [same_doc, jnp.ones((per_dev, BLK, R * BLK), dtype=jnp.bool_)], axis=2
    )
    near_scores = jnp.where(allowed[:, None], near_scores, big_negative)
    row_peak = jnp.maximum(jnp.max(near_scores, axis=3), jnp.max(far_scores, axis=3))
    near_exp = jnp.exp(near_scores - row_peak[..., None])
    far_exp = jnp.exp(far_scores - row_peak[..., None])
    denominator = jnp.sum(near_exp, axis=3) + jnp.sum(far_exp, axis=3)
    mixed_sum = jnp.einsum(
        "bhqk,bkhd->bqhd",
        near_exp.astype(jnp.bfloat16),
        near_values,
        preferred_element_type=jnp.float32,
    )
    mixed_sum = mixed_sum + jnp.einsum(
        "bhqk,khd->bqhd",
        far_exp.astype(jnp.bfloat16),
        glob_values,
        preferred_element_type=jnp.float32,
    )
    sparse = (mixed_sum / jnp.transpose(denominator, (0, 2, 1))[..., None]).reshape(
        tok_dev, columns
    )
    sparse = sparse.astype(jnp.bfloat16)
    glob_queries = global_rows[:, 0, :].reshape(tok_dev, heads_here, HD)
    local_keys = routed[:, 1, :].reshape(tok_dev, heads_here, HD)
    local_values = routed[:, 2, :].reshape(tok_dev, heads_here, HD).astype(jnp.float32)
    all_scores = (
        jnp.einsum("qhd,khd->hqk", glob_queries, local_keys, preferred_element_type=jnp.float32)
        * score_scale
    )
    local_peak = jnp.max(all_scores, axis=2)
    weights = jnp.exp(all_scores - local_peak[..., None])
    part_total = jnp.sum(weights, axis=2)
    part_accum = jnp.einsum("hqk,khd->hqd", weights, local_values, precision=lax.Precision.HIGHEST)
    peak_all, total_all, accum_all = combined_all(
        (local_peak, part_total, part_accum), "seq", combine_parts
    )
    glob_out = jnp.transpose(accum_all / total_all[..., None], (1, 0, 2)).reshape(tok_dev, columns)
    glob_out = glob_out.astype(jnp.bfloat16)
    attn_rows = jnp.where(own_index == owner_dev, glob_out, sparse)
    return lax.psum_scatter(
        jnp.dot(attn_rows, out_weight, preferred_element_type=jnp.float32).astype(jnp.bfloat16),
        "head",
        scatter_dimension=0,
        tiled=True,
    )


def ring_gather(block, own_index, owners):
    if owners % 2:
        ring = list(range(owners))
    else:
        half = owners // 2
        ring = [2 * i for i in range(half)] + [2 * i + 1 for i in reversed(range(half))]
    place = [0] * owners
    for i, s in enumerate(ring):
        place[s] = i
    right = [(ring[i], ring[(i + 1) % owners]) for i in range(owners)]
    left = [(ring[i], ring[(i - 1) % owners]) for i in range(owners)]
    pieces = {0: block}
    moving_right = block
    moving_left = block
    for step in range(1, owners // 2 + 1):
        moving_right = jax.tree.map(lambda x: lax.ppermute(x, "seq", right), moving_right)
        pieces[-step] = moving_right
        if step <= (owners - 1) // 2:
            moving_left = jax.tree.map(lambda x: lax.ppermute(x, "seq", left), moving_left)
            moving_right, moving_left = lax.optimization_barrier((moving_right, moving_left))
            pieces[step] = moving_left
        pieces[-step] = moving_right
    offsets = sorted(pieces)
    stacked = jax.tree.map(
        lambda *parts: jnp.concatenate(parts, axis=0), *[pieces[k] for k in offsets]
    )
    where = jnp.asarray(place, jnp.int32)[own_index]
    order = jnp.asarray(ring, jnp.int32)[(where + jnp.asarray(offsets, jnp.int32)) % owners]
    return stacked, order


def gathered_plan(projected, destination, doc_lengths, random_blocks, global_owner, out_weight):
    owners = lax.axis_size("seq")
    own_index = lax.axis_index("seq")
    tok_dev = projected.shape[0]
    columns = projected.shape[2]
    heads_here = columns // HD
    tokens = owners * tok_dev
    blocks_all = tokens // BLK
    score_scale = 1.0 / math.sqrt(HD)
    capacity = 2 * (tok_dev // owners)
    (keyval, key_dest), key_order = ring_gather(
        (projected[:, 1:, :], destination), own_index, owners
    )
    arrival_dest = key_dest
    target_all = arrival_dest.reshape(owners, tok_dev) // tok_dev
    onehot = (target_all[:, :, None] == jnp.arange(owners, dtype=jnp.int32)).astype(jnp.int32)
    slot_all = jnp.sum((jnp.cumsum(onehot, axis=1) - onehot) * onehot, axis=2)
    target = destination // tok_dev
    mine = (target[:, None] == jnp.arange(owners, dtype=jnp.int32)[None, :]).astype(jnp.int32)
    slot = jnp.sum((jnp.cumsum(mine, axis=0) - mine) * mine, axis=1)
    send_col = target * capacity + slot
    send_pick = (
        jnp.arange(owners * capacity, dtype=jnp.int32)[:, None] == send_col[None, :]
    ).astype(projected.dtype)
    outgoing = jnp.dot(send_pick, projected[:, 0, :], preferred_element_type=jnp.float32)
    outgoing = outgoing.astype(projected.dtype).reshape(owners, capacity, columns)
    incoming = lax.all_to_all(outgoing, "seq", split_axis=0, concat_axis=0, tiled=True)
    my_pos = own_index * tok_dev + jnp.arange(tok_dev, dtype=jnp.int32)
    source = jnp.repeat(key_order, tok_dev)
    land_col = (source * capacity + slot_all.reshape(-1))[None, :]
    hit = arrival_dest[None, :] == my_pos[:, None]
    col_of_pos = jnp.sum(jnp.where(hit, land_col, 0), axis=1)
    land_pick = (
        col_of_pos[:, None] == jnp.arange(owners * capacity, dtype=jnp.int32)[None, :]
    ).astype(projected.dtype)
    queries = jnp.dot(
        land_pick, incoming.reshape(owners * capacity, columns), preferred_element_type=jnp.float32
    )
    queries = queries.astype(projected.dtype).reshape(tok_dev, heads_here, HD)
    keys = keyval[:, 0, :].reshape(tokens, heads_here, HD)
    values = keyval[:, 1, :].reshape(tokens, heads_here, HD)
    scores = (
        jnp.einsum("qhd,khd->hqk", queries, keys, preferred_element_type=jnp.float32)
        * score_scale
    )
    bounds = jnp.cumsum(doc_lengths)
    key_block = key_dest // BLK
    key_doc = segment_of(key_dest, bounds)
    query_block = my_pos // BLK
    query_doc = segment_of(my_pos, bounds)
    same_doc = query_doc[:, None] == key_doc[None, :]
    window = jnp.zeros((tok_dev, tokens), jnp.int32)
    for step in (-1, 0, 1):
        near = (query_block + step) % blocks_all
        window = window + (key_block[None, :] == near[:, None]).astype(jnp.int32)
    window = jnp.where(same_doc, window, 0)
    chosen = random_blocks[query_block]
    drawn = jnp.zeros((tok_dev, tokens), jnp.int32)
    for r in range(chosen.shape[1]):
        drawn = drawn + (key_block[None, :] == chosen[:, r][:, None]).astype(jnp.int32)
    glob_start = global_owner[0] * tok_dev
    in_glob = (key_dest >= glob_start) & (key_dest < glob_start + tok_dev)
    holds_glob = own_index == global_owner[0]
    count = window + drawn + in_glob[None, :].astype(jnp.int32)
    count = jnp.where(holds_glob, 1, count)
    live = count > 0
    near_scores = jnp.where(live[None], scores, big_negative)
    row_peak = jnp.max(near_scores, axis=2)
    near_exp = jnp.exp(near_scores - row_peak[..., None])
    count_f = count.astype(jnp.float32)[None]
    denominator = jnp.sum(near_exp * count_f, axis=2)
    rounded = jnp.where(holds_glob, near_exp, near_exp.astype(jnp.bfloat16).astype(jnp.float32))
    weighted = rounded * count_f
    weight_hi = weighted.astype(jnp.bfloat16)
    weight_lo = (weighted - weight_hi.astype(jnp.float32)).astype(jnp.bfloat16)
    mixed_sum = jnp.einsum("hqk,khd->qhd", weight_hi, values, preferred_element_type=jnp.float32)
    mixed_sum = mixed_sum + jnp.einsum(
        "hqk,khd->qhd", weight_lo, values, preferred_element_type=jnp.float32
    )
    attn_rows = (mixed_sum / jnp.transpose(denominator)[..., None]).reshape(tok_dev, columns)
    attn_rows = attn_rows.astype(jnp.bfloat16)
    projected_rows = jnp.dot(attn_rows, out_weight, preferred_element_type=jnp.float32)
    return head_sum(lax.optimization_barrier(projected_rows))


def head_sum(partial):
    members = lax.axis_size("head")
    if members & (members - 1):
        return lax.psum_scatter(
            partial.astype(jnp.bfloat16), "head", scatter_dimension=0, tiled=True
        )
    me = lax.axis_index("head")
    rows = partial.shape[0] // members
    partial = partial.reshape(members, rows, partial.shape[1])
    bit = 1
    while bit < members:
        pairs = partial.reshape(partial.shape[0] // 2, 2, rows, partial.shape[2])
        upper = (me & bit) != 0
        keep = jnp.where(upper, pairs[:, 1], pairs[:, 0])
        send = jnp.where(upper, pairs[:, 0], pairs[:, 1]).astype(jnp.bfloat16)
        got = lax.ppermute(send, "head", [(i, i ^ bit) for i in range(members)])
        partial = keep + got.astype(jnp.float32)
        bit *= 2
    partial = partial.reshape(rows, partial.shape[2])
    return partial.astype(jnp.bfloat16)


GATHER_LIMIT = 16 * 2**20


def shards(projected, destination, doc_lengths, random_blocks, global_owner, out_weight):
    gathered_bytes = lax.axis_size("seq") * projected.size * projected.dtype.itemsize
    if gathered_bytes <= GATHER_LIMIT:
        return gathered_plan(
            projected, destination, doc_lengths, random_blocks, global_owner, out_weight
        )
    return shards_ring(projected, destination, doc_lengths, random_blocks, global_owner, out_weight)


def solution(mesh):
    in_specs = (P("seq", None, "head"), P("seq"), P(), P(), P(), P("head", None))
    out_specs = P(("seq", "head"), None)
    return jax.shard_map(shards, mesh=mesh, in_specs=in_specs, out_specs=out_specs, check_vma=False)
```

```python
import math

import jax
import jax.numpy as jnp
from jax import lax
from jax.sharding import PartitionSpec as P

HD = 128
BLK = 128
R = 3
RDEV = 2


big_negative = -1e30


def from_behind(block, axis, distance):
    devices = range(lax.axis_size(axis))
    route = [((i - distance) % len(devices), i) for i in devices]
    return lax.ppermute(block, axis, route)


def from_root(x, axis, root):
    mine = lax.axis_index(axis) == root
    return lax.psum(jnp.where(mine, x, jnp.zeros_like(x)), axis)


def combined_all(x, axis, combine):
    everything = jax.tree.map(lambda part: lax.all_gather(part, axis), x)
    first = jax.tree.map(lambda part: part[0], everything)

    def step(k, so_far):
        return combine(so_far, jax.tree.map(lambda part: part[k], everything))

    return lax.fori_loop(1, lax.axis_size(axis), step, first)


def segment_of(positions, bounds):
    return jnp.sum((bounds[None, :] <= positions[:, None]).astype(jnp.int32), axis=1)


def combine_parts(left_part, right_part):
    top_left, total_left, accum_left = left_part
    top_right, total_right, accum_right = right_part
    row_peak = jnp.maximum(top_left, top_right)
    factor_left = jnp.exp(top_left - row_peak)
    factor_right = jnp.exp(top_right - row_peak)
    return (
        row_peak,
        total_left * factor_left + total_right * factor_right,
        accum_left * factor_left[:, :, None] + accum_right * factor_right[:, :, None],
    )


def shards_ring(projected, destination, doc_lengths, random_blocks, global_owner, out_weight):
    owners = lax.axis_size("seq")
    own_index = lax.axis_index("seq")
    tok_dev = projected.shape[0]
    columns = projected.shape[2]
    heads_here = columns // HD
    per_dev = tok_dev // BLK
    blocks_all = owners * per_dev
    capacity = 2 * (tok_dev // owners)
    score_scale = 1.0 / math.sqrt(HD)
    target_owner = destination // tok_dev
    onehot = (target_owner[:, None] == jnp.arange(owners, dtype=jnp.int32)[None, :]).astype(
        jnp.int32
    )
    before = jnp.cumsum(onehot, axis=0) - onehot
    slot_rank = jnp.sum(before * onehot, axis=1)
    outgoing = (
        jnp.zeros((owners, capacity, 3, columns), projected.dtype)
        .at[target_owner, slot_rank]
        .set(projected)
    )
    slots = (
        jnp.full((owners, capacity), -1, jnp.int32)
        .at[target_owner, slot_rank]
        .set(destination % tok_dev)
    )
    incoming, landing = (
        lax.all_to_all(outgoing, "seq", split_axis=0, concat_axis=0, tiled=True),
        lax.all_to_all(slots, "seq", split_axis=0, concat_axis=0, tiled=True),
    )
    landing = landing.reshape(-1)
    landing = jnp.where(landing >= 0, landing, tok_dev)
    routed = (
        jnp.zeros((tok_dev, 3, columns), projected.dtype)
        .at[landing]
        .set(incoming.reshape(owners * capacity, 3, columns), mode="drop")
    )
    keyval = routed[:, 1:, :]
    fetched = {0: keyval}
    offsets = list(range(-RDEV, 0)) + list(range(1, RDEV + 1))
    for offset in offsets:
        fetched[offset] = from_behind(keyval, "seq", -offset)
    band_blocks = jnp.stack([fetched[offset] for offset in range(-RDEV, RDEV + 1)])
    block_ids = own_index * per_dev + jnp.arange(per_dev, dtype=jnp.int32)
    local_pick = jnp.arange(per_dev, dtype=jnp.int32) + RDEV * per_dev
    window_pick = local_pick[:, None] + jnp.arange(-1, 2, dtype=jnp.int32)[None, :]
    chosen_rand = lax.dynamic_slice_in_dim(random_blocks, own_index * per_dev, per_dev, 0)
    away_dev = (chosen_rand // per_dev - own_index) % owners
    away_dev = jnp.where(away_dev > owners // 2, away_dev - owners, away_dev)
    rand_pick = (away_dev + RDEV) * per_dev + chosen_rand % per_dev
    block_picks = jnp.concatenate([window_pick, rand_pick], axis=1)
    gathered = jnp.take(band_blocks, block_picks, axis=0)
    near_keys = gathered[:, :, :, 0, :].reshape(per_dev, (3 + R) * BLK, heads_here, HD)
    near_values = gathered[:, :, :, 1, :].reshape(per_dev, (3 + R) * BLK, heads_here, HD)
    owner_dev = global_owner[0]
    global_rows = from_root(routed, "seq", owner_dev)
    glob_keys = global_rows[:, 1, :].reshape(tok_dev, heads_here, HD)
    glob_values = global_rows[:, 2, :].reshape(tok_dev, heads_here, HD)
    queries = routed[:, 0, :].reshape(per_dev, BLK, heads_here, HD)
    near_scores = (
        jnp.einsum("bqhd,bkhd->bhqk", queries, near_keys, preferred_element_type=jnp.float32)
        * score_scale
    )
    far_scores = (
        jnp.einsum("bqhd,khd->bhqk", queries, glob_keys, preferred_element_type=jnp.float32)
        * score_scale
    )
    bounds = jnp.cumsum(doc_lengths)
    query_pos = own_index * tok_dev + jnp.arange(tok_dev, dtype=jnp.int32)
    query_doc = segment_of(query_pos, bounds).reshape(per_dev, BLK)
    window_blocks = (block_ids[:, None] + jnp.arange(-1, 2, dtype=jnp.int32)[None, :]) % blocks_all
    key_pos = (
        window_blocks[:, :, None] * BLK + jnp.arange(BLK, dtype=jnp.int32)[None, None, :]
    ).reshape(-1)
    key_doc = segment_of(key_pos, bounds).reshape(per_dev, 3 * BLK)
    same_doc = query_doc[:, :, None] == key_doc[:, None, :]
    allowed = jnp.concatenate(
        [same_doc, jnp.ones((per_dev, BLK, R * BLK), dtype=jnp.bool_)], axis=2
    )
    near_scores = jnp.where(allowed[:, None], near_scores, big_negative)
    row_peak = jnp.maximum(jnp.max(near_scores, axis=3), jnp.max(far_scores, axis=3))
    near_exp = jnp.exp(near_scores - row_peak[..., None])
    far_exp = jnp.exp(far_scores - row_peak[..., None])
    denominator = jnp.sum(near_exp, axis=3) + jnp.sum(far_exp, axis=3)
    mixed_sum = jnp.einsum(
        "bhqk,bkhd->bqhd",
        near_exp.astype(jnp.bfloat16),
        near_values,
        preferred_element_type=jnp.float32,
    )
    mixed_sum = mixed_sum + jnp.einsum(
        "bhqk,khd->bqhd",
        far_exp.astype(jnp.bfloat16),
        glob_values,
        preferred_element_type=jnp.float32,
    )
    sparse = (mixed_sum / jnp.transpose(denominator, (0, 2, 1))[..., None]).reshape(
        tok_dev, columns
    )
    sparse = sparse.astype(jnp.bfloat16)
    glob_queries = global_rows[:, 0, :].reshape(tok_dev, heads_here, HD)
    local_keys = routed[:, 1, :].reshape(tok_dev, heads_here, HD)
    local_values = routed[:, 2, :].reshape(tok_dev, heads_here, HD).astype(jnp.float32)
    all_scores = (
        jnp.einsum("qhd,khd->hqk", glob_queries, local_keys, preferred_element_type=jnp.float32)
        * score_scale
    )
    local_peak = jnp.max(all_scores, axis=2)
    weights = jnp.exp(all_scores - local_peak[..., None])
    part_total = jnp.sum(weights, axis=2)
    part_accum = jnp.einsum("hqk,khd->hqd", weights, local_values, precision=lax.Precision.HIGHEST)
    peak_all, total_all, accum_all = combined_all(
        (local_peak, part_total, part_accum), "seq", combine_parts
    )
    glob_out = jnp.transpose(accum_all / total_all[..., None], (1, 0, 2)).reshape(tok_dev, columns)
    glob_out = glob_out.astype(jnp.bfloat16)
    attn_rows = jnp.where(own_index == owner_dev, glob_out, sparse)
    return lax.psum_scatter(
        jnp.dot(attn_rows, out_weight, preferred_element_type=jnp.float32).astype(jnp.bfloat16),
        "head",
        scatter_dimension=0,
        tiled=True,
    )


def ring_gather(block, own_index, owners):
    if owners % 2:
        ring = list(range(owners))
    else:
        half = owners // 2
        ring = [2 * i for i in range(half)] + [2 * i + 1 for i in reversed(range(half))]
    place = [0] * owners
    for i, s in enumerate(ring):
        place[s] = i
    right = [(ring[i], ring[(i + 1) % owners]) for i in range(owners)]
    left = [(ring[i], ring[(i - 1) % owners]) for i in range(owners)]
    pieces = {0: block}
    moving_right = block
    moving_left = block
    for step in range(1, owners // 2 + 1):
        if step == owners - step:
            cut = jax.tree.leaves(block)[0].shape[0] // 2
            head_half = jax.tree.map(lambda x: lax.ppermute(x[:cut], "seq", right), moving_right)
            tail_half = jax.tree.map(lambda x: lax.ppermute(x[cut:], "seq", left), moving_left)
            head_half, tail_half = lax.optimization_barrier((head_half, tail_half))
            pieces[-step] = jax.tree.map(
                lambda a, b: jnp.concatenate([a, b], axis=0), head_half, tail_half
            )
            break
        moving_right = jax.tree.map(lambda x: lax.ppermute(x, "seq", right), moving_right)
        moving_left = jax.tree.map(lambda x: lax.ppermute(x, "seq", left), moving_left)
        moving_right, moving_left = lax.optimization_barrier((moving_right, moving_left))
        pieces[-step] = moving_right
        pieces[step] = moving_left
    offsets = sorted(pieces)
    stacked = jax.tree.map(
        lambda *parts: jnp.concatenate(parts, axis=0), *[pieces[k] for k in offsets]
    )
    where = jnp.asarray(place, jnp.int32)[own_index]
    order = jnp.asarray(ring, jnp.int32)[(where + jnp.asarray(offsets, jnp.int32)) % owners]
    return stacked, order


def gathered_plan(projected, destination, doc_lengths, random_blocks, global_owner, out_weight):
    owners = lax.axis_size("seq")
    own_index = lax.axis_index("seq")
    tok_dev = projected.shape[0]
    columns = projected.shape[2]
    heads_here = columns // HD
    tokens = owners * tok_dev
    blocks_all = tokens // BLK
    score_scale = 1.0 / math.sqrt(HD)
    capacity = 2 * (tok_dev // owners)
    (keyval, key_dest), key_order = ring_gather(
        (projected[:, 1:, :], destination), own_index, owners
    )
    arrival_dest = key_dest
    target_all = arrival_dest.reshape(owners, tok_dev) // tok_dev
    onehot = (target_all[:, :, None] == jnp.arange(owners, dtype=jnp.int32)).astype(jnp.int32)
    slot_all = jnp.sum((jnp.cumsum(onehot, axis=1) - onehot) * onehot, axis=2)
    target = destination // tok_dev
    mine = (target[:, None] == jnp.arange(owners, dtype=jnp.int32)[None, :]).astype(jnp.int32)
    slot = jnp.sum((jnp.cumsum(mine, axis=0) - mine) * mine, axis=1)
    send_col = target * capacity + slot
    send_pick = (
        jnp.arange(owners * capacity, dtype=jnp.int32)[:, None] == send_col[None, :]
    ).astype(projected.dtype)
    outgoing = jnp.dot(send_pick, projected[:, 0, :], preferred_element_type=jnp.float32)
    outgoing = outgoing.astype(projected.dtype).reshape(owners, capacity, columns)
    incoming = lax.all_to_all(outgoing, "seq", split_axis=0, concat_axis=0, tiled=True)
    my_pos = own_index * tok_dev + jnp.arange(tok_dev, dtype=jnp.int32)
    source = jnp.repeat(key_order, tok_dev)
    land_col = (source * capacity + slot_all.reshape(-1))[None, :]
    hit = arrival_dest[None, :] == my_pos[:, None]
    col_of_pos = jnp.sum(jnp.where(hit, land_col, 0), axis=1)
    land_pick = (
        col_of_pos[:, None] == jnp.arange(owners * capacity, dtype=jnp.int32)[None, :]
    ).astype(projected.dtype)
    queries = jnp.dot(
        land_pick, incoming.reshape(owners * capacity, columns), preferred_element_type=jnp.float32
    )
    queries = queries.astype(projected.dtype).reshape(tok_dev, heads_here, HD)
    keys = keyval[:, 0, :].reshape(tokens, heads_here, HD)
    values = keyval[:, 1, :].reshape(tokens, heads_here, HD)
    scores = (
        jnp.einsum("qhd,khd->hqk", queries, keys, preferred_element_type=jnp.float32)
        * score_scale
    )
    bounds = jnp.cumsum(doc_lengths)
    key_block = key_dest // BLK
    key_doc = segment_of(key_dest, bounds)
    query_block = my_pos // BLK
    query_doc = segment_of(my_pos, bounds)
    same_doc = query_doc[:, None] == key_doc[None, :]
    window = jnp.zeros((tok_dev, tokens), jnp.int32)
    for step in (-1, 0, 1):
        near = (query_block + step) % blocks_all
        window = window + (key_block[None, :] == near[:, None]).astype(jnp.int32)
    window = jnp.where(same_doc, window, 0)
    chosen = random_blocks[query_block]
    drawn = jnp.zeros((tok_dev, tokens), jnp.int32)
    for r in range(chosen.shape[1]):
        drawn = drawn + (key_block[None, :] == chosen[:, r][:, None]).astype(jnp.int32)
    glob_start = global_owner[0] * tok_dev
    in_glob = (key_dest >= glob_start) & (key_dest < glob_start + tok_dev)
    holds_glob = own_index == global_owner[0]
    count = window + drawn + in_glob[None, :].astype(jnp.int32)
    count = jnp.where(holds_glob, 1, count)
    live = count > 0
    near_scores = jnp.where(live[None], scores, big_negative)
    row_peak = jnp.max(near_scores, axis=2)
    near_exp = jnp.exp(near_scores - row_peak[..., None])
    count_f = count.astype(jnp.float32)[None]
    denominator = jnp.sum(near_exp * count_f, axis=2)
    rounded = jnp.where(holds_glob, near_exp, near_exp.astype(jnp.bfloat16).astype(jnp.float32))
    weighted = rounded * count_f
    weight_hi = weighted.astype(jnp.bfloat16)
    weight_lo = (weighted - weight_hi.astype(jnp.float32)).astype(jnp.bfloat16)
    mixed_sum = jnp.einsum("hqk,khd->qhd", weight_hi, values, preferred_element_type=jnp.float32)
    mixed_sum = mixed_sum + jnp.einsum(
        "hqk,khd->qhd", weight_lo, values, preferred_element_type=jnp.float32
    )
    attn_rows = (mixed_sum / jnp.transpose(denominator)[..., None]).reshape(tok_dev, columns)
    attn_rows = attn_rows.astype(jnp.bfloat16)
    projected_rows = jnp.dot(attn_rows, out_weight, preferred_element_type=jnp.float32)
    return head_sum(lax.optimization_barrier(projected_rows))


def head_sum(partial):
    members = lax.axis_size("head")
    if members & (members - 1):
        return lax.psum_scatter(
            partial.astype(jnp.bfloat16), "head", scatter_dimension=0, tiled=True
        )
    me = lax.axis_index("head")
    rows = partial.shape[0] // members
    partial = partial.reshape(members, rows, partial.shape[1])
    bit = 1
    while bit < members:
        pairs = partial.reshape(partial.shape[0] // 2, 2, rows, partial.shape[2])
        upper = (me & bit) != 0
        keep = jnp.where(upper, pairs[:, 1], pairs[:, 0])
        send = jnp.where(upper, pairs[:, 0], pairs[:, 1]).astype(jnp.bfloat16)
        got = lax.ppermute(send, "head", [(i, i ^ bit) for i in range(members)])
        partial = keep + got.astype(jnp.float32)
        bit *= 2
    partial = partial.reshape(rows, partial.shape[2])
    return partial.astype(jnp.bfloat16)


GATHER_LIMIT = 16 * 2**20


def shards(projected, destination, doc_lengths, random_blocks, global_owner, out_weight):
    gathered_bytes = lax.axis_size("seq") * projected.size * projected.dtype.itemsize
    if gathered_bytes <= GATHER_LIMIT:
        return gathered_plan(
            projected, destination, doc_lengths, random_blocks, global_owner, out_weight
        )
    return shards_ring(projected, destination, doc_lengths, random_blocks, global_owner, out_weight)


def solution(mesh):
    in_specs = (P("seq", None, "head"), P("seq"), P(), P(), P(), P("head", None))
    out_specs = P(("seq", "head"), None)
    return jax.shard_map(shards, mesh=mesh, in_specs=in_specs, out_specs=out_specs, check_vma=False)
```

```python
import math

import jax
import jax.numpy as jnp
from jax import lax
from jax.sharding import PartitionSpec as P

HD = 128
BLK = 128
R = 3
RDEV = 2


big_negative = -1e30


def from_behind(block, axis, distance):
    devices = range(lax.axis_size(axis))
    route = [((i - distance) % len(devices), i) for i in devices]
    return lax.ppermute(block, axis, route)


def from_root(x, axis, root):
    mine = lax.axis_index(axis) == root
    return lax.psum(jnp.where(mine, x, jnp.zeros_like(x)), axis)


def combined_all(x, axis, combine):
    everything = jax.tree.map(lambda part: lax.all_gather(part, axis), x)
    first = jax.tree.map(lambda part: part[0], everything)

    def step(k, so_far):
        return combine(so_far, jax.tree.map(lambda part: part[k], everything))

    return lax.fori_loop(1, lax.axis_size(axis), step, first)


def segment_of(positions, bounds):
    return jnp.sum((bounds[None, :] <= positions[:, None]).astype(jnp.int32), axis=1)


def combine_parts(left_part, right_part):
    top_left, total_left, accum_left = left_part
    top_right, total_right, accum_right = right_part
    row_peak = jnp.maximum(top_left, top_right)
    factor_left = jnp.exp(top_left - row_peak)
    factor_right = jnp.exp(top_right - row_peak)
    return (
        row_peak,
        total_left * factor_left + total_right * factor_right,
        accum_left * factor_left[:, :, None] + accum_right * factor_right[:, :, None],
    )


def shards_ring(projected, destination, doc_lengths, random_blocks, global_owner, out_weight):
    owners = lax.axis_size("seq")
    own_index = lax.axis_index("seq")
    tok_dev = projected.shape[0]
    columns = projected.shape[2]
    heads_here = columns // HD
    per_dev = tok_dev // BLK
    blocks_all = owners * per_dev
    capacity = 2 * (tok_dev // owners)
    score_scale = 1.0 / math.sqrt(HD)
    target_owner = destination // tok_dev
    onehot = (target_owner[:, None] == jnp.arange(owners, dtype=jnp.int32)[None, :]).astype(
        jnp.int32
    )
    before = jnp.cumsum(onehot, axis=0) - onehot
    slot_rank = jnp.sum(before * onehot, axis=1)
    outgoing = (
        jnp.zeros((owners, capacity, 3, columns), projected.dtype)
        .at[target_owner, slot_rank]
        .set(projected)
    )
    slots = (
        jnp.full((owners, capacity), -1, jnp.int32)
        .at[target_owner, slot_rank]
        .set(destination % tok_dev)
    )
    incoming, landing = (
        lax.all_to_all(outgoing, "seq", split_axis=0, concat_axis=0, tiled=True),
        lax.all_to_all(slots, "seq", split_axis=0, concat_axis=0, tiled=True),
    )
    landing = landing.reshape(-1)
    landing = jnp.where(landing >= 0, landing, tok_dev)
    routed = (
        jnp.zeros((tok_dev, 3, columns), projected.dtype)
        .at[landing]
        .set(incoming.reshape(owners * capacity, 3, columns), mode="drop")
    )
    keyval = routed[:, 1:, :]
    fetched = {0: keyval}
    offsets = list(range(-RDEV, 0)) + list(range(1, RDEV + 1))
    for offset in offsets:
        fetched[offset] = from_behind(keyval, "seq", -offset)
    band_blocks = jnp.stack([fetched[offset] for offset in range(-RDEV, RDEV + 1)])
    block_ids = own_index * per_dev + jnp.arange(per_dev, dtype=jnp.int32)
    local_pick = jnp.arange(per_dev, dtype=jnp.int32) + RDEV * per_dev
    window_pick = local_pick[:, None] + jnp.arange(-1, 2, dtype=jnp.int32)[None, :]
    chosen_rand = lax.dynamic_slice_in_dim(random_blocks, own_index * per_dev, per_dev, 0)
    away_dev = (chosen_rand // per_dev - own_index) % owners
    away_dev = jnp.where(away_dev > owners // 2, away_dev - owners, away_dev)
    rand_pick = (away_dev + RDEV) * per_dev + chosen_rand % per_dev
    block_picks = jnp.concatenate([window_pick, rand_pick], axis=1)
    gathered = jnp.take(band_blocks, block_picks, axis=0)
    near_keys = gathered[:, :, :, 0, :].reshape(per_dev, (3 + R) * BLK, heads_here, HD)
    near_values = gathered[:, :, :, 1, :].reshape(per_dev, (3 + R) * BLK, heads_here, HD)
    owner_dev = global_owner[0]
    global_rows = from_root(routed, "seq", owner_dev)
    glob_keys = global_rows[:, 1, :].reshape(tok_dev, heads_here, HD)
    glob_values = global_rows[:, 2, :].reshape(tok_dev, heads_here, HD)
    queries = routed[:, 0, :].reshape(per_dev, BLK, heads_here, HD)
    near_scores = (
        jnp.einsum("bqhd,bkhd->bhqk", queries, near_keys, preferred_element_type=jnp.float32)
        * score_scale
    )
    far_scores = (
        jnp.einsum("bqhd,khd->bhqk", queries, glob_keys, preferred_element_type=jnp.float32)
        * score_scale
    )
    bounds = jnp.cumsum(doc_lengths)
    query_pos = own_index * tok_dev + jnp.arange(tok_dev, dtype=jnp.int32)
    query_doc = segment_of(query_pos, bounds).reshape(per_dev, BLK)
    window_blocks = (block_ids[:, None] + jnp.arange(-1, 2, dtype=jnp.int32)[None, :]) % blocks_all
    key_pos = (
        window_blocks[:, :, None] * BLK + jnp.arange(BLK, dtype=jnp.int32)[None, None, :]
    ).reshape(-1)
    key_doc = segment_of(key_pos, bounds).reshape(per_dev, 3 * BLK)
    same_doc = query_doc[:, :, None] == key_doc[:, None, :]
    allowed = jnp.concatenate(
        [same_doc, jnp.ones((per_dev, BLK, R * BLK), dtype=jnp.bool_)], axis=2
    )
    near_scores = jnp.where(allowed[:, None], near_scores, big_negative)
    row_peak = jnp.maximum(jnp.max(near_scores, axis=3), jnp.max(far_scores, axis=3))
    near_exp = jnp.exp(near_scores - row_peak[..., None])
    far_exp = jnp.exp(far_scores - row_peak[..., None])
    denominator = jnp.sum(near_exp, axis=3) + jnp.sum(far_exp, axis=3)
    mixed_sum = jnp.einsum(
        "bhqk,bkhd->bqhd",
        near_exp.astype(jnp.bfloat16),
        near_values,
        preferred_element_type=jnp.float32,
    )
    mixed_sum = mixed_sum + jnp.einsum(
        "bhqk,khd->bqhd",
        far_exp.astype(jnp.bfloat16),
        glob_values,
        preferred_element_type=jnp.float32,
    )
    sparse = (mixed_sum / jnp.transpose(denominator, (0, 2, 1))[..., None]).reshape(
        tok_dev, columns
    )
    sparse = sparse.astype(jnp.bfloat16)
    glob_queries = global_rows[:, 0, :].reshape(tok_dev, heads_here, HD)
    local_keys = routed[:, 1, :].reshape(tok_dev, heads_here, HD)
    local_values = routed[:, 2, :].reshape(tok_dev, heads_here, HD).astype(jnp.float32)
    all_scores = (
        jnp.einsum("qhd,khd->hqk", glob_queries, local_keys, preferred_element_type=jnp.float32)
        * score_scale
    )
    local_peak = jnp.max(all_scores, axis=2)
    weights = jnp.exp(all_scores - local_peak[..., None])
    part_total = jnp.sum(weights, axis=2)
    part_accum = jnp.einsum("hqk,khd->hqd", weights, local_values, precision=lax.Precision.HIGHEST)
    peak_all, total_all, accum_all = combined_all(
        (local_peak, part_total, part_accum), "seq", combine_parts
    )
    glob_out = jnp.transpose(accum_all / total_all[..., None], (1, 0, 2)).reshape(tok_dev, columns)
    glob_out = glob_out.astype(jnp.bfloat16)
    attn_rows = jnp.where(own_index == owner_dev, glob_out, sparse)
    return lax.psum_scatter(
        jnp.dot(attn_rows, out_weight, preferred_element_type=jnp.float32).astype(jnp.bfloat16),
        "head",
        scatter_dimension=0,
        tiled=True,
    )


def ring_gather(block, own_index, owners, rider):
    if owners % 2:
        ring = list(range(owners))
    else:
        half = owners // 2
        ring = [2 * i for i in range(half)] + [2 * i + 1 for i in reversed(range(half))]
    place = [0] * owners
    for i, s in enumerate(ring):
        place[s] = i
    right = [(ring[i], ring[(i + 1) % owners]) for i in range(owners)]
    left = [(ring[i], ring[(i - 1) % owners]) for i in range(owners)]
    pieces = {0: block}
    moving_right = block
    moving_left = block
    for step in range(1, owners // 2 + 1):
        if step == owners - step:
            cut = jax.tree.leaves(block)[0].shape[0] // 2
            head_half = jax.tree.map(lambda x: lax.ppermute(x[:cut], "seq", right), moving_right)
            tail_half = jax.tree.map(lambda x: lax.ppermute(x[cut:], "seq", left), moving_left)
            head_half, tail_half = lax.optimization_barrier((head_half, tail_half))
            pieces[-step] = jax.tree.map(
                lambda a, b: jnp.concatenate([a, b], axis=0), head_half, tail_half
            )
            break
        moving_right = jax.tree.map(lambda x: lax.ppermute(x, "seq", right), moving_right)
        moving_left = jax.tree.map(lambda x: lax.ppermute(x, "seq", left), moving_left)
        if step == owners // 2 - 1 or owners < 4:
            moving_right, moving_left, rider = lax.optimization_barrier(
                (moving_right, moving_left, rider)
            )
        else:
            moving_right, moving_left = lax.optimization_barrier((moving_right, moving_left))
        pieces[-step] = moving_right
        pieces[step] = moving_left
    offsets = sorted(pieces)
    stacked = jax.tree.map(
        lambda *parts: jnp.concatenate(parts, axis=0), *[pieces[k] for k in offsets]
    )
    where = jnp.asarray(place, jnp.int32)[own_index]
    order = jnp.asarray(ring, jnp.int32)[(where + jnp.asarray(offsets, jnp.int32)) % owners]
    return stacked, order, rider


def gathered_plan(projected, destination, doc_lengths, random_blocks, global_owner, out_weight):
    owners = lax.axis_size("seq")
    own_index = lax.axis_index("seq")
    tok_dev = projected.shape[0]
    columns = projected.shape[2]
    heads_here = columns // HD
    tokens = owners * tok_dev
    blocks_all = tokens // BLK
    score_scale = 1.0 / math.sqrt(HD)
    capacity = 2 * (tok_dev // owners)
    target = destination // tok_dev
    mine = (target[:, None] == jnp.arange(owners, dtype=jnp.int32)[None, :]).astype(jnp.int32)
    slot = jnp.sum((jnp.cumsum(mine, axis=0) - mine) * mine, axis=1)
    send_col = target * capacity + slot
    send_pick = (
        jnp.arange(owners * capacity, dtype=jnp.int32)[:, None] == send_col[None, :]
    ).astype(projected.dtype)
    outgoing = jnp.dot(send_pick, projected[:, 0, :], preferred_element_type=jnp.float32)
    outgoing = outgoing.astype(projected.dtype).reshape(owners, capacity, columns)
    (keyval, key_dest), key_order, outgoing = ring_gather(
        (projected[:, 1:, :], destination), own_index, owners, outgoing
    )
    arrival_dest = key_dest
    target_all = arrival_dest.reshape(owners, tok_dev) // tok_dev
    onehot = (target_all[:, :, None] == jnp.arange(owners, dtype=jnp.int32)).astype(jnp.int32)
    slot_all = jnp.sum((jnp.cumsum(onehot, axis=1) - onehot) * onehot, axis=2)
    incoming = lax.all_to_all(outgoing, "seq", split_axis=0, concat_axis=0, tiled=True)
    my_pos = own_index * tok_dev + jnp.arange(tok_dev, dtype=jnp.int32)
    source = jnp.repeat(key_order, tok_dev)
    land_col = (source * capacity + slot_all.reshape(-1))[None, :]
    hit = arrival_dest[None, :] == my_pos[:, None]
    col_of_pos = jnp.sum(jnp.where(hit, land_col, 0), axis=1)
    land_pick = (
        col_of_pos[:, None] == jnp.arange(owners * capacity, dtype=jnp.int32)[None, :]
    ).astype(projected.dtype)
    queries = jnp.dot(
        land_pick, incoming.reshape(owners * capacity, columns), preferred_element_type=jnp.float32
    )
    queries = queries.astype(projected.dtype).reshape(tok_dev, heads_here, HD)
    keys = keyval[:, 0, :].reshape(tokens, heads_here, HD)
    values = keyval[:, 1, :].reshape(tokens, heads_here, HD)
    scores = (
        jnp.einsum("qhd,khd->hqk", queries, keys, preferred_element_type=jnp.float32)
        * score_scale
    )
    bounds = jnp.cumsum(doc_lengths)
    key_block = key_dest // BLK
    key_doc = segment_of(key_dest, bounds)
    query_block = my_pos // BLK
    query_doc = segment_of(my_pos, bounds)
    same_doc = query_doc[:, None] == key_doc[None, :]
    window = jnp.zeros((tok_dev, tokens), jnp.int32)
    for step in (-1, 0, 1):
        near = (query_block + step) % blocks_all
        window = window + (key_block[None, :] == near[:, None]).astype(jnp.int32)
    window = jnp.where(same_doc, window, 0)
    chosen = random_blocks[query_block]
    drawn = jnp.zeros((tok_dev, tokens), jnp.int32)
    for r in range(chosen.shape[1]):
        drawn = drawn + (key_block[None, :] == chosen[:, r][:, None]).astype(jnp.int32)
    glob_start = global_owner[0] * tok_dev
    in_glob = (key_dest >= glob_start) & (key_dest < glob_start + tok_dev)
    holds_glob = own_index == global_owner[0]
    count = window + drawn + in_glob[None, :].astype(jnp.int32)
    count = jnp.where(holds_glob, 1, count)
    live = count > 0
    near_scores = jnp.where(live[None], scores, big_negative)
    row_peak = jnp.max(near_scores, axis=2)
    near_exp = jnp.exp(near_scores - row_peak[..., None])
    count_f = count.astype(jnp.float32)[None]
    denominator = jnp.sum(near_exp * count_f, axis=2)
    rounded = jnp.where(holds_glob, near_exp, near_exp.astype(jnp.bfloat16).astype(jnp.float32))
    weighted = rounded * count_f
    weight_hi = weighted.astype(jnp.bfloat16)
    weight_lo = (weighted - weight_hi.astype(jnp.float32)).astype(jnp.bfloat16)
    mixed_sum = jnp.einsum("hqk,khd->qhd", weight_hi, values, preferred_element_type=jnp.float32)
    mixed_sum = mixed_sum + jnp.einsum(
        "hqk,khd->qhd", weight_lo, values, preferred_element_type=jnp.float32
    )
    attn_rows = (mixed_sum / jnp.transpose(denominator)[..., None]).reshape(tok_dev, columns)
    attn_rows = attn_rows.astype(jnp.bfloat16)
    projected_rows = jnp.dot(attn_rows, out_weight, preferred_element_type=jnp.float32)
    return head_sum(lax.optimization_barrier(projected_rows))


def head_sum(partial):
    members = lax.axis_size("head")
    if members & (members - 1):
        return lax.psum_scatter(
            partial.astype(jnp.bfloat16), "head", scatter_dimension=0, tiled=True
        )
    me = lax.axis_index("head")
    rows = partial.shape[0] // members
    partial = partial.reshape(members, rows, partial.shape[1])
    bit = 1
    while bit < members:
        pairs = partial.reshape(partial.shape[0] // 2, 2, rows, partial.shape[2])
        upper = (me & bit) != 0
        keep = jnp.where(upper, pairs[:, 1], pairs[:, 0])
        send = jnp.where(upper, pairs[:, 0], pairs[:, 1]).astype(jnp.bfloat16)
        got = lax.ppermute(send, "head", [(i, i ^ bit) for i in range(members)])
        partial = keep + got.astype(jnp.float32)
        bit *= 2
    partial = partial.reshape(rows, partial.shape[2])
    return partial.astype(jnp.bfloat16)


GATHER_LIMIT = 16 * 2**20


def shards(projected, destination, doc_lengths, random_blocks, global_owner, out_weight):
    gathered_bytes = lax.axis_size("seq") * projected.size * projected.dtype.itemsize
    if gathered_bytes <= GATHER_LIMIT:
        return gathered_plan(
            projected, destination, doc_lengths, random_blocks, global_owner, out_weight
        )
    return shards_ring(projected, destination, doc_lengths, random_blocks, global_owner, out_weight)


def solution(mesh):
    in_specs = (P("seq", None, "head"), P("seq"), P(), P(), P(), P("head", None))
    out_specs = P(("seq", "head"), None)
    return jax.shard_map(shards, mesh=mesh, in_specs=in_specs, out_specs=out_specs, check_vma=False)
```

```python
import math

import jax
import jax.numpy as jnp
from jax import lax
from jax.sharding import PartitionSpec as P

HD = 128
BLK = 128
R = 3
RDEV = 2


big_negative = -1e30


def from_behind(block, axis, distance):
    devices = range(lax.axis_size(axis))
    route = [((i - distance) % len(devices), i) for i in devices]
    return lax.ppermute(block, axis, route)


def from_root(x, axis, root):
    mine = lax.axis_index(axis) == root
    return lax.psum(jnp.where(mine, x, jnp.zeros_like(x)), axis)


def combined_all(x, axis, combine):
    everything = jax.tree.map(lambda part: lax.all_gather(part, axis), x)
    first = jax.tree.map(lambda part: part[0], everything)

    def step(k, so_far):
        return combine(so_far, jax.tree.map(lambda part: part[k], everything))

    return lax.fori_loop(1, lax.axis_size(axis), step, first)


def segment_of(positions, bounds):
    return jnp.sum((bounds[None, :] <= positions[:, None]).astype(jnp.int32), axis=1)


def combine_parts(left_part, right_part):
    top_left, total_left, accum_left = left_part
    top_right, total_right, accum_right = right_part
    row_peak = jnp.maximum(top_left, top_right)
    factor_left = jnp.exp(top_left - row_peak)
    factor_right = jnp.exp(top_right - row_peak)
    return (
        row_peak,
        total_left * factor_left + total_right * factor_right,
        accum_left * factor_left[:, :, None] + accum_right * factor_right[:, :, None],
    )


def shards_ring(projected, destination, doc_lengths, random_blocks, global_owner, out_weight):
    owners = lax.axis_size("seq")
    own_index = lax.axis_index("seq")
    tok_dev = projected.shape[0]
    columns = projected.shape[2]
    heads_here = columns // HD
    per_dev = tok_dev // BLK
    blocks_all = owners * per_dev
    capacity = 2 * (tok_dev // owners)
    score_scale = 1.0 / math.sqrt(HD)
    target_owner = destination // tok_dev
    onehot = (target_owner[:, None] == jnp.arange(owners, dtype=jnp.int32)[None, :]).astype(
        jnp.int32
    )
    before = jnp.cumsum(onehot, axis=0) - onehot
    slot_rank = jnp.sum(before * onehot, axis=1)
    outgoing = (
        jnp.zeros((owners, capacity, 3, columns), projected.dtype)
        .at[target_owner, slot_rank]
        .set(projected)
    )
    slots = (
        jnp.full((owners, capacity), -1, jnp.int32)
        .at[target_owner, slot_rank]
        .set(destination % tok_dev)
    )
    incoming, landing = (
        lax.all_to_all(outgoing, "seq", split_axis=0, concat_axis=0, tiled=True),
        lax.all_to_all(slots, "seq", split_axis=0, concat_axis=0, tiled=True),
    )
    landing = landing.reshape(-1)
    landing = jnp.where(landing >= 0, landing, tok_dev)
    routed = (
        jnp.zeros((tok_dev, 3, columns), projected.dtype)
        .at[landing]
        .set(incoming.reshape(owners * capacity, 3, columns), mode="drop")
    )
    keyval = routed[:, 1:, :]
    fetched = {0: keyval}
    offsets = list(range(-RDEV, 0)) + list(range(1, RDEV + 1))
    for offset in offsets:
        fetched[offset] = from_behind(keyval, "seq", -offset)
    band_blocks = jnp.stack([fetched[offset] for offset in range(-RDEV, RDEV + 1)])
    block_ids = own_index * per_dev + jnp.arange(per_dev, dtype=jnp.int32)
    local_pick = jnp.arange(per_dev, dtype=jnp.int32) + RDEV * per_dev
    window_pick = local_pick[:, None] + jnp.arange(-1, 2, dtype=jnp.int32)[None, :]
    chosen_rand = lax.dynamic_slice_in_dim(random_blocks, own_index * per_dev, per_dev, 0)
    away_dev = (chosen_rand // per_dev - own_index) % owners
    away_dev = jnp.where(away_dev > owners // 2, away_dev - owners, away_dev)
    rand_pick = (away_dev + RDEV) * per_dev + chosen_rand % per_dev
    block_picks = jnp.concatenate([window_pick, rand_pick], axis=1)
    gathered = jnp.take(band_blocks, block_picks, axis=0)
    near_keys = gathered[:, :, :, 0, :].reshape(per_dev, (3 + R) * BLK, heads_here, HD)
    near_values = gathered[:, :, :, 1, :].reshape(per_dev, (3 + R) * BLK, heads_here, HD)
    owner_dev = global_owner[0]
    global_rows = from_root(routed, "seq", owner_dev)
    glob_keys = global_rows[:, 1, :].reshape(tok_dev, heads_here, HD)
    glob_values = global_rows[:, 2, :].reshape(tok_dev, heads_here, HD)
    queries = routed[:, 0, :].reshape(per_dev, BLK, heads_here, HD)
    near_scores = (
        jnp.einsum("bqhd,bkhd->bhqk", queries, near_keys, preferred_element_type=jnp.float32)
        * score_scale
    )
    far_scores = (
        jnp.einsum("bqhd,khd->bhqk", queries, glob_keys, preferred_element_type=jnp.float32)
        * score_scale
    )
    bounds = jnp.cumsum(doc_lengths)
    query_pos = own_index * tok_dev + jnp.arange(tok_dev, dtype=jnp.int32)
    query_doc = segment_of(query_pos, bounds).reshape(per_dev, BLK)
    window_blocks = (block_ids[:, None] + jnp.arange(-1, 2, dtype=jnp.int32)[None, :]) % blocks_all
    key_pos = (
        window_blocks[:, :, None] * BLK + jnp.arange(BLK, dtype=jnp.int32)[None, None, :]
    ).reshape(-1)
    key_doc = segment_of(key_pos, bounds).reshape(per_dev, 3 * BLK)
    same_doc = query_doc[:, :, None] == key_doc[:, None, :]
    allowed = jnp.concatenate(
        [same_doc, jnp.ones((per_dev, BLK, R * BLK), dtype=jnp.bool_)], axis=2
    )
    near_scores = jnp.where(allowed[:, None], near_scores, big_negative)
    row_peak = jnp.maximum(jnp.max(near_scores, axis=3), jnp.max(far_scores, axis=3))
    near_exp = jnp.exp(near_scores - row_peak[..., None])
    far_exp = jnp.exp(far_scores - row_peak[..., None])
    denominator = jnp.sum(near_exp, axis=3) + jnp.sum(far_exp, axis=3)
    mixed_sum = jnp.einsum(
        "bhqk,bkhd->bqhd",
        near_exp.astype(jnp.bfloat16),
        near_values,
        preferred_element_type=jnp.float32,
    )
    mixed_sum = mixed_sum + jnp.einsum(
        "bhqk,khd->bqhd",
        far_exp.astype(jnp.bfloat16),
        glob_values,
        preferred_element_type=jnp.float32,
    )
    sparse = (mixed_sum / jnp.transpose(denominator, (0, 2, 1))[..., None]).reshape(
        tok_dev, columns
    )
    sparse = sparse.astype(jnp.bfloat16)
    glob_queries = global_rows[:, 0, :].reshape(tok_dev, heads_here, HD)
    local_keys = routed[:, 1, :].reshape(tok_dev, heads_here, HD)
    local_values = routed[:, 2, :].reshape(tok_dev, heads_here, HD).astype(jnp.float32)
    all_scores = (
        jnp.einsum("qhd,khd->hqk", glob_queries, local_keys, preferred_element_type=jnp.float32)
        * score_scale
    )
    local_peak = jnp.max(all_scores, axis=2)
    weights = jnp.exp(all_scores - local_peak[..., None])
    part_total = jnp.sum(weights, axis=2)
    part_accum = jnp.einsum("hqk,khd->hqd", weights, local_values, precision=lax.Precision.HIGHEST)
    peak_all, total_all, accum_all = combined_all(
        (local_peak, part_total, part_accum), "seq", combine_parts
    )
    glob_out = jnp.transpose(accum_all / total_all[..., None], (1, 0, 2)).reshape(tok_dev, columns)
    glob_out = glob_out.astype(jnp.bfloat16)
    attn_rows = jnp.where(own_index == owner_dev, glob_out, sparse)
    return lax.psum_scatter(
        jnp.dot(attn_rows, out_weight, preferred_element_type=jnp.float32).astype(jnp.bfloat16),
        "head",
        scatter_dimension=0,
        tiled=True,
    )


def ring_gather(block, own_index, owners):
    if owners % 2:
        ring = list(range(owners))
    else:
        half = owners // 2
        ring = [2 * i for i in range(half)] + [2 * i + 1 for i in reversed(range(half))]
    place = [0] * owners
    for i, s in enumerate(ring):
        place[s] = i
    right = [(ring[i], ring[(i + 1) % owners]) for i in range(owners)]
    left = [(ring[i], ring[(i - 1) % owners]) for i in range(owners)]
    pieces = {0: block}
    moving_right = block
    moving_left = block
    for step in range(1, owners // 2 + 1):
        moving_right = jax.tree.map(lambda x: lax.ppermute(x, "seq", right), moving_right)
        pieces[-step] = moving_right
        if step <= (owners - 1) // 2:
            moving_left = jax.tree.map(lambda x: lax.ppermute(x, "seq", left), moving_left)
            moving_right, moving_left = lax.optimization_barrier((moving_right, moving_left))
            pieces[step] = moving_left
        pieces[-step] = moving_right
    offsets = sorted(pieces)
    stacked = jax.tree.map(
        lambda *parts: jnp.concatenate(parts, axis=0), *[pieces[k] for k in offsets]
    )
    where = jnp.asarray(place, jnp.int32)[own_index]
    order = jnp.asarray(ring, jnp.int32)[(where + jnp.asarray(offsets, jnp.int32)) % owners]
    return stacked, order, [pieces[k] for k in offsets]


def gathered_plan(projected, destination, doc_lengths, random_blocks, global_owner, out_weight):
    owners = lax.axis_size("seq")
    own_index = lax.axis_index("seq")
    tok_dev = projected.shape[0]
    columns = projected.shape[2]
    heads_here = columns // HD
    tokens = owners * tok_dev
    blocks_all = tokens // BLK
    score_scale = 1.0 / math.sqrt(HD)
    capacity = 2 * (tok_dev // owners)
    (_, key_dest), key_order, arrived = ring_gather(
        (projected[:, 1:, :], destination), own_index, owners
    )
    arrived = [piece for piece, _ in arrived]
    arrival_dest = key_dest
    target_all = arrival_dest.reshape(owners, tok_dev) // tok_dev
    onehot = (target_all[:, :, None] == jnp.arange(owners, dtype=jnp.int32)).astype(jnp.int32)
    slot_all = jnp.sum((jnp.cumsum(onehot, axis=1) - onehot) * onehot, axis=2)
    target = destination // tok_dev
    mine = (target[:, None] == jnp.arange(owners, dtype=jnp.int32)[None, :]).astype(jnp.int32)
    slot = jnp.sum((jnp.cumsum(mine, axis=0) - mine) * mine, axis=1)
    send_col = target * capacity + slot
    send_pick = (
        jnp.arange(owners * capacity, dtype=jnp.int32)[:, None] == send_col[None, :]
    ).astype(projected.dtype)
    outgoing = jnp.dot(send_pick, projected[:, 0, :], preferred_element_type=jnp.float32)
    outgoing = outgoing.astype(projected.dtype).reshape(owners, capacity, columns)
    incoming = lax.all_to_all(outgoing, "seq", split_axis=0, concat_axis=0, tiled=True)
    my_pos = own_index * tok_dev + jnp.arange(tok_dev, dtype=jnp.int32)
    source = jnp.repeat(key_order, tok_dev)
    land_col = (source * capacity + slot_all.reshape(-1))[None, :]
    hit = arrival_dest[None, :] == my_pos[:, None]
    col_of_pos = jnp.sum(jnp.where(hit, land_col, 0), axis=1)
    land_pick = (
        col_of_pos[:, None] == jnp.arange(owners * capacity, dtype=jnp.int32)[None, :]
    ).astype(projected.dtype)
    queries = jnp.dot(
        land_pick, incoming.reshape(owners * capacity, columns), preferred_element_type=jnp.float32
    )
    queries = queries.astype(projected.dtype).reshape(tok_dev, heads_here, HD)
    values = [piece[:, 1, :].reshape(tok_dev, heads_here, HD) for piece in arrived]
    scores = jnp.concatenate(
        [
            jnp.einsum(
                "qhd,khd->hqk",
                queries,
                piece[:, 0, :].reshape(tok_dev, heads_here, HD),
                preferred_element_type=jnp.float32,
            )
            for piece in arrived
        ],
        axis=2,
    ) * score_scale
    bounds = jnp.cumsum(doc_lengths)
    key_block = key_dest // BLK
    key_doc = segment_of(key_dest, bounds)
    query_block = my_pos // BLK
    query_doc = segment_of(my_pos, bounds)
    same_doc = query_doc[:, None] == key_doc[None, :]
    window = jnp.zeros((tok_dev, tokens), jnp.int32)
    for step in (-1, 0, 1):
        near = (query_block + step) % blocks_all
        window = window + (key_block[None, :] == near[:, None]).astype(jnp.int32)
    window = jnp.where(same_doc, window, 0)
    chosen = random_blocks[query_block]
    drawn = jnp.zeros((tok_dev, tokens), jnp.int32)
    for r in range(chosen.shape[1]):
        drawn = drawn + (key_block[None, :] == chosen[:, r][:, None]).astype(jnp.int32)
    glob_start = global_owner[0] * tok_dev
    in_glob = (key_dest >= glob_start) & (key_dest < glob_start + tok_dev)
    holds_glob = own_index == global_owner[0]
    count = window + drawn + in_glob[None, :].astype(jnp.int32)
    count = jnp.where(holds_glob, 1, count)
    live = count > 0
    near_scores = jnp.where(live[None], scores, big_negative)
    row_peak = jnp.max(near_scores, axis=2)
    near_exp = jnp.exp(near_scores - row_peak[..., None])
    count_f = count.astype(jnp.float32)[None]
    denominator = jnp.sum(near_exp * count_f, axis=2)
    rounded = jnp.where(holds_glob, near_exp, near_exp.astype(jnp.bfloat16).astype(jnp.float32))
    weighted = rounded * count_f
    weight_hi = weighted.astype(jnp.bfloat16)
    weight_lo = (weighted - weight_hi.astype(jnp.float32)).astype(jnp.bfloat16)
    mixed_sum = 0.0
    for index, piece_values in enumerate(values):
        span = slice(index * tok_dev, (index + 1) * tok_dev)
        for weight in (weight_hi, weight_lo):
            mixed_sum = mixed_sum + jnp.einsum(
                "hqk,khd->qhd", weight[:, :, span], piece_values, preferred_element_type=jnp.float32
            )
    attn_rows = (mixed_sum / jnp.transpose(denominator)[..., None]).reshape(tok_dev, columns)
    attn_rows = attn_rows.astype(jnp.bfloat16)
    projected_rows = jnp.dot(attn_rows, out_weight, preferred_element_type=jnp.float32)
    return head_sum(lax.optimization_barrier(projected_rows))


def head_sum(partial):
    members = lax.axis_size("head")
    if members & (members - 1):
        return lax.psum_scatter(
            partial.astype(jnp.bfloat16), "head", scatter_dimension=0, tiled=True
        )
    me = lax.axis_index("head")
    rows = partial.shape[0] // members
    partial = partial.reshape(members, rows, partial.shape[1])
    bit = 1
    while bit < members:
        pairs = partial.reshape(partial.shape[0] // 2, 2, rows, partial.shape[2])
        upper = (me & bit) != 0
        keep = jnp.where(upper, pairs[:, 1], pairs[:, 0])
        send = jnp.where(upper, pairs[:, 0], pairs[:, 1]).astype(jnp.bfloat16)
        got = lax.ppermute(send, "head", [(i, i ^ bit) for i in range(members)])
        partial = keep + got.astype(jnp.float32)
        bit *= 2
    partial = partial.reshape(rows, partial.shape[2])
    return partial.astype(jnp.bfloat16)


GATHER_LIMIT = 16 * 2**20


def shards(projected, destination, doc_lengths, random_blocks, global_owner, out_weight):
    gathered_bytes = lax.axis_size("seq") * projected.size * projected.dtype.itemsize
    if gathered_bytes <= GATHER_LIMIT:
        return gathered_plan(
            projected, destination, doc_lengths, random_blocks, global_owner, out_weight
        )
    return shards_ring(projected, destination, doc_lengths, random_blocks, global_owner, out_weight)


def solution(mesh):
    in_specs = (P("seq", None, "head"), P("seq"), P(), P(), P(), P("head", None))
    out_specs = P(("seq", "head"), None)
    return jax.shard_map(shards, mesh=mesh, in_specs=in_specs, out_specs=out_specs, check_vma=False)
```

```python
import math

import jax
import jax.numpy as jnp
from jax import lax
from jax.sharding import PartitionSpec as P

HD = 128
BLK = 128
R = 3
RDEV = 2


big_negative = -1e30


def from_behind(block, axis, distance):
    devices = range(lax.axis_size(axis))
    route = [((i - distance) % len(devices), i) for i in devices]
    return lax.ppermute(block, axis, route)


def from_root(x, axis, root):
    mine = lax.axis_index(axis) == root
    return lax.psum(jnp.where(mine, x, jnp.zeros_like(x)), axis)


def combined_all(x, axis, combine):
    everything = jax.tree.map(lambda part: lax.all_gather(part, axis), x)
    first = jax.tree.map(lambda part: part[0], everything)

    def step(k, so_far):
        return combine(so_far, jax.tree.map(lambda part: part[k], everything))

    return lax.fori_loop(1, lax.axis_size(axis), step, first)


def segment_of(positions, bounds):
    return jnp.sum((bounds[None, :] <= positions[:, None]).astype(jnp.int32), axis=1)


def combine_parts(left_part, right_part):
    top_left, total_left, accum_left = left_part
    top_right, total_right, accum_right = right_part
    row_peak = jnp.maximum(top_left, top_right)
    factor_left = jnp.exp(top_left - row_peak)
    factor_right = jnp.exp(top_right - row_peak)
    return (
        row_peak,
        total_left * factor_left + total_right * factor_right,
        accum_left * factor_left[:, :, None] + accum_right * factor_right[:, :, None],
    )


def shards_ring(projected, destination, doc_lengths, random_blocks, global_owner, out_weight):
    owners = lax.axis_size("seq")
    own_index = lax.axis_index("seq")
    tok_dev = projected.shape[0]
    columns = projected.shape[2]
    heads_here = columns // HD
    per_dev = tok_dev // BLK
    blocks_all = owners * per_dev
    capacity = 2 * (tok_dev // owners)
    score_scale = 1.0 / math.sqrt(HD)
    target_owner = destination // tok_dev
    onehot = (target_owner[:, None] == jnp.arange(owners, dtype=jnp.int32)[None, :]).astype(
        jnp.int32
    )
    before = jnp.cumsum(onehot, axis=0) - onehot
    slot_rank = jnp.sum(before * onehot, axis=1)
    outgoing = (
        jnp.zeros((owners, capacity, 3, columns), projected.dtype)
        .at[target_owner, slot_rank]
        .set(projected)
    )
    slots = (
        jnp.full((owners, capacity), -1, jnp.int32)
        .at[target_owner, slot_rank]
        .set(destination % tok_dev)
    )
    incoming, landing = (
        lax.all_to_all(outgoing, "seq", split_axis=0, concat_axis=0, tiled=True),
        lax.all_to_all(slots, "seq", split_axis=0, concat_axis=0, tiled=True),
    )
    landing = landing.reshape(-1)
    landing = jnp.where(landing >= 0, landing, tok_dev)
    routed = (
        jnp.zeros((tok_dev, 3, columns), projected.dtype)
        .at[landing]
        .set(incoming.reshape(owners * capacity, 3, columns), mode="drop")
    )
    keyval = routed[:, 1:, :]
    fetched = {0: keyval}
    offsets = list(range(-RDEV, 0)) + list(range(1, RDEV + 1))
    for offset in offsets:
        fetched[offset] = from_behind(keyval, "seq", -offset)
    band_blocks = jnp.stack([fetched[offset] for offset in range(-RDEV, RDEV + 1)])
    block_ids = own_index * per_dev + jnp.arange(per_dev, dtype=jnp.int32)
    local_pick = jnp.arange(per_dev, dtype=jnp.int32) + RDEV * per_dev
    window_pick = local_pick[:, None] + jnp.arange(-1, 2, dtype=jnp.int32)[None, :]
    chosen_rand = lax.dynamic_slice_in_dim(random_blocks, own_index * per_dev, per_dev, 0)
    away_dev = (chosen_rand // per_dev - own_index) % owners
    away_dev = jnp.where(away_dev > owners // 2, away_dev - owners, away_dev)
    rand_pick = (away_dev + RDEV) * per_dev + chosen_rand % per_dev
    block_picks = jnp.concatenate([window_pick, rand_pick], axis=1)
    gathered = jnp.take(band_blocks, block_picks, axis=0)
    near_keys = gathered[:, :, :, 0, :].reshape(per_dev, (3 + R) * BLK, heads_here, HD)
    near_values = gathered[:, :, :, 1, :].reshape(per_dev, (3 + R) * BLK, heads_here, HD)
    owner_dev = global_owner[0]
    global_rows = from_root(routed, "seq", owner_dev)
    glob_keys = global_rows[:, 1, :].reshape(tok_dev, heads_here, HD)
    glob_values = global_rows[:, 2, :].reshape(tok_dev, heads_here, HD)
    queries = routed[:, 0, :].reshape(per_dev, BLK, heads_here, HD)
    near_scores = (
        jnp.einsum("bqhd,bkhd->bhqk", queries, near_keys, preferred_element_type=jnp.float32)
        * score_scale
    )
    far_scores = (
        jnp.einsum("bqhd,khd->bhqk", queries, glob_keys, preferred_element_type=jnp.float32)
        * score_scale
    )
    bounds = jnp.cumsum(doc_lengths)
    query_pos = own_index * tok_dev + jnp.arange(tok_dev, dtype=jnp.int32)
    query_doc = segment_of(query_pos, bounds).reshape(per_dev, BLK)
    window_blocks = (block_ids[:, None] + jnp.arange(-1, 2, dtype=jnp.int32)[None, :]) % blocks_all
    key_pos = (
        window_blocks[:, :, None] * BLK + jnp.arange(BLK, dtype=jnp.int32)[None, None, :]
    ).reshape(-1)
    key_doc = segment_of(key_pos, bounds).reshape(per_dev, 3 * BLK)
    same_doc = query_doc[:, :, None] == key_doc[:, None, :]
    allowed = jnp.concatenate(
        [same_doc, jnp.ones((per_dev, BLK, R * BLK), dtype=jnp.bool_)], axis=2
    )
    near_scores = jnp.where(allowed[:, None], near_scores, big_negative)
    row_peak = jnp.maximum(jnp.max(near_scores, axis=3), jnp.max(far_scores, axis=3))
    near_exp = jnp.exp(near_scores - row_peak[..., None])
    far_exp = jnp.exp(far_scores - row_peak[..., None])
    denominator = jnp.sum(near_exp, axis=3) + jnp.sum(far_exp, axis=3)
    mixed_sum = jnp.einsum(
        "bhqk,bkhd->bqhd",
        near_exp.astype(jnp.bfloat16),
        near_values,
        preferred_element_type=jnp.float32,
    )
    mixed_sum = mixed_sum + jnp.einsum(
        "bhqk,khd->bqhd",
        far_exp.astype(jnp.bfloat16),
        glob_values,
        preferred_element_type=jnp.float32,
    )
    sparse = (mixed_sum / jnp.transpose(denominator, (0, 2, 1))[..., None]).reshape(
        tok_dev, columns
    )
    sparse = sparse.astype(jnp.bfloat16)
    glob_queries = global_rows[:, 0, :].reshape(tok_dev, heads_here, HD)
    local_keys = routed[:, 1, :].reshape(tok_dev, heads_here, HD)
    local_values = routed[:, 2, :].reshape(tok_dev, heads_here, HD).astype(jnp.float32)
    all_scores = (
        jnp.einsum("qhd,khd->hqk", glob_queries, local_keys, preferred_element_type=jnp.float32)
        * score_scale
    )
    local_peak = jnp.max(all_scores, axis=2)
    weights = jnp.exp(all_scores - local_peak[..., None])
    part_total = jnp.sum(weights, axis=2)
    part_accum = jnp.einsum("hqk,khd->hqd", weights, local_values, precision=lax.Precision.HIGHEST)
    peak_all, total_all, accum_all = combined_all(
        (local_peak, part_total, part_accum), "seq", combine_parts
    )
    glob_out = jnp.transpose(accum_all / total_all[..., None], (1, 0, 2)).reshape(tok_dev, columns)
    glob_out = glob_out.astype(jnp.bfloat16)
    attn_rows = jnp.where(own_index == owner_dev, glob_out, sparse)
    return lax.psum_scatter(
        jnp.dot(attn_rows, out_weight, preferred_element_type=jnp.float32).astype(jnp.bfloat16),
        "head",
        scatter_dimension=0,
        tiled=True,
    )


def ring_gather(block, own_index, owners, rider):
    if owners % 2:
        ring = list(range(owners))
    else:
        half = owners // 2
        ring = [2 * i for i in range(half)] + [2 * i + 1 for i in reversed(range(half))]
    place = [0] * owners
    for i, s in enumerate(ring):
        place[s] = i
    right = [(ring[i], ring[(i + 1) % owners]) for i in range(owners)]
    left = [(ring[i], ring[(i - 1) % owners]) for i in range(owners)]
    pieces = {0: block}
    moving_right = block
    moving_left = block
    for step in range(1, owners // 2 + 1):
        moving_right = jax.tree.map(lambda x: lax.ppermute(x, "seq", right), moving_right)
        pieces[-step] = moving_right
        if step <= (owners - 1) // 2:
            moving_left = jax.tree.map(lambda x: lax.ppermute(x, "seq", left), moving_left)
            if step == 1:
                moving_right, moving_left, rider = lax.optimization_barrier(
                    (moving_right, moving_left, rider)
                )
            else:
                moving_right, moving_left = lax.optimization_barrier((moving_right, moving_left))
            pieces[step] = moving_left
        pieces[-step] = moving_right
    offsets = sorted(pieces)
    stacked = jax.tree.map(
        lambda *parts: jnp.concatenate(parts, axis=0), *[pieces[k] for k in offsets]
    )
    where = jnp.asarray(place, jnp.int32)[own_index]
    order = jnp.asarray(ring, jnp.int32)[(where + jnp.asarray(offsets, jnp.int32)) % owners]
    return stacked, order, rider


def gathered_plan(projected, destination, doc_lengths, random_blocks, global_owner, out_weight):
    owners = lax.axis_size("seq")
    own_index = lax.axis_index("seq")
    tok_dev = projected.shape[0]
    columns = projected.shape[2]
    heads_here = columns // HD
    tokens = owners * tok_dev
    blocks_all = tokens // BLK
    score_scale = 1.0 / math.sqrt(HD)
    capacity = 2 * (tok_dev // owners)
    keyval, key_order, arrival = ring_gather(projected[:, 1:, :], own_index, owners, destination)
    key_dest = lax.all_gather(arrival, "seq", tiled=True).reshape(owners, tok_dev)[key_order]
    key_dest = key_dest.reshape(-1)
    arrival_dest = key_dest
    target_all = arrival_dest.reshape(owners, tok_dev) // tok_dev
    onehot = (target_all[:, :, None] == jnp.arange(owners, dtype=jnp.int32)).astype(jnp.int32)
    slot_all = jnp.sum((jnp.cumsum(onehot, axis=1) - onehot) * onehot, axis=2)
    target = destination // tok_dev
    mine = (target[:, None] == jnp.arange(owners, dtype=jnp.int32)[None, :]).astype(jnp.int32)
    slot = jnp.sum((jnp.cumsum(mine, axis=0) - mine) * mine, axis=1)
    send_col = target * capacity + slot
    send_pick = (
        jnp.arange(owners * capacity, dtype=jnp.int32)[:, None] == send_col[None, :]
    ).astype(projected.dtype)
    outgoing = jnp.dot(send_pick, projected[:, 0, :], preferred_element_type=jnp.float32)
    outgoing = outgoing.astype(projected.dtype).reshape(owners, capacity, columns)
    incoming = lax.all_to_all(outgoing, "seq", split_axis=0, concat_axis=0, tiled=True)
    my_pos = own_index * tok_dev + jnp.arange(tok_dev, dtype=jnp.int32)
    source = jnp.repeat(key_order, tok_dev)
    land_col = (source * capacity + slot_all.reshape(-1))[None, :]
    hit = arrival_dest[None, :] == my_pos[:, None]
    col_of_pos = jnp.sum(jnp.where(hit, land_col, 0), axis=1)
    land_pick = (
        col_of_pos[:, None] == jnp.arange(owners * capacity, dtype=jnp.int32)[None, :]
    ).astype(projected.dtype)
    queries = jnp.dot(
        land_pick, incoming.reshape(owners * capacity, columns), preferred_element_type=jnp.float32
    )
    queries = queries.astype(projected.dtype).reshape(tok_dev, heads_here, HD)
    keys = keyval[:, 0, :].reshape(tokens, heads_here, HD)
    values = keyval[:, 1, :].reshape(tokens, heads_here, HD)
    scores = (
        jnp.einsum("qhd,khd->hqk", queries, keys, preferred_element_type=jnp.float32)
        * score_scale
    )
    bounds = jnp.cumsum(doc_lengths)
    key_block = key_dest // BLK
    key_doc = segment_of(key_dest, bounds)
    query_block = my_pos // BLK
    query_doc = segment_of(my_pos, bounds)
    same_doc = query_doc[:, None] == key_doc[None, :]
    window = jnp.zeros((tok_dev, tokens), jnp.int32)
    for step in (-1, 0, 1):
        near = (query_block + step) % blocks_all
        window = window + (key_block[None, :] == near[:, None]).astype(jnp.int32)
    window = jnp.where(same_doc, window, 0)
    chosen = random_blocks[query_block]
    drawn = jnp.zeros((tok_dev, tokens), jnp.int32)
    for r in range(chosen.shape[1]):
        drawn = drawn + (key_block[None, :] == chosen[:, r][:, None]).astype(jnp.int32)
    glob_start = global_owner[0] * tok_dev
    in_glob = (key_dest >= glob_start) & (key_dest < glob_start + tok_dev)
    holds_glob = own_index == global_owner[0]
    count = window + drawn + in_glob[None, :].astype(jnp.int32)
    count = jnp.where(holds_glob, 1, count)
    live = count > 0
    near_scores = jnp.where(live[None], scores, big_negative)
    row_peak = jnp.max(near_scores, axis=2)
    near_exp = jnp.exp(near_scores - row_peak[..., None])
    count_f = count.astype(jnp.float32)[None]
    denominator = jnp.sum(near_exp * count_f, axis=2)
    rounded = jnp.where(holds_glob, near_exp, near_exp.astype(jnp.bfloat16).astype(jnp.float32))
    weighted = rounded * count_f
    weight_hi = weighted.astype(jnp.bfloat16)
    weight_lo = (weighted - weight_hi.astype(jnp.float32)).astype(jnp.bfloat16)
    mixed_sum = jnp.einsum("hqk,khd->qhd", weight_hi, values, preferred_element_type=jnp.float32)
    mixed_sum = mixed_sum + jnp.einsum(
        "hqk,khd->qhd", weight_lo, values, preferred_element_type=jnp.float32
    )
    attn_rows = (mixed_sum / jnp.transpose(denominator)[..., None]).reshape(tok_dev, columns)
    attn_rows = attn_rows.astype(jnp.bfloat16)
    projected_rows = jnp.dot(attn_rows, out_weight, preferred_element_type=jnp.float32)
    return head_sum(lax.optimization_barrier(projected_rows))


def head_sum(partial):
    members = lax.axis_size("head")
    if members & (members - 1):
        return lax.psum_scatter(
            partial.astype(jnp.bfloat16), "head", scatter_dimension=0, tiled=True
        )
    me = lax.axis_index("head")
    rows = partial.shape[0] // members
    partial = partial.reshape(members, rows, partial.shape[1])
    bit = 1
    while bit < members:
        pairs = partial.reshape(partial.shape[0] // 2, 2, rows, partial.shape[2])
        upper = (me & bit) != 0
        keep = jnp.where(upper, pairs[:, 1], pairs[:, 0])
        send = jnp.where(upper, pairs[:, 0], pairs[:, 1]).astype(jnp.bfloat16)
        got = lax.ppermute(send, "head", [(i, i ^ bit) for i in range(members)])
        partial = keep + got.astype(jnp.float32)
        bit *= 2
    partial = partial.reshape(rows, partial.shape[2])
    return partial.astype(jnp.bfloat16)


GATHER_LIMIT = 16 * 2**20


def shards(projected, destination, doc_lengths, random_blocks, global_owner, out_weight):
    gathered_bytes = lax.axis_size("seq") * projected.size * projected.dtype.itemsize
    if gathered_bytes <= GATHER_LIMIT:
        return gathered_plan(
            projected, destination, doc_lengths, random_blocks, global_owner, out_weight
        )
    return shards_ring(projected, destination, doc_lengths, random_blocks, global_owner, out_weight)


def solution(mesh):
    in_specs = (P("seq", None, "head"), P("seq"), P(), P(), P(), P("head", None))
    out_specs = P(("seq", "head"), None)
    return jax.shard_map(shards, mesh=mesh, in_specs=in_specs, out_specs=out_specs, check_vma=False)
```

```python
import math

import jax
import jax.numpy as jnp
from jax import lax
from jax.sharding import PartitionSpec as P

HD = 128
BLK = 128
R = 3
RDEV = 2


big_negative = -1e30


def from_behind(block, axis, distance):
    devices = range(lax.axis_size(axis))
    route = [((i - distance) % len(devices), i) for i in devices]
    return lax.ppermute(block, axis, route)


def from_root(x, axis, root):
    mine = lax.axis_index(axis) == root
    return lax.psum(jnp.where(mine, x, jnp.zeros_like(x)), axis)


def combined_all(x, axis, combine):
    everything = jax.tree.map(lambda part: lax.all_gather(part, axis), x)
    first = jax.tree.map(lambda part: part[0], everything)

    def step(k, so_far):
        return combine(so_far, jax.tree.map(lambda part: part[k], everything))

    return lax.fori_loop(1, lax.axis_size(axis), step, first)


def segment_of(positions, bounds):
    return jnp.sum((bounds[None, :] <= positions[:, None]).astype(jnp.int32), axis=1)


def combine_parts(left_part, right_part):
    top_left, total_left, accum_left = left_part
    top_right, total_right, accum_right = right_part
    row_peak = jnp.maximum(top_left, top_right)
    factor_left = jnp.exp(top_left - row_peak)
    factor_right = jnp.exp(top_right - row_peak)
    return (
        row_peak,
        total_left * factor_left + total_right * factor_right,
        accum_left * factor_left[:, :, None] + accum_right * factor_right[:, :, None],
    )


def shards_ring(projected, destination, doc_lengths, random_blocks, global_owner, out_weight):
    owners = lax.axis_size("seq")
    own_index = lax.axis_index("seq")
    tok_dev = projected.shape[0]
    columns = projected.shape[2]
    heads_here = columns // HD
    per_dev = tok_dev // BLK
    blocks_all = owners * per_dev
    capacity = 2 * (tok_dev // owners)
    score_scale = 1.0 / math.sqrt(HD)
    target_owner = destination // tok_dev
    onehot = (target_owner[:, None] == jnp.arange(owners, dtype=jnp.int32)[None, :]).astype(
        jnp.int32
    )
    before = jnp.cumsum(onehot, axis=0) - onehot
    slot_rank = jnp.sum(before * onehot, axis=1)
    outgoing = (
        jnp.zeros((owners, capacity, 3, columns), projected.dtype)
        .at[target_owner, slot_rank]
        .set(projected)
    )
    slots = (
        jnp.full((owners, capacity), -1, jnp.int32)
        .at[target_owner, slot_rank]
        .set(destination % tok_dev)
    )
    incoming, landing = (
        lax.all_to_all(outgoing, "seq", split_axis=0, concat_axis=0, tiled=True),
        lax.all_to_all(slots, "seq", split_axis=0, concat_axis=0, tiled=True),
    )
    landing = landing.reshape(-1)
    landing = jnp.where(landing >= 0, landing, tok_dev)
    routed = (
        jnp.zeros((tok_dev, 3, columns), projected.dtype)
        .at[landing]
        .set(incoming.reshape(owners * capacity, 3, columns), mode="drop")
    )
    keyval = routed[:, 1:, :]
    fetched = {0: keyval}
    offsets = list(range(-RDEV, 0)) + list(range(1, RDEV + 1))
    for offset in offsets:
        fetched[offset] = from_behind(keyval, "seq", -offset)
    band_blocks = jnp.stack([fetched[offset] for offset in range(-RDEV, RDEV + 1)])
    block_ids = own_index * per_dev + jnp.arange(per_dev, dtype=jnp.int32)
    local_pick = jnp.arange(per_dev, dtype=jnp.int32) + RDEV * per_dev
    window_pick = local_pick[:, None] + jnp.arange(-1, 2, dtype=jnp.int32)[None, :]
    chosen_rand = lax.dynamic_slice_in_dim(random_blocks, own_index * per_dev, per_dev, 0)
    away_dev = (chosen_rand // per_dev - own_index) % owners
    away_dev = jnp.where(away_dev > owners // 2, away_dev - owners, away_dev)
    rand_pick = (away_dev + RDEV) * per_dev + chosen_rand % per_dev
    block_picks = jnp.concatenate([window_pick, rand_pick], axis=1)
    gathered = jnp.take(band_blocks, block_picks, axis=0)
    near_keys = gathered[:, :, :, 0, :].reshape(per_dev, (3 + R) * BLK, heads_here, HD)
    near_values = gathered[:, :, :, 1, :].reshape(per_dev, (3 + R) * BLK, heads_here, HD)
    owner_dev = global_owner[0]
    global_rows = from_root(routed, "seq", owner_dev)
    glob_keys = global_rows[:, 1, :].reshape(tok_dev, heads_here, HD)
    glob_values = global_rows[:, 2, :].reshape(tok_dev, heads_here, HD)
    queries = routed[:, 0, :].reshape(per_dev, BLK, heads_here, HD)
    near_scores = (
        jnp.einsum("bqhd,bkhd->bhqk", queries, near_keys, preferred_element_type=jnp.float32)
        * score_scale
    )
    far_scores = (
        jnp.einsum("bqhd,khd->bhqk", queries, glob_keys, preferred_element_type=jnp.float32)
        * score_scale
    )
    bounds = jnp.cumsum(doc_lengths)
    query_pos = own_index * tok_dev + jnp.arange(tok_dev, dtype=jnp.int32)
    query_doc = segment_of(query_pos, bounds).reshape(per_dev, BLK)
    window_blocks = (block_ids[:, None] + jnp.arange(-1, 2, dtype=jnp.int32)[None, :]) % blocks_all
    key_pos = (
        window_blocks[:, :, None] * BLK + jnp.arange(BLK, dtype=jnp.int32)[None, None, :]
    ).reshape(-1)
    key_doc = segment_of(key_pos, bounds).reshape(per_dev, 3 * BLK)
    same_doc = query_doc[:, :, None] == key_doc[:, None, :]
    allowed = jnp.concatenate(
        [same_doc, jnp.ones((per_dev, BLK, R * BLK), dtype=jnp.bool_)], axis=2
    )
    near_scores = jnp.where(allowed[:, None], near_scores, big_negative)
    row_peak = jnp.maximum(jnp.max(near_scores, axis=3), jnp.max(far_scores, axis=3))
    near_exp = jnp.exp(near_scores - row_peak[..., None])
    far_exp = jnp.exp(far_scores - row_peak[..., None])
    denominator = jnp.sum(near_exp, axis=3) + jnp.sum(far_exp, axis=3)
    mixed_sum = jnp.einsum(
        "bhqk,bkhd->bqhd",
        near_exp.astype(jnp.bfloat16),
        near_values,
        preferred_element_type=jnp.float32,
    )
    mixed_sum = mixed_sum + jnp.einsum(
        "bhqk,khd->bqhd",
        far_exp.astype(jnp.bfloat16),
        glob_values,
        preferred_element_type=jnp.float32,
    )
    sparse = (mixed_sum / jnp.transpose(denominator, (0, 2, 1))[..., None]).reshape(
        tok_dev, columns
    )
    sparse = sparse.astype(jnp.bfloat16)
    glob_queries = global_rows[:, 0, :].reshape(tok_dev, heads_here, HD)
    local_keys = routed[:, 1, :].reshape(tok_dev, heads_here, HD)
    local_values = routed[:, 2, :].reshape(tok_dev, heads_here, HD).astype(jnp.float32)
    all_scores = (
        jnp.einsum("qhd,khd->hqk", glob_queries, local_keys, preferred_element_type=jnp.float32)
        * score_scale
    )
    local_peak = jnp.max(all_scores, axis=2)
    weights = jnp.exp(all_scores - local_peak[..., None])
    part_total = jnp.sum(weights, axis=2)
    part_accum = jnp.einsum("hqk,khd->hqd", weights, local_values, precision=lax.Precision.HIGHEST)
    peak_all, total_all, accum_all = combined_all(
        (local_peak, part_total, part_accum), "seq", combine_parts
    )
    glob_out = jnp.transpose(accum_all / total_all[..., None], (1, 0, 2)).reshape(tok_dev, columns)
    glob_out = glob_out.astype(jnp.bfloat16)
    attn_rows = jnp.where(own_index == owner_dev, glob_out, sparse)
    return lax.psum_scatter(
        jnp.dot(attn_rows, out_weight, preferred_element_type=jnp.float32).astype(jnp.bfloat16),
        "head",
        scatter_dimension=0,
        tiled=True,
    )


def ring_gather(block, own_index, owners, rider):
    if owners % 2:
        ring = list(range(owners))
    else:
        half = owners // 2
        ring = [2 * i for i in range(half)] + [2 * i + 1 for i in reversed(range(half))]
    place = [0] * owners
    for i, s in enumerate(ring):
        place[s] = i
    right = [(ring[i], ring[(i + 1) % owners]) for i in range(owners)]
    left = [(ring[i], ring[(i - 1) % owners]) for i in range(owners)]
    pieces = {0: block}
    moving_right = block
    moving_left = block
    for step in range(1, owners // 2 + 1):
        moving_right = jax.tree.map(lambda x: lax.ppermute(x, "seq", right), moving_right)
        pieces[-step] = moving_right
        if step <= (owners - 1) // 2:
            moving_left = jax.tree.map(lambda x: lax.ppermute(x, "seq", left), moving_left)
            if step == 1:
                moving_right, moving_left, first = lax.optimization_barrier(
                    (moving_right, moving_left, rider[0])
                )
                rider = (first, rider[1])
            elif step == owners // 2 - 1:
                moving_right, moving_left, second = lax.optimization_barrier(
                    (moving_right, moving_left, rider[1])
                )
                rider = (rider[0], second)
            else:
                moving_right, moving_left = lax.optimization_barrier((moving_right, moving_left))
            pieces[step] = moving_left
        pieces[-step] = moving_right
    offsets = sorted(pieces)
    stacked = jax.tree.map(
        lambda *parts: jnp.concatenate(parts, axis=0), *[pieces[k] for k in offsets]
    )
    where = jnp.asarray(place, jnp.int32)[own_index]
    order = jnp.asarray(ring, jnp.int32)[(where + jnp.asarray(offsets, jnp.int32)) % owners]
    return stacked, order, rider


def gathered_plan(projected, destination, doc_lengths, random_blocks, global_owner, out_weight):
    owners = lax.axis_size("seq")
    own_index = lax.axis_index("seq")
    tok_dev = projected.shape[0]
    columns = projected.shape[2]
    heads_here = columns // HD
    tokens = owners * tok_dev
    blocks_all = tokens // BLK
    score_scale = 1.0 / math.sqrt(HD)
    capacity = 2 * (tok_dev // owners)
    target = destination // tok_dev
    mine = (target[:, None] == jnp.arange(owners, dtype=jnp.int32)[None, :]).astype(jnp.int32)
    slot = jnp.sum((jnp.cumsum(mine, axis=0) - mine) * mine, axis=1)
    send_col = target * capacity + slot
    send_pick = (
        jnp.arange(owners * capacity, dtype=jnp.int32)[:, None] == send_col[None, :]
    ).astype(projected.dtype)
    outgoing = jnp.dot(send_pick, projected[:, 0, :], preferred_element_type=jnp.float32)
    outgoing = outgoing.astype(projected.dtype).reshape(owners, capacity, columns)
    keyval, key_order, (arrival, outgoing) = ring_gather(
        projected[:, 1:, :], own_index, owners, (destination, outgoing)
    )
    key_dest = lax.all_gather(arrival, "seq", tiled=True).reshape(owners, tok_dev)[key_order]
    key_dest = key_dest.reshape(-1)
    arrival_dest = key_dest
    target_all = arrival_dest.reshape(owners, tok_dev) // tok_dev
    onehot = (target_all[:, :, None] == jnp.arange(owners, dtype=jnp.int32)).astype(jnp.int32)
    slot_all = jnp.sum((jnp.cumsum(onehot, axis=1) - onehot) * onehot, axis=2)
    incoming = lax.all_to_all(outgoing, "seq", split_axis=0, concat_axis=0, tiled=True)
    my_pos = own_index * tok_dev + jnp.arange(tok_dev, dtype=jnp.int32)
    source = jnp.repeat(key_order, tok_dev)
    land_col = (source * capacity + slot_all.reshape(-1))[None, :]
    hit = arrival_dest[None, :] == my_pos[:, None]
    col_of_pos = jnp.sum(jnp.where(hit, land_col, 0), axis=1)
    land_pick = (
        col_of_pos[:, None] == jnp.arange(owners * capacity, dtype=jnp.int32)[None, :]
    ).astype(projected.dtype)
    queries = jnp.dot(
        land_pick, incoming.reshape(owners * capacity, columns), preferred_element_type=jnp.float32
    )
    queries = queries.astype(projected.dtype).reshape(tok_dev, heads_here, HD)
    keys = keyval[:, 0, :].reshape(tokens, heads_here, HD)
    values = keyval[:, 1, :].reshape(tokens, heads_here, HD)
    scores = (
        jnp.einsum("qhd,khd->hqk", queries, keys, preferred_element_type=jnp.float32)
        * score_scale
    )
    bounds = jnp.cumsum(doc_lengths)
    key_block = key_dest // BLK
    key_doc = segment_of(key_dest, bounds)
    query_block = my_pos // BLK
    query_doc = segment_of(my_pos, bounds)
    same_doc = query_doc[:, None] == key_doc[None, :]
    window = jnp.zeros((tok_dev, tokens), jnp.int32)
    for step in (-1, 0, 1):
        near = (query_block + step) % blocks_all
        window = window + (key_block[None, :] == near[:, None]).astype(jnp.int32)
    window = jnp.where(same_doc, window, 0)
    chosen = random_blocks[query_block]
    drawn = jnp.zeros((tok_dev, tokens), jnp.int32)
    for r in range(chosen.shape[1]):
        drawn = drawn + (key_block[None, :] == chosen[:, r][:, None]).astype(jnp.int32)
    glob_start = global_owner[0] * tok_dev
    in_glob = (key_dest >= glob_start) & (key_dest < glob_start + tok_dev)
    holds_glob = own_index == global_owner[0]
    count = window + drawn + in_glob[None, :].astype(jnp.int32)
    count = jnp.where(holds_glob, 1, count)
    live = count > 0
    near_scores = jnp.where(live[None], scores, big_negative)
    row_peak = jnp.max(near_scores, axis=2)
    near_exp = jnp.exp(near_scores - row_peak[..., None])
    count_f = count.astype(jnp.float32)[None]
    denominator = jnp.sum(near_exp * count_f, axis=2)
    rounded = jnp.where(holds_glob, near_exp, near_exp.astype(jnp.bfloat16).astype(jnp.float32))
    weighted = rounded * count_f
    weight_hi = weighted.astype(jnp.bfloat16)
    weight_lo = (weighted - weight_hi.astype(jnp.float32)).astype(jnp.bfloat16)
    mixed_sum = jnp.einsum("hqk,khd->qhd", weight_hi, values, preferred_element_type=jnp.float32)
    mixed_sum = mixed_sum + jnp.einsum(
        "hqk,khd->qhd", weight_lo, values, preferred_element_type=jnp.float32
    )
    attn_rows = (mixed_sum / jnp.transpose(denominator)[..., None]).reshape(tok_dev, columns)
    attn_rows = attn_rows.astype(jnp.bfloat16)
    projected_rows = jnp.dot(attn_rows, out_weight, preferred_element_type=jnp.float32)
    return head_sum(lax.optimization_barrier(projected_rows))


def head_sum(partial):
    members = lax.axis_size("head")
    if members & (members - 1):
        return lax.psum_scatter(
            partial.astype(jnp.bfloat16), "head", scatter_dimension=0, tiled=True
        )
    me = lax.axis_index("head")
    rows = partial.shape[0] // members
    partial = partial.reshape(members, rows, partial.shape[1])
    bit = 1
    while bit < members:
        pairs = partial.reshape(partial.shape[0] // 2, 2, rows, partial.shape[2])
        upper = (me & bit) != 0
        keep = jnp.where(upper, pairs[:, 1], pairs[:, 0])
        send = jnp.where(upper, pairs[:, 0], pairs[:, 1]).astype(jnp.bfloat16)
        got = lax.ppermute(send, "head", [(i, i ^ bit) for i in range(members)])
        partial = keep + got.astype(jnp.float32)
        bit *= 2
    partial = partial.reshape(rows, partial.shape[2])
    return partial.astype(jnp.bfloat16)


GATHER_LIMIT = 16 * 2**20


def shards(projected, destination, doc_lengths, random_blocks, global_owner, out_weight):
    gathered_bytes = lax.axis_size("seq") * projected.size * projected.dtype.itemsize
    if gathered_bytes <= GATHER_LIMIT:
        return gathered_plan(
            projected, destination, doc_lengths, random_blocks, global_owner, out_weight
        )
    return shards_ring(projected, destination, doc_lengths, random_blocks, global_owner, out_weight)


def solution(mesh):
    in_specs = (P("seq", None, "head"), P("seq"), P(), P(), P(), P("head", None))
    out_specs = P(("seq", "head"), None)
    return jax.shard_map(shards, mesh=mesh, in_specs=in_specs, out_specs=out_specs, check_vma=False)
```

```python
import math

import jax
import jax.numpy as jnp
from jax import lax
from jax.sharding import PartitionSpec as P

HD = 128
BLK = 128
R = 3
RDEV = 2


big_negative = -1e30


def from_behind(block, axis, distance):
    devices = range(lax.axis_size(axis))
    route = [((i - distance) % len(devices), i) for i in devices]
    return lax.ppermute(block, axis, route)


def from_root(x, axis, root):
    mine = lax.axis_index(axis) == root
    return lax.psum(jnp.where(mine, x, jnp.zeros_like(x)), axis)


def combined_all(x, axis, combine):
    everything = jax.tree.map(lambda part: lax.all_gather(part, axis), x)
    first = jax.tree.map(lambda part: part[0], everything)

    def step(k, so_far):
        return combine(so_far, jax.tree.map(lambda part: part[k], everything))

    return lax.fori_loop(1, lax.axis_size(axis), step, first)


def segment_of(positions, bounds):
    return jnp.sum((bounds[None, :] <= positions[:, None]).astype(jnp.int32), axis=1)


def combine_parts(left_part, right_part):
    top_left, total_left, accum_left = left_part
    top_right, total_right, accum_right = right_part
    row_peak = jnp.maximum(top_left, top_right)
    factor_left = jnp.exp(top_left - row_peak)
    factor_right = jnp.exp(top_right - row_peak)
    return (
        row_peak,
        total_left * factor_left + total_right * factor_right,
        accum_left * factor_left[:, :, None] + accum_right * factor_right[:, :, None],
    )


def shards_ring(projected, destination, doc_lengths, random_blocks, global_owner, out_weight):
    owners = lax.axis_size("seq")
    own_index = lax.axis_index("seq")
    tok_dev = projected.shape[0]
    columns = projected.shape[2]
    heads_here = columns // HD
    per_dev = tok_dev // BLK
    blocks_all = owners * per_dev
    capacity = 2 * (tok_dev // owners)
    score_scale = 1.0 / math.sqrt(HD)
    target_owner = destination // tok_dev
    onehot = (target_owner[:, None] == jnp.arange(owners, dtype=jnp.int32)[None, :]).astype(
        jnp.int32
    )
    before = jnp.cumsum(onehot, axis=0) - onehot
    slot_rank = jnp.sum(before * onehot, axis=1)
    outgoing = (
        jnp.zeros((owners, capacity, 3, columns), projected.dtype)
        .at[target_owner, slot_rank]
        .set(projected)
    )
    slots = (
        jnp.full((owners, capacity), -1, jnp.int32)
        .at[target_owner, slot_rank]
        .set(destination % tok_dev)
    )
    incoming, landing = (
        lax.all_to_all(outgoing, "seq", split_axis=0, concat_axis=0, tiled=True),
        lax.all_to_all(slots, "seq", split_axis=0, concat_axis=0, tiled=True),
    )
    landing = landing.reshape(-1)
    landing = jnp.where(landing >= 0, landing, tok_dev)
    routed = (
        jnp.zeros((tok_dev, 3, columns), projected.dtype)
        .at[landing]
        .set(incoming.reshape(owners * capacity, 3, columns), mode="drop")
    )
    keyval = routed[:, 1:, :]
    fetched = {0: keyval}
    offsets = list(range(-RDEV, 0)) + list(range(1, RDEV + 1))
    for offset in offsets:
        fetched[offset] = from_behind(keyval, "seq", -offset)
    band_blocks = jnp.stack([fetched[offset] for offset in range(-RDEV, RDEV + 1)])
    block_ids = own_index * per_dev + jnp.arange(per_dev, dtype=jnp.int32)
    local_pick = jnp.arange(per_dev, dtype=jnp.int32) + RDEV * per_dev
    window_pick = local_pick[:, None] + jnp.arange(-1, 2, dtype=jnp.int32)[None, :]
    chosen_rand = lax.dynamic_slice_in_dim(random_blocks, own_index * per_dev, per_dev, 0)
    away_dev = (chosen_rand // per_dev - own_index) % owners
    away_dev = jnp.where(away_dev > owners // 2, away_dev - owners, away_dev)
    rand_pick = (away_dev + RDEV) * per_dev + chosen_rand % per_dev
    block_picks = jnp.concatenate([window_pick, rand_pick], axis=1)
    gathered = jnp.take(band_blocks, block_picks, axis=0)
    near_keys = gathered[:, :, :, 0, :].reshape(per_dev, (3 + R) * BLK, heads_here, HD)
    near_values = gathered[:, :, :, 1, :].reshape(per_dev, (3 + R) * BLK, heads_here, HD)
    owner_dev = global_owner[0]
    global_rows = from_root(routed, "seq", owner_dev)
    glob_keys = global_rows[:, 1, :].reshape(tok_dev, heads_here, HD)
    glob_values = global_rows[:, 2, :].reshape(tok_dev, heads_here, HD)
    queries = routed[:, 0, :].reshape(per_dev, BLK, heads_here, HD)
    near_scores = (
        jnp.einsum("bqhd,bkhd->bhqk", queries, near_keys, preferred_element_type=jnp.float32)
        * score_scale
    )
    far_scores = (
        jnp.einsum("bqhd,khd->bhqk", queries, glob_keys, preferred_element_type=jnp.float32)
        * score_scale
    )
    bounds = jnp.cumsum(doc_lengths)
    query_pos = own_index * tok_dev + jnp.arange(tok_dev, dtype=jnp.int32)
    query_doc = segment_of(query_pos, bounds).reshape(per_dev, BLK)
    window_blocks = (block_ids[:, None] + jnp.arange(-1, 2, dtype=jnp.int32)[None, :]) % blocks_all
    key_pos = (
        window_blocks[:, :, None] * BLK + jnp.arange(BLK, dtype=jnp.int32)[None, None, :]
    ).reshape(-1)
    key_doc = segment_of(key_pos, bounds).reshape(per_dev, 3 * BLK)
    same_doc = query_doc[:, :, None] == key_doc[:, None, :]
    allowed = jnp.concatenate(
        [same_doc, jnp.ones((per_dev, BLK, R * BLK), dtype=jnp.bool_)], axis=2
    )
    near_scores = jnp.where(allowed[:, None], near_scores, big_negative)
    row_peak = jnp.maximum(jnp.max(near_scores, axis=3), jnp.max(far_scores, axis=3))
    near_exp = jnp.exp(near_scores - row_peak[..., None])
    far_exp = jnp.exp(far_scores - row_peak[..., None])
    denominator = jnp.sum(near_exp, axis=3) + jnp.sum(far_exp, axis=3)
    mixed_sum = jnp.einsum(
        "bhqk,bkhd->bqhd",
        near_exp.astype(jnp.bfloat16),
        near_values,
        preferred_element_type=jnp.float32,
    )
    mixed_sum = mixed_sum + jnp.einsum(
        "bhqk,khd->bqhd",
        far_exp.astype(jnp.bfloat16),
        glob_values,
        preferred_element_type=jnp.float32,
    )
    sparse = (mixed_sum / jnp.transpose(denominator, (0, 2, 1))[..., None]).reshape(
        tok_dev, columns
    )
    sparse = sparse.astype(jnp.bfloat16)
    glob_queries = global_rows[:, 0, :].reshape(tok_dev, heads_here, HD)
    local_keys = routed[:, 1, :].reshape(tok_dev, heads_here, HD)
    local_values = routed[:, 2, :].reshape(tok_dev, heads_here, HD).astype(jnp.float32)
    all_scores = (
        jnp.einsum("qhd,khd->hqk", glob_queries, local_keys, preferred_element_type=jnp.float32)
        * score_scale
    )
    local_peak = jnp.max(all_scores, axis=2)
    weights = jnp.exp(all_scores - local_peak[..., None])
    part_total = jnp.sum(weights, axis=2)
    part_accum = jnp.einsum("hqk,khd->hqd", weights, local_values, precision=lax.Precision.HIGHEST)
    peak_all, total_all, accum_all = combined_all(
        (local_peak, part_total, part_accum), "seq", combine_parts
    )
    glob_out = jnp.transpose(accum_all / total_all[..., None], (1, 0, 2)).reshape(tok_dev, columns)
    glob_out = glob_out.astype(jnp.bfloat16)
    attn_rows = jnp.where(own_index == owner_dev, glob_out, sparse)
    return lax.psum_scatter(
        jnp.dot(attn_rows, out_weight, preferred_element_type=jnp.float32).astype(jnp.bfloat16),
        "head",
        scatter_dimension=0,
        tiled=True,
    )


def ring_gather(block, own_index, owners, rider):
    if owners % 2:
        ring = list(range(owners))
    else:
        half = owners // 2
        ring = [2 * i for i in range(half)] + [2 * i + 1 for i in reversed(range(half))]
    place = [0] * owners
    for i, s in enumerate(ring):
        place[s] = i
    right = [(ring[i], ring[(i + 1) % owners]) for i in range(owners)]
    left = [(ring[i], ring[(i - 1) % owners]) for i in range(owners)]
    pieces = {0: block}
    moving_right = block
    moving_left = block
    for step in range(1, owners // 2 + 1):
        moving_right = jax.tree.map(lambda x: lax.ppermute(x, "seq", right), moving_right)
        pieces[-step] = moving_right
        if step <= (owners - 1) // 2:
            moving_left = jax.tree.map(lambda x: lax.ppermute(x, "seq", left), moving_left)
            if step == owners // 2 - 1:
                moving_right, moving_left, rider = lax.optimization_barrier(
                    (moving_right, moving_left, rider)
                )
            else:
                moving_right, moving_left = lax.optimization_barrier((moving_right, moving_left))
            pieces[step] = moving_left
        pieces[-step] = moving_right
    offsets = sorted(pieces)
    stacked = jax.tree.map(
        lambda *parts: jnp.concatenate(parts, axis=0), *[pieces[k] for k in offsets]
    )
    where = jnp.asarray(place, jnp.int32)[own_index]
    order = jnp.asarray(ring, jnp.int32)[(where + jnp.asarray(offsets, jnp.int32)) % owners]
    return stacked, order, rider


def gathered_plan(projected, destination, doc_lengths, random_blocks, global_owner, out_weight):
    owners = lax.axis_size("seq")
    own_index = lax.axis_index("seq")
    tok_dev = projected.shape[0]
    columns = projected.shape[2]
    heads_here = columns // HD
    tokens = owners * tok_dev
    blocks_all = tokens // BLK
    score_scale = 1.0 / math.sqrt(HD)
    capacity = 2 * (tok_dev // owners)
    lanes = jnp.arange(128, dtype=jnp.int32)[None, :]
    dest_hi = jnp.where(lanes == 0, (destination // 32)[:, None], 0)
    dest_lo = jnp.where(lanes == 0, (destination % 32)[:, None], 0)
    tag = jnp.stack([dest_hi, dest_lo], axis=1).astype(projected.dtype)
    message = jnp.concatenate([projected[:, 1:, :], tag], axis=2)
    target = destination // tok_dev
    mine = (target[:, None] == jnp.arange(owners, dtype=jnp.int32)[None, :]).astype(jnp.int32)
    slot = jnp.sum((jnp.cumsum(mine, axis=0) - mine) * mine, axis=1)
    send_col = target * capacity + slot
    send_pick = (
        jnp.arange(owners * capacity, dtype=jnp.int32)[:, None] == send_col[None, :]
    ).astype(projected.dtype)
    outgoing = jnp.dot(send_pick, projected[:, 0, :], preferred_element_type=jnp.float32)
    outgoing = outgoing.astype(projected.dtype).reshape(owners, capacity, columns)
    stacked, key_order, outgoing = ring_gather(message, own_index, owners, outgoing)
    key_dest = stacked[:, 0, columns].astype(jnp.int32) * 32 + stacked[:, 1, columns].astype(
        jnp.int32
    )
    keyval = stacked[:, :, :columns]
    arrival_dest = key_dest
    target_all = arrival_dest.reshape(owners, tok_dev) // tok_dev
    onehot = (target_all[:, :, None] == jnp.arange(owners, dtype=jnp.int32)).astype(jnp.int32)
    slot_all = jnp.sum((jnp.cumsum(onehot, axis=1) - onehot) * onehot, axis=2)
    incoming = lax.all_to_all(outgoing, "seq", split_axis=0, concat_axis=0, tiled=True)
    my_pos = own_index * tok_dev + jnp.arange(tok_dev, dtype=jnp.int32)
    source = jnp.repeat(key_order, tok_dev)
    land_col = (source * capacity + slot_all.reshape(-1))[None, :]
    hit = arrival_dest[None, :] == my_pos[:, None]
    col_of_pos = jnp.sum(jnp.where(hit, land_col, 0), axis=1)
    land_pick = (
        col_of_pos[:, None] == jnp.arange(owners * capacity, dtype=jnp.int32)[None, :]
    ).astype(projected.dtype)
    queries = jnp.dot(
        land_pick, incoming.reshape(owners * capacity, columns), preferred_element_type=jnp.float32
    )
    queries = queries.astype(projected.dtype).reshape(tok_dev, heads_here, HD)
    keys = keyval[:, 0, :].reshape(tokens, heads_here, HD)
    values = keyval[:, 1, :].reshape(tokens, heads_here, HD)
    scores = (
        jnp.einsum("qhd,khd->hqk", queries, keys, preferred_element_type=jnp.float32)
        * score_scale
    )
    bounds = jnp.cumsum(doc_lengths)
    key_block = key_dest // BLK
    key_doc = segment_of(key_dest, bounds)
    query_block = my_pos // BLK
    query_doc = segment_of(my_pos, bounds)
    same_doc = query_doc[:, None] == key_doc[None, :]
    window = jnp.zeros((tok_dev, tokens), jnp.int32)
    for step in (-1, 0, 1):
        near = (query_block + step) % blocks_all
        window = window + (key_block[None, :] == near[:, None]).astype(jnp.int32)
    window = jnp.where(same_doc, window, 0)
    chosen = random_blocks[query_block]
    drawn = jnp.zeros((tok_dev, tokens), jnp.int32)
    for r in range(chosen.shape[1]):
        drawn = drawn + (key_block[None, :] == chosen[:, r][:, None]).astype(jnp.int32)
    glob_start = global_owner[0] * tok_dev
    in_glob = (key_dest >= glob_start) & (key_dest < glob_start + tok_dev)
    holds_glob = own_index == global_owner[0]
    count = window + drawn + in_glob[None, :].astype(jnp.int32)
    count = jnp.where(holds_glob, 1, count)
    live = count > 0
    near_scores = jnp.where(live[None], scores, big_negative)
    row_peak = jnp.max(near_scores, axis=2)
    near_exp = jnp.exp(near_scores - row_peak[..., None])
    count_f = count.astype(jnp.float32)[None]
    denominator = jnp.sum(near_exp * count_f, axis=2)
    rounded = jnp.where(holds_glob, near_exp, near_exp.astype(jnp.bfloat16).astype(jnp.float32))
    weighted = rounded * count_f
    weight_hi = weighted.astype(jnp.bfloat16)
    weight_lo = (weighted - weight_hi.astype(jnp.float32)).astype(jnp.bfloat16)
    mixed_sum = jnp.einsum("hqk,khd->qhd", weight_hi, values, preferred_element_type=jnp.float32)
    mixed_sum = mixed_sum + jnp.einsum(
        "hqk,khd->qhd", weight_lo, values, preferred_element_type=jnp.float32
    )
    attn_rows = (mixed_sum / jnp.transpose(denominator)[..., None]).reshape(tok_dev, columns)
    attn_rows = attn_rows.astype(jnp.bfloat16)
    projected_rows = jnp.dot(attn_rows, out_weight, preferred_element_type=jnp.float32)
    return head_sum(lax.optimization_barrier(projected_rows))


def head_sum(partial):
    members = lax.axis_size("head")
    if members & (members - 1):
        return lax.psum_scatter(
            partial.astype(jnp.bfloat16), "head", scatter_dimension=0, tiled=True
        )
    me = lax.axis_index("head")
    rows = partial.shape[0] // members
    partial = partial.reshape(members, rows, partial.shape[1])
    bit = 1
    while bit < members:
        pairs = partial.reshape(partial.shape[0] // 2, 2, rows, partial.shape[2])
        upper = (me & bit) != 0
        keep = jnp.where(upper, pairs[:, 1], pairs[:, 0])
        send = jnp.where(upper, pairs[:, 0], pairs[:, 1]).astype(jnp.bfloat16)
        got = lax.ppermute(send, "head", [(i, i ^ bit) for i in range(members)])
        partial = keep + got.astype(jnp.float32)
        bit *= 2
    partial = partial.reshape(rows, partial.shape[2])
    return partial.astype(jnp.bfloat16)


GATHER_LIMIT = 16 * 2**20


def shards(projected, destination, doc_lengths, random_blocks, global_owner, out_weight):
    gathered_bytes = lax.axis_size("seq") * projected.size * projected.dtype.itemsize
    if gathered_bytes <= GATHER_LIMIT:
        return gathered_plan(
            projected, destination, doc_lengths, random_blocks, global_owner, out_weight
        )
    return shards_ring(projected, destination, doc_lengths, random_blocks, global_owner, out_weight)


def solution(mesh):
    in_specs = (P("seq", None, "head"), P("seq"), P(), P(), P(), P("head", None))
    out_specs = P(("seq", "head"), None)
    return jax.shard_map(shards, mesh=mesh, in_specs=in_specs, out_specs=out_specs, check_vma=False)
```

```python
import math

import jax
import jax.numpy as jnp
from jax import lax
from jax.sharding import PartitionSpec as P

HD = 128
BLK = 128
R = 3
RDEV = 2


big_negative = -1e30


def from_behind(block, axis, distance):
    devices = range(lax.axis_size(axis))
    route = [((i - distance) % len(devices), i) for i in devices]
    return lax.ppermute(block, axis, route)


def from_root(x, axis, root):
    mine = lax.axis_index(axis) == root
    return lax.psum(jnp.where(mine, x, jnp.zeros_like(x)), axis)


def combined_all(x, axis, combine):
    everything = jax.tree.map(lambda part: lax.all_gather(part, axis), x)
    first = jax.tree.map(lambda part: part[0], everything)

    def step(k, so_far):
        return combine(so_far, jax.tree.map(lambda part: part[k], everything))

    return lax.fori_loop(1, lax.axis_size(axis), step, first)


def segment_of(positions, bounds):
    return jnp.sum((bounds[None, :] <= positions[:, None]).astype(jnp.int32), axis=1)


def combine_parts(left_part, right_part):
    top_left, total_left, accum_left = left_part
    top_right, total_right, accum_right = right_part
    row_peak = jnp.maximum(top_left, top_right)
    factor_left = jnp.exp(top_left - row_peak)
    factor_right = jnp.exp(top_right - row_peak)
    return (
        row_peak,
        total_left * factor_left + total_right * factor_right,
        accum_left * factor_left[:, :, None] + accum_right * factor_right[:, :, None],
    )


def shards_ring(projected, destination, doc_lengths, random_blocks, global_owner, out_weight):
    owners = lax.axis_size("seq")
    own_index = lax.axis_index("seq")
    tok_dev = projected.shape[0]
    columns = projected.shape[2]
    heads_here = columns // HD
    per_dev = tok_dev // BLK
    blocks_all = owners * per_dev
    capacity = 2 * (tok_dev // owners)
    score_scale = 1.0 / math.sqrt(HD)
    target_owner = destination // tok_dev
    onehot = (target_owner[:, None] == jnp.arange(owners, dtype=jnp.int32)[None, :]).astype(
        jnp.int32
    )
    before = jnp.cumsum(onehot, axis=0) - onehot
    slot_rank = jnp.sum(before * onehot, axis=1)
    outgoing = (
        jnp.zeros((owners, capacity, 3, columns), projected.dtype)
        .at[target_owner, slot_rank]
        .set(projected)
    )
    slots = (
        jnp.full((owners, capacity), -1, jnp.int32)
        .at[target_owner, slot_rank]
        .set(destination % tok_dev)
    )
    incoming, landing = (
        lax.all_to_all(outgoing, "seq", split_axis=0, concat_axis=0, tiled=True),
        lax.all_to_all(slots, "seq", split_axis=0, concat_axis=0, tiled=True),
    )
    landing = landing.reshape(-1)
    landing = jnp.where(landing >= 0, landing, tok_dev)
    routed = (
        jnp.zeros((tok_dev, 3, columns), projected.dtype)
        .at[landing]
        .set(incoming.reshape(owners * capacity, 3, columns), mode="drop")
    )
    keyval = routed[:, 1:, :]
    fetched = {0: keyval}
    offsets = list(range(-RDEV, 0)) + list(range(1, RDEV + 1))
    for offset in offsets:
        fetched[offset] = from_behind(keyval, "seq", -offset)
    band_blocks = jnp.stack([fetched[offset] for offset in range(-RDEV, RDEV + 1)])
    block_ids = own_index * per_dev + jnp.arange(per_dev, dtype=jnp.int32)
    local_pick = jnp.arange(per_dev, dtype=jnp.int32) + RDEV * per_dev
    window_pick = local_pick[:, None] + jnp.arange(-1, 2, dtype=jnp.int32)[None, :]
    chosen_rand = lax.dynamic_slice_in_dim(random_blocks, own_index * per_dev, per_dev, 0)
    away_dev = (chosen_rand // per_dev - own_index) % owners
    away_dev = jnp.where(away_dev > owners // 2, away_dev - owners, away_dev)
    rand_pick = (away_dev + RDEV) * per_dev + chosen_rand % per_dev
    block_picks = jnp.concatenate([window_pick, rand_pick], axis=1)
    gathered = jnp.take(band_blocks, block_picks, axis=0)
    near_keys = gathered[:, :, :, 0, :].reshape(per_dev, (3 + R) * BLK, heads_here, HD)
    near_values = gathered[:, :, :, 1, :].reshape(per_dev, (3 + R) * BLK, heads_here, HD)
    owner_dev = global_owner[0]
    global_rows = from_root(routed, "seq", owner_dev)
    glob_keys = global_rows[:, 1, :].reshape(tok_dev, heads_here, HD)
    glob_values = global_rows[:, 2, :].reshape(tok_dev, heads_here, HD)
    queries = routed[:, 0, :].reshape(per_dev, BLK, heads_here, HD)
    near_scores = (
        jnp.einsum("bqhd,bkhd->bhqk", queries, near_keys, preferred_element_type=jnp.float32)
        * score_scale
    )
    far_scores = (
        jnp.einsum("bqhd,khd->bhqk", queries, glob_keys, preferred_element_type=jnp.float32)
        * score_scale
    )
    bounds = jnp.cumsum(doc_lengths)
    query_pos = own_index * tok_dev + jnp.arange(tok_dev, dtype=jnp.int32)
    query_doc = segment_of(query_pos, bounds).reshape(per_dev, BLK)
    window_blocks = (block_ids[:, None] + jnp.arange(-1, 2, dtype=jnp.int32)[None, :]) % blocks_all
    key_pos = (
        window_blocks[:, :, None] * BLK + jnp.arange(BLK, dtype=jnp.int32)[None, None, :]
    ).reshape(-1)
    key_doc = segment_of(key_pos, bounds).reshape(per_dev, 3 * BLK)
    same_doc = query_doc[:, :, None] == key_doc[:, None, :]
    allowed = jnp.concatenate(
        [same_doc, jnp.ones((per_dev, BLK, R * BLK), dtype=jnp.bool_)], axis=2
    )
    near_scores = jnp.where(allowed[:, None], near_scores, big_negative)
    row_peak = jnp.maximum(jnp.max(near_scores, axis=3), jnp.max(far_scores, axis=3))
    near_exp = jnp.exp(near_scores - row_peak[..., None])
    far_exp = jnp.exp(far_scores - row_peak[..., None])
    denominator = jnp.sum(near_exp, axis=3) + jnp.sum(far_exp, axis=3)
    mixed_sum = jnp.einsum(
        "bhqk,bkhd->bqhd",
        near_exp.astype(jnp.bfloat16),
        near_values,
        preferred_element_type=jnp.float32,
    )
    mixed_sum = mixed_sum + jnp.einsum(
        "bhqk,khd->bqhd",
        far_exp.astype(jnp.bfloat16),
        glob_values,
        preferred_element_type=jnp.float32,
    )
    sparse = (mixed_sum / jnp.transpose(denominator, (0, 2, 1))[..., None]).reshape(
        tok_dev, columns
    )
    sparse = sparse.astype(jnp.bfloat16)
    glob_queries = global_rows[:, 0, :].reshape(tok_dev, heads_here, HD)
    local_keys = routed[:, 1, :].reshape(tok_dev, heads_here, HD)
    local_values = routed[:, 2, :].reshape(tok_dev, heads_here, HD).astype(jnp.float32)
    all_scores = (
        jnp.einsum("qhd,khd->hqk", glob_queries, local_keys, preferred_element_type=jnp.float32)
        * score_scale
    )
    local_peak = jnp.max(all_scores, axis=2)
    weights = jnp.exp(all_scores - local_peak[..., None])
    part_total = jnp.sum(weights, axis=2)
    part_accum = jnp.einsum("hqk,khd->hqd", weights, local_values, precision=lax.Precision.HIGHEST)
    peak_all, total_all, accum_all = combined_all(
        (local_peak, part_total, part_accum), "seq", combine_parts
    )
    glob_out = jnp.transpose(accum_all / total_all[..., None], (1, 0, 2)).reshape(tok_dev, columns)
    glob_out = glob_out.astype(jnp.bfloat16)
    attn_rows = jnp.where(own_index == owner_dev, glob_out, sparse)
    return lax.psum_scatter(
        jnp.dot(attn_rows, out_weight, preferred_element_type=jnp.float32).astype(jnp.bfloat16),
        "head",
        scatter_dimension=0,
        tiled=True,
    )


def ring_gather(block, own_index, owners, rider=None):
    if owners % 2:
        ring = list(range(owners))
    else:
        half = owners // 2
        ring = [2 * i for i in range(half)] + [2 * i + 1 for i in reversed(range(half))]
    place = [0] * owners
    for i, s in enumerate(ring):
        place[s] = i
    right = [(ring[i], ring[(i + 1) % owners]) for i in range(owners)]
    left = [(ring[i], ring[(i - 1) % owners]) for i in range(owners)]
    pieces = {0: block}
    moving_right = block
    moving_left = block
    for step in range(1, owners // 2 + 1):
        moving_right = jax.tree.map(lambda x: lax.ppermute(x, "seq", right), moving_right)
        pieces[-step] = moving_right
        if step <= (owners - 1) // 2:
            moving_left = jax.tree.map(lambda x: lax.ppermute(x, "seq", left), moving_left)
            if step == 1 and rider is not None:
                moving_right, moving_left, rider = lax.optimization_barrier(
                    (moving_right, moving_left, rider)
                )
            else:
                moving_right, moving_left = lax.optimization_barrier((moving_right, moving_left))
            pieces[step] = moving_left
        pieces[-step] = moving_right
    offsets = sorted(pieces)
    stacked = jax.tree.map(
        lambda *parts: jnp.concatenate(parts, axis=0), *[pieces[k] for k in offsets]
    )
    where = jnp.asarray(place, jnp.int32)[own_index]
    order = jnp.asarray(ring, jnp.int32)[(where + jnp.asarray(offsets, jnp.int32)) % owners]
    return stacked, order, rider


def gathered_plan(projected, destination, doc_lengths, random_blocks, global_owner, out_weight):
    owners = lax.axis_size("seq")
    own_index = lax.axis_index("seq")
    tok_dev = projected.shape[0]
    columns = projected.shape[2]
    heads_here = columns // HD
    tokens = owners * tok_dev
    blocks_all = tokens // BLK
    score_scale = 1.0 / math.sqrt(HD)
    capacity = 2 * (tok_dev // owners)
    dest_ring, key_order, _ = ring_gather(destination, own_index, owners)
    keyval, _, key_dest = ring_gather(projected[:, 1:, :], own_index, owners, dest_ring)
    arrival_dest = key_dest
    target_all = arrival_dest.reshape(owners, tok_dev) // tok_dev
    onehot = (target_all[:, :, None] == jnp.arange(owners, dtype=jnp.int32)).astype(jnp.int32)
    slot_all = jnp.sum((jnp.cumsum(onehot, axis=1) - onehot) * onehot, axis=2)
    target = destination // tok_dev
    mine = (target[:, None] == jnp.arange(owners, dtype=jnp.int32)[None, :]).astype(jnp.int32)
    slot = jnp.sum((jnp.cumsum(mine, axis=0) - mine) * mine, axis=1)
    send_col = target * capacity + slot
    send_pick = (
        jnp.arange(owners * capacity, dtype=jnp.int32)[:, None] == send_col[None, :]
    ).astype(projected.dtype)
    outgoing = jnp.dot(send_pick, projected[:, 0, :], preferred_element_type=jnp.float32)
    outgoing = outgoing.astype(projected.dtype).reshape(owners, capacity, columns)
    incoming = lax.all_to_all(outgoing, "seq", split_axis=0, concat_axis=0, tiled=True)
    my_pos = own_index * tok_dev + jnp.arange(tok_dev, dtype=jnp.int32)
    source = jnp.repeat(key_order, tok_dev)
    land_col = (source * capacity + slot_all.reshape(-1))[None, :]
    hit = arrival_dest[None, :] == my_pos[:, None]
    col_of_pos = jnp.sum(jnp.where(hit, land_col, 0), axis=1)
    land_pick = (
        col_of_pos[:, None] == jnp.arange(owners * capacity, dtype=jnp.int32)[None, :]
    ).astype(projected.dtype)
    queries = jnp.dot(
        land_pick, incoming.reshape(owners * capacity, columns), preferred_element_type=jnp.float32
    )
    queries = queries.astype(projected.dtype).reshape(tok_dev, heads_here, HD)
    keys = keyval[:, 0, :].reshape(tokens, heads_here, HD)
    values = keyval[:, 1, :].reshape(tokens, heads_here, HD)
    scores = (
        jnp.einsum("qhd,khd->hqk", queries, keys, preferred_element_type=jnp.float32)
        * score_scale
    )
    bounds = jnp.cumsum(doc_lengths)
    key_block = key_dest // BLK
    key_doc = segment_of(key_dest, bounds)
    query_block = my_pos // BLK
    query_doc = segment_of(my_pos, bounds)
    same_doc = query_doc[:, None] == key_doc[None, :]
    window = jnp.zeros((tok_dev, tokens), jnp.int32)
    for step in (-1, 0, 1):
        near = (query_block + step) % blocks_all
        window = window + (key_block[None, :] == near[:, None]).astype(jnp.int32)
    window = jnp.where(same_doc, window, 0)
    chosen = random_blocks[query_block]
    drawn = jnp.zeros((tok_dev, tokens), jnp.int32)
    for r in range(chosen.shape[1]):
        drawn = drawn + (key_block[None, :] == chosen[:, r][:, None]).astype(jnp.int32)
    glob_start = global_owner[0] * tok_dev
    in_glob = (key_dest >= glob_start) & (key_dest < glob_start + tok_dev)
    holds_glob = own_index == global_owner[0]
    count = window + drawn + in_glob[None, :].astype(jnp.int32)
    count = jnp.where(holds_glob, 1, count)
    live = count > 0
    near_scores = jnp.where(live[None], scores, big_negative)
    row_peak = jnp.max(near_scores, axis=2)
    near_exp = jnp.exp(near_scores - row_peak[..., None])
    count_f = count.astype(jnp.float32)[None]
    denominator = jnp.sum(near_exp * count_f, axis=2)
    rounded = jnp.where(holds_glob, near_exp, near_exp.astype(jnp.bfloat16).astype(jnp.float32))
    weighted = rounded * count_f
    weight_hi = weighted.astype(jnp.bfloat16)
    weight_lo = (weighted - weight_hi.astype(jnp.float32)).astype(jnp.bfloat16)
    mixed_sum = jnp.einsum("hqk,khd->qhd", weight_hi, values, preferred_element_type=jnp.float32)
    mixed_sum = mixed_sum + jnp.einsum(
        "hqk,khd->qhd", weight_lo, values, preferred_element_type=jnp.float32
    )
    attn_rows = (mixed_sum / jnp.transpose(denominator)[..., None]).reshape(tok_dev, columns)
    attn_rows = attn_rows.astype(jnp.bfloat16)
    projected_rows = jnp.dot(attn_rows, out_weight, preferred_element_type=jnp.float32)
    return head_sum(lax.optimization_barrier(projected_rows))


def head_sum(partial):
    members = lax.axis_size("head")
    if members & (members - 1):
        return lax.psum_scatter(
            partial.astype(jnp.bfloat16), "head", scatter_dimension=0, tiled=True
        )
    me = lax.axis_index("head")
    rows = partial.shape[0] // members
    partial = partial.reshape(members, rows, partial.shape[1])
    bit = 1
    while bit < members:
        pairs = partial.reshape(partial.shape[0] // 2, 2, rows, partial.shape[2])
        upper = (me & bit) != 0
        keep = jnp.where(upper, pairs[:, 1], pairs[:, 0])
        send = jnp.where(upper, pairs[:, 0], pairs[:, 1]).astype(jnp.bfloat16)
        got = lax.ppermute(send, "head", [(i, i ^ bit) for i in range(members)])
        partial = keep + got.astype(jnp.float32)
        bit *= 2
    partial = partial.reshape(rows, partial.shape[2])
    return partial.astype(jnp.bfloat16)


GATHER_LIMIT = 16 * 2**20


def shards(projected, destination, doc_lengths, random_blocks, global_owner, out_weight):
    gathered_bytes = lax.axis_size("seq") * projected.size * projected.dtype.itemsize
    if gathered_bytes <= GATHER_LIMIT:
        return gathered_plan(
            projected, destination, doc_lengths, random_blocks, global_owner, out_weight
        )
    return shards_ring(projected, destination, doc_lengths, random_blocks, global_owner, out_weight)


def solution(mesh):
    in_specs = (P("seq", None, "head"), P("seq"), P(), P(), P(), P("head", None))
    out_specs = P(("seq", "head"), None)
    return jax.shard_map(shards, mesh=mesh, in_specs=in_specs, out_specs=out_specs, check_vma=False)
```

```python
import math

import jax
import jax.numpy as jnp
from jax import lax
from jax.sharding import PartitionSpec as P

HD = 128
BLK = 128
R = 3
RDEV = 2


big_negative = -1e30


def from_behind(block, axis, distance):
    devices = range(lax.axis_size(axis))
    route = [((i - distance) % len(devices), i) for i in devices]
    return lax.ppermute(block, axis, route)


def from_root(x, axis, root):
    mine = lax.axis_index(axis) == root
    return lax.psum(jnp.where(mine, x, jnp.zeros_like(x)), axis)


def combined_all(x, axis, combine):
    everything = jax.tree.map(lambda part: lax.all_gather(part, axis), x)
    first = jax.tree.map(lambda part: part[0], everything)

    def step(k, so_far):
        return combine(so_far, jax.tree.map(lambda part: part[k], everything))

    return lax.fori_loop(1, lax.axis_size(axis), step, first)


def segment_of(positions, bounds):
    return jnp.sum((bounds[None, :] <= positions[:, None]).astype(jnp.int32), axis=1)


def combine_parts(left_part, right_part):
    top_left, total_left, accum_left = left_part
    top_right, total_right, accum_right = right_part
    row_peak = jnp.maximum(top_left, top_right)
    factor_left = jnp.exp(top_left - row_peak)
    factor_right = jnp.exp(top_right - row_peak)
    return (
        row_peak,
        total_left * factor_left + total_right * factor_right,
        accum_left * factor_left[:, :, None] + accum_right * factor_right[:, :, None],
    )


def shards_ring(projected, destination, doc_lengths, random_blocks, global_owner, out_weight):
    owners = lax.axis_size("seq")
    own_index = lax.axis_index("seq")
    tok_dev = projected.shape[0]
    columns = projected.shape[2]
    heads_here = columns // HD
    per_dev = tok_dev // BLK
    blocks_all = owners * per_dev
    capacity = 2 * (tok_dev // owners)
    score_scale = 1.0 / math.sqrt(HD)
    target_owner = destination // tok_dev
    onehot = (target_owner[:, None] == jnp.arange(owners, dtype=jnp.int32)[None, :]).astype(
        jnp.int32
    )
    before = jnp.cumsum(onehot, axis=0) - onehot
    slot_rank = jnp.sum(before * onehot, axis=1)
    outgoing = (
        jnp.zeros((owners, capacity, 3, columns), projected.dtype)
        .at[target_owner, slot_rank]
        .set(projected)
    )
    slots = (
        jnp.full((owners, capacity), -1, jnp.int32)
        .at[target_owner, slot_rank]
        .set(destination % tok_dev)
    )
    incoming, landing = (
        lax.all_to_all(outgoing, "seq", split_axis=0, concat_axis=0, tiled=True),
        lax.all_to_all(slots, "seq", split_axis=0, concat_axis=0, tiled=True),
    )
    landing = landing.reshape(-1)
    landing = jnp.where(landing >= 0, landing, tok_dev)
    routed = (
        jnp.zeros((tok_dev, 3, columns), projected.dtype)
        .at[landing]
        .set(incoming.reshape(owners * capacity, 3, columns), mode="drop")
    )
    keyval = routed[:, 1:, :]
    fetched = {0: keyval}
    offsets = list(range(-RDEV, 0)) + list(range(1, RDEV + 1))
    for offset in offsets:
        fetched[offset] = from_behind(keyval, "seq", -offset)
    band_blocks = jnp.stack([fetched[offset] for offset in range(-RDEV, RDEV + 1)])
    block_ids = own_index * per_dev + jnp.arange(per_dev, dtype=jnp.int32)
    local_pick = jnp.arange(per_dev, dtype=jnp.int32) + RDEV * per_dev
    window_pick = local_pick[:, None] + jnp.arange(-1, 2, dtype=jnp.int32)[None, :]
    chosen_rand = lax.dynamic_slice_in_dim(random_blocks, own_index * per_dev, per_dev, 0)
    away_dev = (chosen_rand // per_dev - own_index) % owners
    away_dev = jnp.where(away_dev > owners // 2, away_dev - owners, away_dev)
    rand_pick = (away_dev + RDEV) * per_dev + chosen_rand % per_dev
    block_picks = jnp.concatenate([window_pick, rand_pick], axis=1)
    gathered = jnp.take(band_blocks, block_picks, axis=0)
    near_keys = gathered[:, :, :, 0, :].reshape(per_dev, (3 + R) * BLK, heads_here, HD)
    near_values = gathered[:, :, :, 1, :].reshape(per_dev, (3 + R) * BLK, heads_here, HD)
    owner_dev = global_owner[0]
    global_rows = from_root(routed, "seq", owner_dev)
    glob_keys = global_rows[:, 1, :].reshape(tok_dev, heads_here, HD)
    glob_values = global_rows[:, 2, :].reshape(tok_dev, heads_here, HD)
    queries = routed[:, 0, :].reshape(per_dev, BLK, heads_here, HD)
    near_scores = (
        jnp.einsum("bqhd,bkhd->bhqk", queries, near_keys, preferred_element_type=jnp.float32)
        * score_scale
    )
    far_scores = (
        jnp.einsum("bqhd,khd->bhqk", queries, glob_keys, preferred_element_type=jnp.float32)
        * score_scale
    )
    bounds = jnp.cumsum(doc_lengths)
    query_pos = own_index * tok_dev + jnp.arange(tok_dev, dtype=jnp.int32)
    query_doc = segment_of(query_pos, bounds).reshape(per_dev, BLK)
    window_blocks = (block_ids[:, None] + jnp.arange(-1, 2, dtype=jnp.int32)[None, :]) % blocks_all
    key_pos = (
        window_blocks[:, :, None] * BLK + jnp.arange(BLK, dtype=jnp.int32)[None, None, :]
    ).reshape(-1)
    key_doc = segment_of(key_pos, bounds).reshape(per_dev, 3 * BLK)
    same_doc = query_doc[:, :, None] == key_doc[:, None, :]
    allowed = jnp.concatenate(
        [same_doc, jnp.ones((per_dev, BLK, R * BLK), dtype=jnp.bool_)], axis=2
    )
    near_scores = jnp.where(allowed[:, None], near_scores, big_negative)
    row_peak = jnp.maximum(jnp.max(near_scores, axis=3), jnp.max(far_scores, axis=3))
    near_exp = jnp.exp(near_scores - row_peak[..., None])
    far_exp = jnp.exp(far_scores - row_peak[..., None])
    denominator = jnp.sum(near_exp, axis=3) + jnp.sum(far_exp, axis=3)
    mixed_sum = jnp.einsum(
        "bhqk,bkhd->bqhd",
        near_exp.astype(jnp.bfloat16),
        near_values,
        preferred_element_type=jnp.float32,
    )
    mixed_sum = mixed_sum + jnp.einsum(
        "bhqk,khd->bqhd",
        far_exp.astype(jnp.bfloat16),
        glob_values,
        preferred_element_type=jnp.float32,
    )
    sparse = (mixed_sum / jnp.transpose(denominator, (0, 2, 1))[..., None]).reshape(
        tok_dev, columns
    )
    sparse = sparse.astype(jnp.bfloat16)
    glob_queries = global_rows[:, 0, :].reshape(tok_dev, heads_here, HD)
    local_keys = routed[:, 1, :].reshape(tok_dev, heads_here, HD)
    local_values = routed[:, 2, :].reshape(tok_dev, heads_here, HD).astype(jnp.float32)
    all_scores = (
        jnp.einsum("qhd,khd->hqk", glob_queries, local_keys, preferred_element_type=jnp.float32)
        * score_scale
    )
    local_peak = jnp.max(all_scores, axis=2)
    weights = jnp.exp(all_scores - local_peak[..., None])
    part_total = jnp.sum(weights, axis=2)
    part_accum = jnp.einsum("hqk,khd->hqd", weights, local_values, precision=lax.Precision.HIGHEST)
    peak_all, total_all, accum_all = combined_all(
        (local_peak, part_total, part_accum), "seq", combine_parts
    )
    glob_out = jnp.transpose(accum_all / total_all[..., None], (1, 0, 2)).reshape(tok_dev, columns)
    glob_out = glob_out.astype(jnp.bfloat16)
    attn_rows = jnp.where(own_index == owner_dev, glob_out, sparse)
    return lax.psum_scatter(
        jnp.dot(attn_rows, out_weight, preferred_element_type=jnp.float32).astype(jnp.bfloat16),
        "head",
        scatter_dimension=0,
        tiled=True,
    )


def ring_gather(block, own_index, owners):
    if owners % 2:
        ring = list(range(owners))
    else:
        half = owners // 2
        ring = [2 * i for i in range(half)] + [2 * i + 1 for i in reversed(range(half))]
    place = [0] * owners
    for i, s in enumerate(ring):
        place[s] = i
    right = [(ring[i], ring[(i + 1) % owners]) for i in range(owners)]
    left = [(ring[i], ring[(i - 1) % owners]) for i in range(owners)]
    pieces = {0: block}
    moving_right = block
    moving_left = block
    for step in range(1, owners // 2 + 1):
        moving_right = jax.tree.map(lambda x: lax.ppermute(x, "seq", right), moving_right)
        pieces[-step] = moving_right
        if step <= (owners - 1) // 2:
            moving_left = jax.tree.map(lambda x: lax.ppermute(x, "seq", left), moving_left)
            moving_right, moving_left = lax.optimization_barrier((moving_right, moving_left))
            pieces[step] = moving_left
        pieces[-step] = moving_right
    offsets = sorted(pieces)
    stacked = jax.tree.map(
        lambda *parts: jnp.concatenate(parts, axis=0), *[pieces[k] for k in offsets]
    )
    where = jnp.asarray(place, jnp.int32)[own_index]
    order = jnp.asarray(ring, jnp.int32)[(where + jnp.asarray(offsets, jnp.int32)) % owners]
    return stacked, order


def gathered_plan(projected, destination, doc_lengths, random_blocks, global_owner, out_weight):
    owners = lax.axis_size("seq")
    own_index = lax.axis_index("seq")
    tok_dev = projected.shape[0]
    columns = projected.shape[2]
    heads_here = columns // HD
    tokens = owners * tok_dev
    blocks_all = tokens // BLK
    score_scale = 1.0 / math.sqrt(HD)
    capacity = 2 * (tok_dev // owners)
    (keyval, key_dest), key_order = ring_gather(
        (projected[:, 1:, :], destination), own_index, owners
    )
    arrival_dest = key_dest
    target_all = arrival_dest.reshape(owners, tok_dev) // tok_dev
    onehot = (target_all[:, :, None] == jnp.arange(owners, dtype=jnp.int32)).astype(jnp.int32)
    slot_all = jnp.sum((jnp.cumsum(onehot, axis=1) - onehot) * onehot, axis=2)
    target = destination // tok_dev
    mine = (target[:, None] == jnp.arange(owners, dtype=jnp.int32)[None, :]).astype(jnp.int32)
    slot = jnp.sum((jnp.cumsum(mine, axis=0) - mine) * mine, axis=1)
    send_col = target * capacity + slot
    send_pick = (
        jnp.arange(owners * capacity, dtype=jnp.int32)[:, None] == send_col[None, :]
    ).astype(projected.dtype)
    outgoing = jnp.dot(send_pick, projected[:, 0, :], preferred_element_type=jnp.float32)
    outgoing = outgoing.astype(projected.dtype).reshape(owners, capacity, columns)
    incoming = lax.all_to_all(outgoing, "seq", split_axis=0, concat_axis=0, tiled=True)
    my_pos = own_index * tok_dev + jnp.arange(tok_dev, dtype=jnp.int32)
    source = jnp.repeat(key_order, tok_dev)
    land_col = (source * capacity + slot_all.reshape(-1))[None, :]
    hit = arrival_dest[None, :] == my_pos[:, None]
    col_of_pos = jnp.sum(jnp.where(hit, land_col, 0), axis=1)
    land_pick = (
        col_of_pos[:, None] == jnp.arange(owners * capacity, dtype=jnp.int32)[None, :]
    ).astype(projected.dtype)
    queries = jnp.dot(
        land_pick, incoming.reshape(owners * capacity, columns), preferred_element_type=jnp.float32
    )
    queries = queries.astype(projected.dtype).reshape(tok_dev, heads_here, HD)
    keys = keyval[:, 0, :].reshape(tokens, heads_here, HD)
    values = keyval[:, 1, :].reshape(tokens, heads_here, HD)
    scores = (
        jnp.einsum("qhd,khd->hqk", queries, keys, preferred_element_type=jnp.float32)
        * score_scale
    )
    bounds = jnp.cumsum(doc_lengths)
    key_block = key_dest // BLK
    key_doc = segment_of(key_dest, bounds)
    query_block = my_pos // BLK
    query_doc = segment_of(my_pos, bounds)
    same_doc = query_doc[:, None] == key_doc[None, :]
    window = jnp.zeros((tok_dev, tokens), jnp.int32)
    for step in (-1, 0, 1):
        near = (query_block + step) % blocks_all
        window = window + (key_block[None, :] == near[:, None]).astype(jnp.int32)
    window = jnp.where(same_doc, window, 0)
    chosen = random_blocks[query_block]
    drawn = jnp.zeros((tok_dev, tokens), jnp.int32)
    for r in range(chosen.shape[1]):
        drawn = drawn + (key_block[None, :] == chosen[:, r][:, None]).astype(jnp.int32)
    glob_start = global_owner[0] * tok_dev
    in_glob = (key_dest >= glob_start) & (key_dest < glob_start + tok_dev)
    holds_glob = own_index == global_owner[0]
    count = window + drawn + in_glob[None, :].astype(jnp.int32)
    count = jnp.where(holds_glob, 1, count)
    live = count > 0
    near_scores = jnp.where(live[None], scores, big_negative)
    row_peak = jnp.max(near_scores, axis=2)
    near_exp = jnp.exp(near_scores - row_peak[..., None])
    count_f = count.astype(jnp.float32)[None]
    denominator = jnp.sum(near_exp * count_f, axis=2)
    rounded = jnp.where(holds_glob, near_exp, near_exp.astype(jnp.bfloat16).astype(jnp.float32))
    weighted = rounded * count_f
    weight_hi = weighted.astype(jnp.bfloat16)
    weight_lo = (weighted - weight_hi.astype(jnp.float32)).astype(jnp.bfloat16)
    both = jnp.concatenate([weight_hi, weight_lo], axis=1)
    both_sum = jnp.einsum("hqk,khd->qhd", both, values, preferred_element_type=jnp.float32)
    mixed_sum = both_sum[:tok_dev] + both_sum[tok_dev:]
    attn_rows = (mixed_sum / jnp.transpose(denominator)[..., None]).reshape(tok_dev, columns)
    attn_rows = attn_rows.astype(jnp.bfloat16)
    projected_rows = jnp.dot(attn_rows, out_weight, preferred_element_type=jnp.float32)
    return head_sum(lax.optimization_barrier(projected_rows))


def head_sum(partial):
    members = lax.axis_size("head")
    if members & (members - 1):
        return lax.psum_scatter(
            partial.astype(jnp.bfloat16), "head", scatter_dimension=0, tiled=True
        )
    me = lax.axis_index("head")
    rows = partial.shape[0] // members
    partial = partial.reshape(members, rows, partial.shape[1])
    bit = 1
    while bit < members:
        pairs = partial.reshape(partial.shape[0] // 2, 2, rows, partial.shape[2])
        upper = (me & bit) != 0
        keep = jnp.where(upper, pairs[:, 1], pairs[:, 0])
        send = jnp.where(upper, pairs[:, 0], pairs[:, 1]).astype(jnp.bfloat16)
        got = lax.ppermute(send, "head", [(i, i ^ bit) for i in range(members)])
        partial = keep + got.astype(jnp.float32)
        bit *= 2
    partial = partial.reshape(rows, partial.shape[2])
    return partial.astype(jnp.bfloat16)


GATHER_LIMIT = 16 * 2**20


def shards(projected, destination, doc_lengths, random_blocks, global_owner, out_weight):
    gathered_bytes = lax.axis_size("seq") * projected.size * projected.dtype.itemsize
    if gathered_bytes <= GATHER_LIMIT:
        return gathered_plan(
            projected, destination, doc_lengths, random_blocks, global_owner, out_weight
        )
    return shards_ring(projected, destination, doc_lengths, random_blocks, global_owner, out_weight)


def solution(mesh):
    in_specs = (P("seq", None, "head"), P("seq"), P(), P(), P(), P("head", None))
    out_specs = P(("seq", "head"), None)
    return jax.shard_map(shards, mesh=mesh, in_specs=in_specs, out_specs=out_specs, check_vma=False)
```

```python
import math

import jax
import jax.numpy as jnp
from jax import lax
from jax.sharding import PartitionSpec as P

HD = 128
BLK = 128
R = 3
RDEV = 2


big_negative = -1e30


def from_behind(block, axis, distance):
    devices = range(lax.axis_size(axis))
    route = [((i - distance) % len(devices), i) for i in devices]
    return lax.ppermute(block, axis, route)


def from_root(x, axis, root):
    mine = lax.axis_index(axis) == root
    return lax.psum(jnp.where(mine, x, jnp.zeros_like(x)), axis)


def combined_all(x, axis, combine):
    everything = jax.tree.map(lambda part: lax.all_gather(part, axis), x)
    first = jax.tree.map(lambda part: part[0], everything)

    def step(k, so_far):
        return combine(so_far, jax.tree.map(lambda part: part[k], everything))

    return lax.fori_loop(1, lax.axis_size(axis), step, first)


def segment_of(positions, bounds):
    return jnp.sum((bounds[None, :] <= positions[:, None]).astype(jnp.int32), axis=1)


def combine_parts(left_part, right_part):
    top_left, total_left, accum_left = left_part
    top_right, total_right, accum_right = right_part
    row_peak = jnp.maximum(top_left, top_right)
    factor_left = jnp.exp(top_left - row_peak)
    factor_right = jnp.exp(top_right - row_peak)
    return (
        row_peak,
        total_left * factor_left + total_right * factor_right,
        accum_left * factor_left[:, :, None] + accum_right * factor_right[:, :, None],
    )


def shards_ring(projected, destination, doc_lengths, random_blocks, global_owner, out_weight):
    owners = lax.axis_size("seq")
    own_index = lax.axis_index("seq")
    tok_dev = projected.shape[0]
    columns = projected.shape[2]
    heads_here = columns // HD
    per_dev = tok_dev // BLK
    blocks_all = owners * per_dev
    capacity = 2 * (tok_dev // owners)
    score_scale = 1.0 / math.sqrt(HD)
    target_owner = destination // tok_dev
    onehot = (target_owner[:, None] == jnp.arange(owners, dtype=jnp.int32)[None, :]).astype(
        jnp.int32
    )
    before = jnp.cumsum(onehot, axis=0) - onehot
    slot_rank = jnp.sum(before * onehot, axis=1)
    outgoing = (
        jnp.zeros((owners, capacity, 3, columns), projected.dtype)
        .at[target_owner, slot_rank]
        .set(projected)
    )
    slots = (
        jnp.full((owners, capacity), -1, jnp.int32)
        .at[target_owner, slot_rank]
        .set(destination % tok_dev)
    )
    incoming, landing = (
        lax.all_to_all(outgoing, "seq", split_axis=0, concat_axis=0, tiled=True),
        lax.all_to_all(slots, "seq", split_axis=0, concat_axis=0, tiled=True),
    )
    landing = landing.reshape(-1)
    landing = jnp.where(landing >= 0, landing, tok_dev)
    routed = (
        jnp.zeros((tok_dev, 3, columns), projected.dtype)
        .at[landing]
        .set(incoming.reshape(owners * capacity, 3, columns), mode="drop")
    )
    keyval = routed[:, 1:, :]
    fetched = {0: keyval}
    offsets = list(range(-RDEV, 0)) + list(range(1, RDEV + 1))
    for offset in offsets:
        fetched[offset] = from_behind(keyval, "seq", -offset)
    band_blocks = jnp.stack([fetched[offset] for offset in range(-RDEV, RDEV + 1)])
    block_ids = own_index * per_dev + jnp.arange(per_dev, dtype=jnp.int32)
    local_pick = jnp.arange(per_dev, dtype=jnp.int32) + RDEV * per_dev
    window_pick = local_pick[:, None] + jnp.arange(-1, 2, dtype=jnp.int32)[None, :]
    chosen_rand = lax.dynamic_slice_in_dim(random_blocks, own_index * per_dev, per_dev, 0)
    away_dev = (chosen_rand // per_dev - own_index) % owners
    away_dev = jnp.where(away_dev > owners // 2, away_dev - owners, away_dev)
    rand_pick = (away_dev + RDEV) * per_dev + chosen_rand % per_dev
    block_picks = jnp.concatenate([window_pick, rand_pick], axis=1)
    gathered = jnp.take(band_blocks, block_picks, axis=0)
    near_keys = gathered[:, :, :, 0, :].reshape(per_dev, (3 + R) * BLK, heads_here, HD)
    near_values = gathered[:, :, :, 1, :].reshape(per_dev, (3 + R) * BLK, heads_here, HD)
    owner_dev = global_owner[0]
    global_rows = from_root(routed, "seq", owner_dev)
    glob_keys = global_rows[:, 1, :].reshape(tok_dev, heads_here, HD)
    glob_values = global_rows[:, 2, :].reshape(tok_dev, heads_here, HD)
    queries = routed[:, 0, :].reshape(per_dev, BLK, heads_here, HD)
    near_scores = (
        jnp.einsum("bqhd,bkhd->bhqk", queries, near_keys, preferred_element_type=jnp.float32)
        * score_scale
    )
    far_scores = (
        jnp.einsum("bqhd,khd->bhqk", queries, glob_keys, preferred_element_type=jnp.float32)
        * score_scale
    )
    bounds = jnp.cumsum(doc_lengths)
    query_pos = own_index * tok_dev + jnp.arange(tok_dev, dtype=jnp.int32)
    query_doc = segment_of(query_pos, bounds).reshape(per_dev, BLK)
    window_blocks = (block_ids[:, None] + jnp.arange(-1, 2, dtype=jnp.int32)[None, :]) % blocks_all
    key_pos = (
        window_blocks[:, :, None] * BLK + jnp.arange(BLK, dtype=jnp.int32)[None, None, :]
    ).reshape(-1)
    key_doc = segment_of(key_pos, bounds).reshape(per_dev, 3 * BLK)
    same_doc = query_doc[:, :, None] == key_doc[:, None, :]
    allowed = jnp.concatenate(
        [same_doc, jnp.ones((per_dev, BLK, R * BLK), dtype=jnp.bool_)], axis=2
    )
    near_scores = jnp.where(allowed[:, None], near_scores, big_negative)
    row_peak = jnp.maximum(jnp.max(near_scores, axis=3), jnp.max(far_scores, axis=3))
    near_exp = jnp.exp(near_scores - row_peak[..., None])
    far_exp = jnp.exp(far_scores - row_peak[..., None])
    denominator = jnp.sum(near_exp, axis=3) + jnp.sum(far_exp, axis=3)
    mixed_sum = jnp.einsum(
        "bhqk,bkhd->bqhd",
        near_exp.astype(jnp.bfloat16),
        near_values,
        preferred_element_type=jnp.float32,
    )
    mixed_sum = mixed_sum + jnp.einsum(
        "bhqk,khd->bqhd",
        far_exp.astype(jnp.bfloat16),
        glob_values,
        preferred_element_type=jnp.float32,
    )
    sparse = (mixed_sum / jnp.transpose(denominator, (0, 2, 1))[..., None]).reshape(
        tok_dev, columns
    )
    sparse = sparse.astype(jnp.bfloat16)
    glob_queries = global_rows[:, 0, :].reshape(tok_dev, heads_here, HD)
    local_keys = routed[:, 1, :].reshape(tok_dev, heads_here, HD)
    local_values = routed[:, 2, :].reshape(tok_dev, heads_here, HD).astype(jnp.float32)
    all_scores = (
        jnp.einsum("qhd,khd->hqk", glob_queries, local_keys, preferred_element_type=jnp.float32)
        * score_scale
    )
    local_peak = jnp.max(all_scores, axis=2)
    weights = jnp.exp(all_scores - local_peak[..., None])
    part_total = jnp.sum(weights, axis=2)
    part_accum = jnp.einsum("hqk,khd->hqd", weights, local_values, precision=lax.Precision.HIGHEST)
    peak_all, total_all, accum_all = combined_all(
        (local_peak, part_total, part_accum), "seq", combine_parts
    )
    glob_out = jnp.transpose(accum_all / total_all[..., None], (1, 0, 2)).reshape(tok_dev, columns)
    glob_out = glob_out.astype(jnp.bfloat16)
    attn_rows = jnp.where(own_index == owner_dev, glob_out, sparse)
    return lax.psum_scatter(
        jnp.dot(attn_rows, out_weight, preferred_element_type=jnp.float32).astype(jnp.bfloat16),
        "head",
        scatter_dimension=0,
        tiled=True,
    )


def ring_gather(block, own_index, owners):
    if owners % 2:
        ring = list(range(owners))
    else:
        half = owners // 2
        ring = [2 * i for i in range(half)] + [2 * i + 1 for i in reversed(range(half))]
    place = [0] * owners
    for i, s in enumerate(ring):
        place[s] = i
    right = [(ring[i], ring[(i + 1) % owners]) for i in range(owners)]
    left = [(ring[i], ring[(i - 1) % owners]) for i in range(owners)]
    pieces = {0: block}
    moving_right = block
    moving_left = block
    for step in range(1, owners // 2 + 1):
        moving_right = jax.tree.map(lambda x: lax.ppermute(x, "seq", right), moving_right)
        pieces[-step] = moving_right
        if step <= (owners - 1) // 2:
            moving_left = jax.tree.map(lambda x: lax.ppermute(x, "seq", left), moving_left)
            moving_right, moving_left = lax.optimization_barrier((moving_right, moving_left))
            pieces[step] = moving_left
        pieces[-step] = moving_right
    offsets = sorted(pieces)
    stacked = jax.tree.map(
        lambda *parts: jnp.concatenate(parts, axis=0), *[pieces[k] for k in offsets]
    )
    where = jnp.asarray(place, jnp.int32)[own_index]
    order = jnp.asarray(ring, jnp.int32)[(where + jnp.asarray(offsets, jnp.int32)) % owners]
    return stacked, order


def gathered_plan(projected, destination, doc_lengths, random_blocks, global_owner, out_weight):
    owners = lax.axis_size("seq")
    own_index = lax.axis_index("seq")
    tok_dev = projected.shape[0]
    columns = projected.shape[2]
    heads_here = columns // HD
    tokens = owners * tok_dev
    blocks_all = tokens // BLK
    score_scale = 1.0 / math.sqrt(HD)
    capacity = 2 * (tok_dev // owners)
    (keyval, key_dest), key_order = ring_gather(
        (projected[:, 1:, :], destination), own_index, owners
    )
    arrival_dest = key_dest
    target_all = arrival_dest.reshape(owners, tok_dev) // tok_dev
    onehot = (target_all[:, :, None] == jnp.arange(owners, dtype=jnp.int32)).astype(jnp.int32)
    slot_all = jnp.sum((jnp.cumsum(onehot, axis=1) - onehot) * onehot, axis=2)
    target = destination // tok_dev
    mine = (target[:, None] == jnp.arange(owners, dtype=jnp.int32)[None, :]).astype(jnp.int32)
    slot = jnp.sum((jnp.cumsum(mine, axis=0) - mine) * mine, axis=1)
    send_col = target * capacity + slot
    send_pick = (
        jnp.arange(owners * capacity, dtype=jnp.int32)[:, None] == send_col[None, :]
    ).astype(projected.dtype)
    outgoing = jnp.dot(send_pick, projected[:, 0, :], preferred_element_type=jnp.float32)
    outgoing = outgoing.astype(projected.dtype).reshape(owners, capacity, columns)
    incoming = lax.all_to_all(outgoing, "seq", split_axis=0, concat_axis=0, tiled=True)
    my_pos = own_index * tok_dev + jnp.arange(tok_dev, dtype=jnp.int32)
    source = jnp.repeat(key_order, tok_dev)
    land_col = (source * capacity + slot_all.reshape(-1))[None, :]
    hit = arrival_dest[None, :] == my_pos[:, None]
    col_of_pos = jnp.sum(jnp.where(hit, land_col, 0), axis=1)
    land_pick = (
        col_of_pos[:, None] == jnp.arange(owners * capacity, dtype=jnp.int32)[None, :]
    ).astype(projected.dtype)
    queries = jnp.dot(
        land_pick, incoming.reshape(owners * capacity, columns), preferred_element_type=jnp.float32
    )
    queries = queries.astype(projected.dtype).reshape(tok_dev, heads_here, HD)
    queries, out_weight = lax.optimization_barrier((queries, out_weight))
    keys = keyval[:, 0, :].reshape(tokens, heads_here, HD)
    values = keyval[:, 1, :].reshape(tokens, heads_here, HD)
    scores = (
        jnp.einsum("qhd,khd->hqk", queries, keys, preferred_element_type=jnp.float32)
        * score_scale
    )
    bounds = jnp.cumsum(doc_lengths)
    key_block = key_dest // BLK
    key_doc = segment_of(key_dest, bounds)
    query_block = my_pos // BLK
    query_doc = segment_of(my_pos, bounds)
    same_doc = query_doc[:, None] == key_doc[None, :]
    window = jnp.zeros((tok_dev, tokens), jnp.int32)
    for step in (-1, 0, 1):
        near = (query_block + step) % blocks_all
        window = window + (key_block[None, :] == near[:, None]).astype(jnp.int32)
    window = jnp.where(same_doc, window, 0)
    chosen = random_blocks[query_block]
    drawn = jnp.zeros((tok_dev, tokens), jnp.int32)
    for r in range(chosen.shape[1]):
        drawn = drawn + (key_block[None, :] == chosen[:, r][:, None]).astype(jnp.int32)
    glob_start = global_owner[0] * tok_dev
    in_glob = (key_dest >= glob_start) & (key_dest < glob_start + tok_dev)
    holds_glob = own_index == global_owner[0]
    count = window + drawn + in_glob[None, :].astype(jnp.int32)
    count = jnp.where(holds_glob, 1, count)
    live = count > 0
    near_scores = jnp.where(live[None], scores, big_negative)
    row_peak = jnp.max(near_scores, axis=2)
    near_exp = jnp.exp(near_scores - row_peak[..., None])
    count_f = count.astype(jnp.float32)[None]
    denominator = jnp.sum(near_exp * count_f, axis=2)
    rounded = jnp.where(holds_glob, near_exp, near_exp.astype(jnp.bfloat16).astype(jnp.float32))
    weighted = rounded * count_f
    weight_hi = weighted.astype(jnp.bfloat16)
    weight_lo = (weighted - weight_hi.astype(jnp.float32)).astype(jnp.bfloat16)
    both = jnp.concatenate([weight_hi, weight_lo], axis=1)
    both_sum = jnp.einsum("hqk,khd->qhd", both, values, preferred_element_type=jnp.float32)
    mixed_sum = both_sum[:tok_dev] + both_sum[tok_dev:]
    attn_rows = (mixed_sum / jnp.transpose(denominator)[..., None]).reshape(tok_dev, columns)
    attn_rows = attn_rows.astype(jnp.bfloat16)
    projected_rows = jnp.dot(attn_rows, out_weight, preferred_element_type=jnp.float32)
    return head_sum(lax.optimization_barrier(projected_rows))


def head_sum(partial):
    members = lax.axis_size("head")
    if members & (members - 1):
        return lax.psum_scatter(
            partial.astype(jnp.bfloat16), "head", scatter_dimension=0, tiled=True
        )
    me = lax.axis_index("head")
    rows = partial.shape[0] // members
    partial = partial.reshape(members, rows, partial.shape[1])
    bit = 1
    while bit < members:
        pairs = partial.reshape(partial.shape[0] // 2, 2, rows, partial.shape[2])
        upper = (me & bit) != 0
        keep = jnp.where(upper, pairs[:, 1], pairs[:, 0])
        send = jnp.where(upper, pairs[:, 0], pairs[:, 1]).astype(jnp.bfloat16)
        got = lax.ppermute(send, "head", [(i, i ^ bit) for i in range(members)])
        partial = keep + got.astype(jnp.float32)
        bit *= 2
    partial = partial.reshape(rows, partial.shape[2])
    return partial.astype(jnp.bfloat16)


GATHER_LIMIT = 16 * 2**20


def shards(projected, destination, doc_lengths, random_blocks, global_owner, out_weight):
    gathered_bytes = lax.axis_size("seq") * projected.size * projected.dtype.itemsize
    if gathered_bytes <= GATHER_LIMIT:
        return gathered_plan(
            projected, destination, doc_lengths, random_blocks, global_owner, out_weight
        )
    return shards_ring(projected, destination, doc_lengths, random_blocks, global_owner, out_weight)


def solution(mesh):
    in_specs = (P("seq", None, "head"), P("seq"), P(), P(), P(), P("head", None))
    out_specs = P(("seq", "head"), None)
    return jax.shard_map(shards, mesh=mesh, in_specs=in_specs, out_specs=out_specs, check_vma=False)
```

```python
import math

import jax
import jax.numpy as jnp
from jax import lax
from jax.sharding import PartitionSpec as P

HD = 128
BLK = 128
R = 3
RDEV = 2


big_negative = -1e30


def from_behind(block, axis, distance):
    devices = range(lax.axis_size(axis))
    route = [((i - distance) % len(devices), i) for i in devices]
    return lax.ppermute(block, axis, route)


def from_root(x, axis, root):
    mine = lax.axis_index(axis) == root
    return lax.psum(jnp.where(mine, x, jnp.zeros_like(x)), axis)


def combined_all(x, axis, combine):
    everything = jax.tree.map(lambda part: lax.all_gather(part, axis), x)
    first = jax.tree.map(lambda part: part[0], everything)

    def step(k, so_far):
        return combine(so_far, jax.tree.map(lambda part: part[k], everything))

    return lax.fori_loop(1, lax.axis_size(axis), step, first)


def segment_of(positions, bounds):
    return jnp.sum((bounds[None, :] <= positions[:, None]).astype(jnp.int32), axis=1)


def combine_parts(left_part, right_part):
    top_left, total_left, accum_left = left_part
    top_right, total_right, accum_right = right_part
    row_peak = jnp.maximum(top_left, top_right)
    factor_left = jnp.exp(top_left - row_peak)
    factor_right = jnp.exp(top_right - row_peak)
    return (
        row_peak,
        total_left * factor_left + total_right * factor_right,
        accum_left * factor_left[:, :, None] + accum_right * factor_right[:, :, None],
    )


def shards_ring(projected, destination, doc_lengths, random_blocks, global_owner, out_weight):
    owners = lax.axis_size("seq")
    own_index = lax.axis_index("seq")
    tok_dev = projected.shape[0]
    columns = projected.shape[2]
    heads_here = columns // HD
    per_dev = tok_dev // BLK
    blocks_all = owners * per_dev
    capacity = 2 * (tok_dev // owners)
    score_scale = 1.0 / math.sqrt(HD)
    target_owner = destination // tok_dev
    onehot = (target_owner[:, None] == jnp.arange(owners, dtype=jnp.int32)[None, :]).astype(
        jnp.int32
    )
    before = jnp.cumsum(onehot, axis=0) - onehot
    slot_rank = jnp.sum(before * onehot, axis=1)
    outgoing = (
        jnp.zeros((owners, capacity, 3, columns), projected.dtype)
        .at[target_owner, slot_rank]
        .set(projected)
    )
    slots = (
        jnp.full((owners, capacity), -1, jnp.int32)
        .at[target_owner, slot_rank]
        .set(destination % tok_dev)
    )
    incoming, landing = (
        lax.all_to_all(outgoing, "seq", split_axis=0, concat_axis=0, tiled=True),
        lax.all_to_all(slots, "seq", split_axis=0, concat_axis=0, tiled=True),
    )
    landing = landing.reshape(-1)
    landing = jnp.where(landing >= 0, landing, tok_dev)
    routed = (
        jnp.zeros((tok_dev, 3, columns), projected.dtype)
        .at[landing]
        .set(incoming.reshape(owners * capacity, 3, columns), mode="drop")
    )
    keyval = routed[:, 1:, :]
    fetched = {0: keyval}
    offsets = list(range(-RDEV, 0)) + list(range(1, RDEV + 1))
    for offset in offsets:
        fetched[offset] = from_behind(keyval, "seq", -offset)
    band_blocks = jnp.stack([fetched[offset] for offset in range(-RDEV, RDEV + 1)])
    block_ids = own_index * per_dev + jnp.arange(per_dev, dtype=jnp.int32)
    local_pick = jnp.arange(per_dev, dtype=jnp.int32) + RDEV * per_dev
    window_pick = local_pick[:, None] + jnp.arange(-1, 2, dtype=jnp.int32)[None, :]
    chosen_rand = lax.dynamic_slice_in_dim(random_blocks, own_index * per_dev, per_dev, 0)
    away_dev = (chosen_rand // per_dev - own_index) % owners
    away_dev = jnp.where(away_dev > owners // 2, away_dev - owners, away_dev)
    rand_pick = (away_dev + RDEV) * per_dev + chosen_rand % per_dev
    block_picks = jnp.concatenate([window_pick, rand_pick], axis=1)
    gathered = jnp.take(band_blocks, block_picks, axis=0)
    near_keys = gathered[:, :, :, 0, :].reshape(per_dev, (3 + R) * BLK, heads_here, HD)
    near_values = gathered[:, :, :, 1, :].reshape(per_dev, (3 + R) * BLK, heads_here, HD)
    owner_dev = global_owner[0]
    global_rows = from_root(routed, "seq", owner_dev)
    glob_keys = global_rows[:, 1, :].reshape(tok_dev, heads_here, HD)
    glob_values = global_rows[:, 2, :].reshape(tok_dev, heads_here, HD)
    queries = routed[:, 0, :].reshape(per_dev, BLK, heads_here, HD)
    near_scores = (
        jnp.einsum("bqhd,bkhd->bhqk", queries, near_keys, preferred_element_type=jnp.float32)
        * score_scale
    )
    far_scores = (
        jnp.einsum("bqhd,khd->bhqk", queries, glob_keys, preferred_element_type=jnp.float32)
        * score_scale
    )
    bounds = jnp.cumsum(doc_lengths)
    query_pos = own_index * tok_dev + jnp.arange(tok_dev, dtype=jnp.int32)
    query_doc = segment_of(query_pos, bounds).reshape(per_dev, BLK)
    window_blocks = (block_ids[:, None] + jnp.arange(-1, 2, dtype=jnp.int32)[None, :]) % blocks_all
    key_pos = (
        window_blocks[:, :, None] * BLK + jnp.arange(BLK, dtype=jnp.int32)[None, None, :]
    ).reshape(-1)
    key_doc = segment_of(key_pos, bounds).reshape(per_dev, 3 * BLK)
    same_doc = query_doc[:, :, None] == key_doc[:, None, :]
    allowed = jnp.concatenate(
        [same_doc, jnp.ones((per_dev, BLK, R * BLK), dtype=jnp.bool_)], axis=2
    )
    near_scores = jnp.where(allowed[:, None], near_scores, big_negative)
    row_peak = jnp.maximum(jnp.max(near_scores, axis=3), jnp.max(far_scores, axis=3))
    near_exp = jnp.exp(near_scores - row_peak[..., None])
    far_exp = jnp.exp(far_scores - row_peak[..., None])
    denominator = jnp.sum(near_exp, axis=3) + jnp.sum(far_exp, axis=3)
    mixed_sum = jnp.einsum(
        "bhqk,bkhd->bqhd",
        near_exp.astype(jnp.bfloat16),
        near_values,
        preferred_element_type=jnp.float32,
    )
    mixed_sum = mixed_sum + jnp.einsum(
        "bhqk,khd->bqhd",
        far_exp.astype(jnp.bfloat16),
        glob_values,
        preferred_element_type=jnp.float32,
    )
    sparse = (mixed_sum / jnp.transpose(denominator, (0, 2, 1))[..., None]).reshape(
        tok_dev, columns
    )
    sparse = sparse.astype(jnp.bfloat16)
    glob_queries = global_rows[:, 0, :].reshape(tok_dev, heads_here, HD)
    local_keys = routed[:, 1, :].reshape(tok_dev, heads_here, HD)
    local_values = routed[:, 2, :].reshape(tok_dev, heads_here, HD).astype(jnp.float32)
    all_scores = (
        jnp.einsum("qhd,khd->hqk", glob_queries, local_keys, preferred_element_type=jnp.float32)
        * score_scale
    )
    local_peak = jnp.max(all_scores, axis=2)
    weights = jnp.exp(all_scores - local_peak[..., None])
    part_total = jnp.sum(weights, axis=2)
    part_accum = jnp.einsum("hqk,khd->hqd", weights, local_values, precision=lax.Precision.HIGHEST)
    peak_all, total_all, accum_all = combined_all(
        (local_peak, part_total, part_accum), "seq", combine_parts
    )
    glob_out = jnp.transpose(accum_all / total_all[..., None], (1, 0, 2)).reshape(tok_dev, columns)
    glob_out = glob_out.astype(jnp.bfloat16)
    attn_rows = jnp.where(own_index == owner_dev, glob_out, sparse)
    return lax.psum_scatter(
        jnp.dot(attn_rows, out_weight, preferred_element_type=jnp.float32).astype(jnp.bfloat16),
        "head",
        scatter_dimension=0,
        tiled=True,
    )


def ring_gather(block, own_index, owners):
    if owners % 2:
        ring = list(range(owners))
    else:
        half = owners // 2
        ring = [2 * i for i in range(half)] + [2 * i + 1 for i in reversed(range(half))]
    place = [0] * owners
    for i, s in enumerate(ring):
        place[s] = i
    right = [(ring[i], ring[(i + 1) % owners]) for i in range(owners)]
    left = [(ring[i], ring[(i - 1) % owners]) for i in range(owners)]
    pieces = {0: block}
    moving_right = block
    moving_left = block
    for step in range(1, owners // 2 + 1):
        moving_right = jax.tree.map(lambda x: lax.ppermute(x, "seq", right), moving_right)
        pieces[-step] = moving_right
        if step <= (owners - 1) // 2:
            moving_left = jax.tree.map(lambda x: lax.ppermute(x, "seq", left), moving_left)
            moving_right, moving_left = lax.optimization_barrier((moving_right, moving_left))
            pieces[step] = moving_left
        pieces[-step] = moving_right
    offsets = sorted(pieces)
    stacked = jax.tree.map(
        lambda *parts: jnp.concatenate(parts, axis=0), *[pieces[k] for k in offsets]
    )
    where = jnp.asarray(place, jnp.int32)[own_index]
    order = jnp.asarray(ring, jnp.int32)[(where + jnp.asarray(offsets, jnp.int32)) % owners]
    return stacked, order


def gathered_plan(projected, destination, doc_lengths, random_blocks, global_owner, out_weight):
    owners = lax.axis_size("seq")
    own_index = lax.axis_index("seq")
    tok_dev = projected.shape[0]
    columns = projected.shape[2]
    heads_here = columns // HD
    tokens = owners * tok_dev
    blocks_all = tokens // BLK
    score_scale = 1.0 / math.sqrt(HD)
    capacity = 2 * (tok_dev // owners)
    (keyval, key_dest), key_order = ring_gather(
        (projected[:, 1:, :], destination), own_index, owners
    )
    arrival_dest = key_dest
    target_all = arrival_dest.reshape(owners, tok_dev) // tok_dev
    onehot = (target_all[:, :, None] == jnp.arange(owners, dtype=jnp.int32)).astype(jnp.int32)
    slot_all = jnp.sum((jnp.cumsum(onehot, axis=1) - onehot) * onehot, axis=2)
    target = destination // tok_dev
    mine = (target[:, None] == jnp.arange(owners, dtype=jnp.int32)[None, :]).astype(jnp.int32)
    slot = jnp.sum((jnp.cumsum(mine, axis=0) - mine) * mine, axis=1)
    send_col = target * capacity + slot
    send_pick = (
        jnp.arange(owners * capacity, dtype=jnp.int32)[:, None] == send_col[None, :]
    ).astype(projected.dtype)
    outgoing = jnp.dot(send_pick, projected[:, 0, :], preferred_element_type=jnp.float32)
    outgoing = outgoing.astype(projected.dtype).reshape(owners, capacity, columns)
    incoming = lax.all_to_all(outgoing, "seq", split_axis=0, concat_axis=0, tiled=True)
    my_pos = own_index * tok_dev + jnp.arange(tok_dev, dtype=jnp.int32)
    source = jnp.repeat(key_order, tok_dev)
    land_col = (source * capacity + slot_all.reshape(-1))[None, :]
    hit = arrival_dest[None, :] == my_pos[:, None]
    col_of_pos = jnp.sum(jnp.where(hit, land_col, 0), axis=1)
    land_pick = (
        col_of_pos[:, None] == jnp.arange(owners * capacity, dtype=jnp.int32)[None, :]
    ).astype(projected.dtype)
    queries = jnp.dot(
        land_pick, incoming.reshape(owners * capacity, columns), preferred_element_type=jnp.float32
    )
    queries = queries.astype(projected.dtype).reshape(tok_dev, heads_here, HD)
    keys = keyval[:, 0, :].reshape(tokens, heads_here, HD)
    values = keyval[:, 1, :].reshape(tokens, heads_here, HD)
    scores = (
        jnp.einsum("qhd,khd->hqk", queries, keys, preferred_element_type=jnp.float32)
        * score_scale
    )
    bounds = jnp.cumsum(doc_lengths)
    query_block = my_pos // BLK
    query_doc = segment_of(my_pos, bounds)
    chosen = random_blocks[query_block]
    glob_start = global_owner[0] * tok_dev
    holds_glob = own_index == global_owner[0]

    def key_count(piece_dest):
        key_block = piece_dest // BLK
        same_doc = query_doc[:, None] == segment_of(piece_dest, bounds)[None, :]
        window = jnp.zeros((tok_dev, piece_dest.shape[0]), jnp.int32)
        for step in (-1, 0, 1):
            near = (query_block + step) % blocks_all
            window = window + (key_block[None, :] == near[:, None]).astype(jnp.int32)
        window = jnp.where(same_doc, window, 0)
        for r in range(chosen.shape[1]):
            window = window + (key_block[None, :] == chosen[:, r][:, None]).astype(jnp.int32)
        in_glob = (piece_dest >= glob_start) & (piece_dest < glob_start + tok_dev)
        return window + in_glob[None, :].astype(jnp.int32)

    count = jnp.concatenate(
        [key_count(key_dest[i * tok_dev : (i + 1) * tok_dev]) for i in range(owners)], axis=1
    )
    count = jnp.where(holds_glob, 1, count)
    live = count > 0
    near_scores = jnp.where(live[None], scores, big_negative)
    row_peak = jnp.max(near_scores, axis=2)
    near_exp = jnp.exp(near_scores - row_peak[..., None])
    count_f = count.astype(jnp.float32)[None]
    denominator = jnp.sum(near_exp * count_f, axis=2)
    rounded = jnp.where(holds_glob, near_exp, near_exp.astype(jnp.bfloat16).astype(jnp.float32))
    weighted = rounded * count_f
    weight_hi = weighted.astype(jnp.bfloat16)
    weight_lo = (weighted - weight_hi.astype(jnp.float32)).astype(jnp.bfloat16)
    both = jnp.concatenate([weight_hi, weight_lo], axis=1)
    both_sum = jnp.einsum("hqk,khd->qhd", both, values, preferred_element_type=jnp.float32)
    mixed_sum = both_sum[:tok_dev] + both_sum[tok_dev:]
    attn_rows = (mixed_sum / jnp.transpose(denominator)[..., None]).reshape(tok_dev, columns)
    attn_rows = attn_rows.astype(jnp.bfloat16)
    projected_rows = jnp.dot(attn_rows, out_weight, preferred_element_type=jnp.float32)
    return head_sum(lax.optimization_barrier(projected_rows))


def head_sum(partial):
    members = lax.axis_size("head")
    if members & (members - 1):
        return lax.psum_scatter(
            partial.astype(jnp.bfloat16), "head", scatter_dimension=0, tiled=True
        )
    me = lax.axis_index("head")
    rows = partial.shape[0] // members
    partial = partial.reshape(members, rows, partial.shape[1])
    bit = 1
    while bit < members:
        pairs = partial.reshape(partial.shape[0] // 2, 2, rows, partial.shape[2])
        upper = (me & bit) != 0
        keep = jnp.where(upper, pairs[:, 1], pairs[:, 0])
        send = jnp.where(upper, pairs[:, 0], pairs[:, 1]).astype(jnp.bfloat16)
        got = lax.ppermute(send, "head", [(i, i ^ bit) for i in range(members)])
        partial = keep + got.astype(jnp.float32)
        bit *= 2
    partial = partial.reshape(rows, partial.shape[2])
    return partial.astype(jnp.bfloat16)


GATHER_LIMIT = 16 * 2**20


def shards(projected, destination, doc_lengths, random_blocks, global_owner, out_weight):
    gathered_bytes = lax.axis_size("seq") * projected.size * projected.dtype.itemsize
    if gathered_bytes <= GATHER_LIMIT:
        return gathered_plan(
            projected, destination, doc_lengths, random_blocks, global_owner, out_weight
        )
    return shards_ring(projected, destination, doc_lengths, random_blocks, global_owner, out_weight)


def solution(mesh):
    in_specs = (P("seq", None, "head"), P("seq"), P(), P(), P(), P("head", None))
    out_specs = P(("seq", "head"), None)
    return jax.shard_map(shards, mesh=mesh, in_specs=in_specs, out_specs=out_specs, check_vma=False)
```
